512 devices in a mesh: ctx: 128 (over x, z, y_lo, core), head: 4 (over y_hi).
Axes of the slice: x: 4, y: 8 (y_hi: 4, y_lo: 2; y = y_hi * 2 + y_lo), z: 8, core: 2. Of those that a mesh axis runs over, the one named last changes fastest.
Arguments:
- queries: bfloat16 [32768, 2048], P('ctx', 'head'), may hold values from -8 to 8
- keys: bfloat16 [32768, 2048], P('ctx', 'head'), may hold values from -8 to 8
- values: bfloat16 [32768, 2048], P('ctx', 'head'), may hold values from -6 to 6
- out_grad: bfloat16 [32768, 2048], P('ctx', 'head'), may hold values from -6 to 6
Outputs:
- attended: bfloat16 [32768, 2048], P('ctx', 'head')
- query_grad: bfloat16 [32768, 2048], P('ctx', 'head')
- key_grad: bfloat16 [32768, 2048], P('ctx', 'head')
- value_grad: bfloat16 [32768, 2048], P('ctx', 'head')
The draws below stay inside these ranges and needn't reach their ends.
All inputs are finite; a program needn't handle non-finite values.
Results may differ from the reference program's by a relative error of at most 0.017.
Values may be sent and summed in bfloat16 or wider, within the bound.
No kernel may reach another device: no remote copies, remote signals or barrier semaphores. Data moves between devices by JAX's collectives and lax.ppermute only.
A program may use at most 64 MiB of HBM per device.

```python
import math
import jax
import jax.numpy as jnp
from jax import lax

HD = 128
HEADS = 16
STRIDE = 128
SUMMARY = 4
SEQ = 32768
NBLK = 256


def base_rows(key):
    normal = jnp.clip(jax.random.normal(key, (SEQ, HEADS * HD), jnp.float32), -4.0, 4.0)
    return normal


def far_rows(key):
    position = jnp.arange(SEQ, dtype=jnp.int32)
    linked = (position % STRIDE == STRIDE // 2) & (position >= SEQ // 2)
    source = (position // STRIDE - NBLK // 2) * STRIDE + STRIDE - 1
    source = jnp.clip(source, 0, SEQ - 1).astype(jnp.int32)
    key_base = base_rows(jax.random.fold_in(key, 2))
    copied = jnp.clip(1.5 * jnp.take(key_base, source, axis=0), -8.0, 8.0)
    return (linked, copied)


def draw_queries(key, part):
    result_rows = base_rows(jax.random.fold_in(key, 1))
    linked, copied = far_rows(key)
    result_rows = jnp.where(linked[:, None], copied, result_rows)
    return result_rows.astype(jnp.bfloat16)


def draw_keys(key, part):
    result_rows = base_rows(jax.random.fold_in(key, 2))
    return result_rows.astype(jnp.bfloat16)


def block_levels(key, shape, pieces, least, top_value):
    loudness, own = 1.0, jax.random.fold_in(key, 6)
    for dim, shards_of in pieces:
        steps = jnp.exp(jax.random.uniform(jax.random.fold_in(own, dim), (shards_of,), jnp.float32, least / len(pieces), top_value / len(pieces)))
        loudness = loudness * jnp.repeat(steps, shape[dim] // shards_of).reshape([-1 if axis == dim else 1 for axis in range(len(shape))])
    return loudness


def gaussian(stream_key, extent, width, most, cuts=(), held_as=jnp.bfloat16):
    drawn = width * jax.random.normal(stream_key, extent, jnp.float32)
    if cuts:
        drawn = drawn * block_levels(stream_key, extent, cuts, -0.22, 0.18)
    return jnp.clip(drawn, -most, most).astype(held_as)


def setup_inputs(seed: int = 0) -> dict:
    key_of = jax.random.split(jax.random.key(seed), 5)
    queries = draw_queries(jax.random.fold_in(key_of[4], 71), 0)
    keys = draw_keys(jax.random.fold_in(key_of[4], 71), 0)
    values = gaussian(key_of[2], (SEQ, HEADS * HD), 1.0, 6.0, ((0, 128), (1, 4)))
    out_grad = gaussian(key_of[3], (SEQ, HEADS * HD), 1.0, 6.0, ((0, 128), (1, 4)))
    return dict(queries=queries, keys=keys, values=values, out_grad=out_grad)


def split_heads(matrix):
    blocks = matrix.shape[0] // STRIDE
    half_heads = matrix.shape[1] // (2 * HD)
    shaped = matrix.reshape(blocks, STRIDE, matrix.shape[1] // (4 * HD), 4, HD)
    fixed = shaped[:, :, :, :2].reshape(blocks, STRIDE, half_heads, HD)
    strided = shaped[:, :, :, 2:].reshape(blocks, STRIDE, half_heads, HD)
    return (fixed, strided)

def join_heads(fixed, strided):
    blocks, positions, half_heads, head_dim = fixed.shape
    paired = jnp.concatenate([fixed.reshape(blocks, positions, half_heads // 2, 2, head_dim), strided.reshape(blocks, positions, half_heads // 2, 2, head_dim)], axis=3)
    return paired.reshape(blocks * positions, 2 * half_heads * head_dim)

def rounded(array):
    return lax.optimization_barrier(array.astype(jnp.bfloat16)).astype(jnp.float32)

def attend_core(query, key_rows, value_rows, grad_rows, allowed, scaling):
    query = query.astype(jnp.float32)
    key_rows = key_rows.astype(jnp.float32)
    value_rows = value_rows.astype(jnp.float32)
    grad_rows = grad_rows.astype(jnp.float32)
    scores = jnp.einsum('gnd,gmd->gnm', query, key_rows) * scaling
    scores = jnp.where(allowed[None], scores, -jnp.inf)
    row_max = lax.optimization_barrier(jnp.max(scores, axis=-1, keepdims=True))
    raised = jnp.exp(scores - row_max)
    weights = raised / lax.optimization_barrier(jnp.sum(raised, axis=-1, keepdims=True))
    weights_low = rounded(weights)
    attended = jnp.einsum('gnm,gmd->gnd', weights_low, value_rows).astype(jnp.bfloat16)
    dweights = jnp.einsum('gnd,gmd->gnm', grad_rows, value_rows)
    row_delta = lax.optimization_barrier(jnp.sum(grad_rows * attended.astype(jnp.float32), axis=-1, keepdims=True))
    dscores = rounded(weights * (dweights - row_delta))
    query_grad = jnp.einsum('gnm,gmd->gnd', dscores, key_rows) * scaling
    key_grad = jnp.einsum('gnm,gnd->gmd', dscores, query) * scaling
    value_grad = jnp.einsum('gnm,gnd->gmd', weights_low, grad_rows)
    return (attended, query_grad, key_grad, value_grad)

def reorder(array):
    return array.transpose(0, 2, 1, 3).astype(jnp.bfloat16)

def fixed_part(query, key_rows, value_rows, grad_rows, scaling):
    blocks, positions, half_heads, head_dim = query.shape
    summary_count = blocks * SUMMARY
    summary_keys = key_rows[:, positions - SUMMARY:].reshape(summary_count, half_heads, head_dim).transpose(1, 0, 2)
    summary_values = value_rows[:, positions - SUMMARY:].reshape(summary_count, half_heads, head_dim).transpose(1, 0, 2)
    causal = jnp.arange(positions)[:, None] >= jnp.arange(positions)[None, :]
    summary_block = jnp.arange(summary_count, dtype=jnp.int32) // SUMMARY

    def per_block(running, inputs):
        block_query, block_keys, block_values, block_grads, block_index = inputs
        keys_all = jnp.concatenate([block_keys.transpose(1, 0, 2), summary_keys], axis=1)
        values_all = jnp.concatenate([block_values.transpose(1, 0, 2), summary_values], axis=1)
        earlier = jnp.broadcast_to((summary_block < block_index)[None, :], (positions, summary_count))
        allowed = jnp.concatenate([causal, earlier], axis=1)
        attended, query_grad, key_grad, value_grad = attend_core(block_query.transpose(1, 0, 2), keys_all, values_all, block_grads.transpose(1, 0, 2), allowed, scaling)
        running = (running[0] + key_grad[:, positions:], running[1] + value_grad[:, positions:])
        return (running, (attended, query_grad, key_grad[:, :positions], value_grad[:, :positions]))
    initial = (jnp.zeros((half_heads, summary_count, head_dim), jnp.float32), jnp.zeros((half_heads, summary_count, head_dim), jnp.float32))
    totals, stacked = lax.scan(per_block, initial, (query, key_rows, value_rows, grad_rows, jnp.arange(blocks, dtype=jnp.int32)))
    attended, query_grad, key_grad, value_grad = stacked
    key_extra = totals[0].reshape(half_heads, blocks, SUMMARY, head_dim).transpose(1, 0, 2, 3)
    value_extra = totals[1].reshape(half_heads, blocks, SUMMARY, head_dim).transpose(1, 0, 2, 3)
    key_grad = key_grad.at[:, :, positions - SUMMARY:].add(key_extra)
    value_grad = value_grad.at[:, :, positions - SUMMARY:].add(value_extra)
    return (reorder(attended), reorder(query_grad), reorder(key_grad), reorder(value_grad))

def strided_part(query, key_rows, value_rows, grad_rows, scaling):
    blocks = query.shape[0]
    causal = jnp.arange(blocks)[:, None] >= jnp.arange(blocks)[None, :]

    def per_residue(residue):

        def residue_of(array):
            return lax.dynamic_index_in_dim(array, residue, 1, keepdims=False).transpose(1, 0, 2)
        results = attend_core(residue_of(query), residue_of(key_rows), residue_of(value_rows), residue_of(grad_rows), causal, scaling)
        return tuple((member.astype(jnp.bfloat16) for member in results))
    stacked = lax.map(per_residue, jnp.arange(STRIDE, dtype=jnp.int32))
    return tuple((member.transpose(2, 0, 1, 3) for member in stacked))

def reference(queries, keys, values, out_grad):
    scaling = 1.0 / math.sqrt(HD)
    query_fixed, query_strided = split_heads(queries)
    key_fixed, key_strided = split_heads(keys)
    value_fixed, value_strided = split_heads(values)
    grad_fixed, grad_strided = split_heads(out_grad)
    fixed_out = fixed_part(query_fixed, key_fixed, value_fixed, grad_fixed, scaling)
    strided_out = strided_part(query_strided, key_strided, value_strided, grad_strided, scaling)
    return (join_heads(fixed_out[0], strided_out[0]), join_heads(fixed_out[1], strided_out[1]), join_heads(fixed_out[2], strided_out[2]), join_heads(fixed_out[3], strided_out[3]))
```

```python
import math

import jax
import jax.numpy as jnp
from jax import lax
from jax.sharding import PartitionSpec as P

HD = 128
STRIDE = 128
SUMMARY = 4


def split_heads(matrix):
    blocks = matrix.shape[0] // STRIDE
    half_heads = matrix.shape[1] // (2 * HD)
    shaped = matrix.reshape(blocks, STRIDE, matrix.shape[1] // (4 * HD), 4, HD)
    fixed = shaped[:, :, :, :2].reshape(blocks, STRIDE, half_heads, HD)
    strided = shaped[:, :, :, 2:].reshape(blocks, STRIDE, half_heads, HD)
    return (fixed, strided)


def join_heads(fixed, strided):
    blocks, positions, half_heads, head_dim = fixed.shape
    paired = jnp.concatenate(
        [
            fixed.reshape(blocks, positions, half_heads // 2, 2, head_dim),
            strided.reshape(blocks, positions, half_heads // 2, 2, head_dim),
        ],
        axis=3,
    )
    return paired.reshape(blocks * positions, 2 * half_heads * head_dim)


def fixed_heads(query, key_rows, value_rows, grad_rows, flat_keys, flat_values, scaling):
    blocks_here, positions, half_heads, head_dim = query.shape
    summary_count = flat_keys.shape[0]
    block_ids = lax.axis_index("ctx") * blocks_here + jnp.arange(blocks_here, dtype=jnp.int32)
    summary_block = jnp.arange(summary_count, dtype=jnp.int32) // SUMMARY
    earlier = (summary_block[None, :] < block_ids[:, None])[:, None, None, :]
    causal = (jnp.arange(positions)[:, None] >= jnp.arange(positions)[None, :])[None, None]
    local_scores = (
        jnp.einsum("bqgd,bkgd->bgqk", query, key_rows, preferred_element_type=jnp.float32) * scaling
    )
    summary_scores = (
        jnp.einsum("bqgd,mgd->bgqm", query, flat_keys, preferred_element_type=jnp.float32) * scaling
    )
    local_scores = jnp.where(causal, local_scores, -jnp.inf)
    summary_scores = jnp.where(earlier, summary_scores, -jnp.inf)
    row_max = jnp.maximum(jnp.max(local_scores, axis=-1), jnp.max(summary_scores, axis=-1))[
        ..., None
    ]
    local_raised = jnp.exp(local_scores - row_max)
    summary_raised = jnp.exp(summary_scores - row_max)
    totals = jnp.sum(local_raised, axis=-1, keepdims=True) + jnp.sum(
        summary_raised, axis=-1, keepdims=True
    )
    local_weights = local_raised / totals
    summary_weights = summary_raised / totals
    local_low = local_weights.astype(jnp.bfloat16)
    summary_low = summary_weights.astype(jnp.bfloat16)
    attended = (
        jnp.einsum("bgqk,bkgd->bqgd", local_low, value_rows, preferred_element_type=jnp.float32)
        + jnp.einsum("bgqm,mgd->bqgd", summary_low, flat_values, preferred_element_type=jnp.float32)
    ).astype(jnp.bfloat16)
    local_dweights = jnp.einsum(
        "bqgd,bkgd->bgqk", grad_rows, value_rows, preferred_element_type=jnp.float32
    )
    summary_dweights = jnp.einsum(
        "bqgd,mgd->bgqm", grad_rows, flat_values, preferred_element_type=jnp.float32
    )
    row_delta = jnp.sum(grad_rows.astype(jnp.float32) * attended.astype(jnp.float32), axis=-1)
    row_delta = jnp.transpose(row_delta, (0, 2, 1))[..., None]
    local_dscores = (local_weights * (local_dweights - row_delta)).astype(jnp.bfloat16)
    summary_dscores = (summary_weights * (summary_dweights - row_delta)).astype(jnp.bfloat16)
    query_grad = (
        jnp.einsum("bgqk,bkgd->bqgd", local_dscores, key_rows, preferred_element_type=jnp.float32)
        + jnp.einsum(
            "bgqm,mgd->bqgd", summary_dscores, flat_keys, preferred_element_type=jnp.float32
        )
    ) * scaling
    key_grad = (
        jnp.einsum("bgqk,bqgd->bkgd", local_dscores, query, preferred_element_type=jnp.float32)
        * scaling
    )
    value_grad = jnp.einsum(
        "bgqk,bqgd->bkgd", local_low, grad_rows, preferred_element_type=jnp.float32
    )
    key_terms = (
        jnp.einsum("bgqm,bqgd->mgd", summary_dscores, query, preferred_element_type=jnp.float32)
        * scaling
    )
    value_terms = jnp.einsum(
        "bgqm,bqgd->mgd", summary_low, grad_rows, preferred_element_type=jnp.float32
    )
    return (attended, query_grad, key_grad, value_grad, jnp.stack([key_terms, value_terms]))


def strided_heads(query_all, keys_all, values_all, grads_all, scaling):
    blocks = query_all.shape[0]
    causal = (jnp.arange(blocks)[:, None] >= jnp.arange(blocks)[None, :])[None, None]
    scores = (
        jnp.einsum("brgd,crgd->rgbc", query_all, keys_all, preferred_element_type=jnp.float32)
        * scaling
    )
    scores = jnp.where(causal, scores, -jnp.inf)
    row_max = jnp.max(scores, axis=-1, keepdims=True)
    raised = jnp.exp(scores - row_max)
    weights = raised / jnp.sum(raised, axis=-1, keepdims=True)
    weights_low = weights.astype(jnp.bfloat16)
    attended = jnp.einsum(
        "rgbc,crgd->brgd", weights_low, values_all, preferred_element_type=jnp.float32
    ).astype(jnp.bfloat16)
    dweights = jnp.einsum(
        "brgd,crgd->rgbc", grads_all, values_all, preferred_element_type=jnp.float32
    )
    row_delta = jnp.sum(grads_all.astype(jnp.float32) * attended.astype(jnp.float32), axis=-1)
    row_delta = jnp.transpose(row_delta, (1, 2, 0))[..., None]
    dscores = (weights * (dweights - row_delta)).astype(jnp.bfloat16)
    query_grad = (
        jnp.einsum("rgbc,crgd->brgd", dscores, keys_all, preferred_element_type=jnp.float32)
        * scaling
    ).astype(jnp.bfloat16)
    key_grad = (
        jnp.einsum("rgbc,brgd->crgd", dscores, query_all, preferred_element_type=jnp.float32)
        * scaling
    ).astype(jnp.bfloat16)
    value_grad = jnp.einsum(
        "rgbc,brgd->crgd", weights_low, grads_all, preferred_element_type=jnp.float32
    ).astype(jnp.bfloat16)
    return jnp.stack([attended, query_grad, key_grad, value_grad])


def shards(queries, keys, values, out_grad):
    scaling = 1.0 / math.sqrt(HD)
    query_fixed, query_strided = split_heads(queries)
    key_fixed, key_strided = split_heads(keys)
    value_fixed, value_strided = split_heads(values)
    grad_fixed, grad_strided = split_heads(out_grad)
    blocks_here, positions, half_heads, head_dim = query_fixed.shape
    peers = lax.axis_size("ctx")
    residues = positions // peers

    strided_rows = jnp.stack([query_strided, key_strided, value_strided, grad_strided])
    strided_rows = strided_rows.reshape(4, blocks_here, peers, residues, half_heads, head_dim)
    strided_rows = strided_rows.transpose(2, 0, 1, 3, 4, 5).reshape(peers, -1)
    summary_rows = jnp.stack(
        [key_fixed[:, positions - SUMMARY :], value_fixed[:, positions - SUMMARY :]]
    ).reshape(1, -1)
    summary_rows = jnp.broadcast_to(summary_rows, (peers, summary_rows.shape[1]))
    strided_size = strided_rows.shape[1]
    received = lax.all_to_all(
        jnp.concatenate([strided_rows, summary_rows], axis=1), "ctx", 0, 0, tiled=True
    )
    gathered = received[:, :strided_size].reshape(
        peers, 4, blocks_here, residues, half_heads, head_dim
    )
    gathered = gathered.transpose(1, 0, 2, 3, 4, 5).reshape(
        4, peers * blocks_here, residues, half_heads, head_dim
    )
    summaries = received[:, strided_size:].reshape(
        peers, 2, blocks_here * SUMMARY, half_heads, head_dim
    )
    summaries = summaries.transpose(1, 0, 2, 3, 4).reshape(
        2, peers * blocks_here * SUMMARY, half_heads, head_dim
    )

    attended, query_grad, key_grad, value_grad, terms = fixed_heads(
        query_fixed,
        key_fixed,
        value_fixed,
        grad_fixed,
        summaries[0],
        summaries[1],
        scaling,
    )
    strided_out = strided_heads(gathered[0], gathered[1], gathered[2], gathered[3], scaling)

    strided_out = strided_out.reshape(4, peers, blocks_here, residues, half_heads, head_dim)
    strided_out = lax.all_to_all(strided_out.reshape(4, peers, -1).transpose(1, 0, 2), "ctx", 0, 0, tiled=True)
    strided_out = strided_out.reshape(peers, 4, blocks_here, residues, half_heads, head_dim)
    strided_out = strided_out.transpose(1, 2, 0, 3, 4, 5).reshape(
        4, blocks_here, positions, half_heads, head_dim
    )
    terms = terms.reshape(2, peers, -1).transpose(1, 0, 2)
    shares = jnp.sum(lax.all_to_all(terms, "ctx", 0, 0, tiled=True), axis=0)
    shares = shares.reshape(2, blocks_here, SUMMARY, half_heads, head_dim)
    key_grad = key_grad.at[:, positions - SUMMARY :].add(shares[0])
    value_grad = value_grad.at[:, positions - SUMMARY :].add(shares[1])
    return (
        join_heads(attended, strided_out[0]),
        join_heads(query_grad.astype(jnp.bfloat16), strided_out[1]),
        join_heads(key_grad.astype(jnp.bfloat16), strided_out[2]),
        join_heads(value_grad.astype(jnp.bfloat16), strided_out[3]),
    )


def solution(mesh):
    return jax.shard_map(
        shards,
        mesh=mesh,
        in_specs=(P("ctx", "head"), P("ctx", "head"), P("ctx", "head"), P("ctx", "head")),
        out_specs=(P("ctx", "head"), P("ctx", "head"), P("ctx", "head"), P("ctx", "head")),
        check_vma=False,
    )
```

```python
import math

import jax
import jax.numpy as jnp
from jax import lax
from jax.sharding import PartitionSpec as P

HD = 128
STRIDE = 128
SUMMARY = 4


def split_heads(matrix):
    blocks = matrix.shape[0] // STRIDE
    half_heads = matrix.shape[1] // (2 * HD)
    shaped = matrix.reshape(blocks, STRIDE, matrix.shape[1] // (4 * HD), 4, HD)
    fixed = shaped[:, :, :, :2].reshape(blocks, STRIDE, half_heads, HD)
    strided = shaped[:, :, :, 2:].reshape(blocks, STRIDE, half_heads, HD)
    return (fixed, strided)


def join_heads(fixed, strided):
    blocks, positions, half_heads, head_dim = fixed.shape
    paired = jnp.concatenate(
        [
            fixed.reshape(blocks, positions, half_heads // 2, 2, head_dim),
            strided.reshape(blocks, positions, half_heads // 2, 2, head_dim),
        ],
        axis=3,
    )
    return paired.reshape(blocks * positions, 2 * half_heads * head_dim)


def fixed_heads(query, key_rows, value_rows, grad_rows, flat_keys, flat_values, scaling):
    blocks_here, positions, half_heads, head_dim = query.shape
    summary_count = flat_keys.shape[0]
    block_ids = lax.axis_index("ctx") * blocks_here + jnp.arange(blocks_here, dtype=jnp.int32)
    summary_block = jnp.arange(summary_count, dtype=jnp.int32) // SUMMARY
    earlier = (summary_block[None, :] < block_ids[:, None])[:, None, None, :]
    causal = (jnp.arange(positions)[:, None] >= jnp.arange(positions)[None, :])[None, None]
    local_scores = (
        jnp.einsum("bqgd,bkgd->bgqk", query, key_rows, preferred_element_type=jnp.float32) * scaling
    )
    summary_scores = (
        jnp.einsum("bqgd,mgd->bgqm", query, flat_keys, preferred_element_type=jnp.float32) * scaling
    )
    local_scores = jnp.where(causal, local_scores, -jnp.inf)
    summary_scores = jnp.where(earlier, summary_scores, -jnp.inf)
    row_max = jnp.maximum(jnp.max(local_scores, axis=-1), jnp.max(summary_scores, axis=-1))[
        ..., None
    ]
    local_raised = jnp.exp(local_scores - row_max)
    summary_raised = jnp.exp(summary_scores - row_max)
    totals = jnp.sum(local_raised, axis=-1, keepdims=True) + jnp.sum(
        summary_raised, axis=-1, keepdims=True
    )
    local_weights = local_raised / totals
    summary_weights = summary_raised / totals
    local_low = local_weights.astype(jnp.bfloat16)
    summary_low = summary_weights.astype(jnp.bfloat16)
    attended = (
        jnp.einsum("bgqk,bkgd->bqgd", local_low, value_rows, preferred_element_type=jnp.float32)
        + jnp.einsum("bgqm,mgd->bqgd", summary_low, flat_values, preferred_element_type=jnp.float32)
    ).astype(jnp.bfloat16)
    local_dweights = jnp.einsum(
        "bqgd,bkgd->bgqk", grad_rows, value_rows, preferred_element_type=jnp.float32
    )
    summary_dweights = jnp.einsum(
        "bqgd,mgd->bgqm", grad_rows, flat_values, preferred_element_type=jnp.float32
    )
    row_delta = jnp.sum(grad_rows.astype(jnp.float32) * attended.astype(jnp.float32), axis=-1)
    row_delta = jnp.transpose(row_delta, (0, 2, 1))[..., None]
    local_dscores = (local_weights * (local_dweights - row_delta)).astype(jnp.bfloat16)
    summary_dscores = (summary_weights * (summary_dweights - row_delta)).astype(jnp.bfloat16)
    query_grad = (
        jnp.einsum("bgqk,bkgd->bqgd", local_dscores, key_rows, preferred_element_type=jnp.float32)
        + jnp.einsum(
            "bgqm,mgd->bqgd", summary_dscores, flat_keys, preferred_element_type=jnp.float32
        )
    ) * scaling
    key_grad = (
        jnp.einsum("bgqk,bqgd->bkgd", local_dscores, query, preferred_element_type=jnp.float32)
        * scaling
    )
    value_grad = jnp.einsum(
        "bgqk,bqgd->bkgd", local_low, grad_rows, preferred_element_type=jnp.float32
    )
    key_terms = (
        jnp.einsum("bgqm,bqgd->mgd", summary_dscores, query, preferred_element_type=jnp.float32)
        * scaling
    )
    value_terms = jnp.einsum(
        "bgqm,bqgd->mgd", summary_low, grad_rows, preferred_element_type=jnp.float32
    )
    return (attended, query_grad, key_grad, value_grad, jnp.stack([key_terms, value_terms]))


def strided_heads(query_all, keys_all, values_all, grads_all, scaling):
    blocks = query_all.shape[0]
    causal = (jnp.arange(blocks)[:, None] >= jnp.arange(blocks)[None, :])[None, None]
    scores = (
        jnp.einsum("brgd,crgd->rgbc", query_all, keys_all, preferred_element_type=jnp.float32)
        * scaling
    )
    scores = jnp.where(causal, scores, -jnp.inf)
    row_max = jnp.max(scores, axis=-1, keepdims=True)
    raised = jnp.exp(scores - row_max)
    weights = raised / jnp.sum(raised, axis=-1, keepdims=True)
    weights_low = weights.astype(jnp.bfloat16)
    attended = jnp.einsum(
        "rgbc,crgd->brgd", weights_low, values_all, preferred_element_type=jnp.float32
    ).astype(jnp.bfloat16)
    dweights = jnp.einsum(
        "brgd,crgd->rgbc", grads_all, values_all, preferred_element_type=jnp.float32
    )
    row_delta = jnp.sum(grads_all.astype(jnp.float32) * attended.astype(jnp.float32), axis=-1)
    row_delta = jnp.transpose(row_delta, (1, 2, 0))[..., None]
    dscores = (weights * (dweights - row_delta)).astype(jnp.bfloat16)
    query_grad = (
        jnp.einsum("rgbc,crgd->brgd", dscores, keys_all, preferred_element_type=jnp.float32)
        * scaling
    ).astype(jnp.bfloat16)
    key_grad = (
        jnp.einsum("rgbc,brgd->crgd", dscores, query_all, preferred_element_type=jnp.float32)
        * scaling
    ).astype(jnp.bfloat16)
    value_grad = jnp.einsum(
        "rgbc,brgd->crgd", weights_low, grads_all, preferred_element_type=jnp.float32
    ).astype(jnp.bfloat16)
    return jnp.stack([attended, query_grad, key_grad, value_grad])


def shards(queries, keys, values, out_grad):
    scaling = 1.0 / math.sqrt(HD)
    query_fixed, query_strided = split_heads(queries)
    key_fixed, key_strided = split_heads(keys)
    value_fixed, value_strided = split_heads(values)
    grad_fixed, grad_strided = split_heads(out_grad)
    blocks_here, positions, half_heads, head_dim = query_fixed.shape
    peers = lax.axis_size("ctx")
    residues = positions // peers

    strided_rows = jnp.stack([query_strided, key_strided, value_strided, grad_strided])
    strided_rows = strided_rows.reshape(4, blocks_here, peers, residues, half_heads, head_dim)
    strided_rows = strided_rows.transpose(2, 0, 1, 3, 4, 5).reshape(peers, -1)
    summary_rows = jnp.stack(
        [key_fixed[:, positions - SUMMARY :], value_fixed[:, positions - SUMMARY :]]
    ).reshape(1, -1)
    summary_rows = jnp.broadcast_to(summary_rows, (peers, summary_rows.shape[1]))
    strided_size = strided_rows.shape[1]
    received = lax.all_to_all(
        jnp.concatenate([strided_rows, summary_rows], axis=1), "ctx", 0, 0, tiled=True
    )
    gathered = received[:, :strided_size].reshape(
        peers, 4, blocks_here, residues, half_heads, head_dim
    )
    gathered = gathered.transpose(1, 0, 2, 3, 4, 5).reshape(
        4, peers * blocks_here, residues, half_heads, head_dim
    )
    summaries = received[:, strided_size:].reshape(
        peers, 2, blocks_here * SUMMARY, half_heads, head_dim
    )
    summaries = summaries.transpose(1, 0, 2, 3, 4).reshape(
        2, peers * blocks_here * SUMMARY, half_heads, head_dim
    )

    attended, query_grad, key_grad, value_grad, terms = fixed_heads(
        query_fixed,
        key_fixed,
        value_fixed,
        grad_fixed,
        summaries[0],
        summaries[1],
        scaling,
    )
    strided_out = strided_heads(gathered[0], gathered[1], gathered[2], gathered[3], scaling)

    strided_out = strided_out.reshape(4, peers, -1).transpose(1, 0, 2).reshape(peers, -1)
    terms = terms.astype(jnp.bfloat16).reshape(2, peers, -1).transpose(1, 0, 2).reshape(peers, -1)
    returned = lax.all_to_all(
        jnp.concatenate([strided_out, terms], axis=1), "ctx", 0, 0, tiled=True
    )
    strided_out = returned[:, :strided_size].reshape(
        peers, 4, blocks_here, residues, half_heads, head_dim
    )
    strided_out = strided_out.transpose(1, 2, 0, 3, 4, 5).reshape(
        4, blocks_here, positions, half_heads, head_dim
    )
    shares = jnp.sum(returned[:, strided_size:].astype(jnp.float32), axis=0)
    shares = shares.reshape(2, blocks_here, SUMMARY, half_heads, head_dim)
    key_grad = key_grad.at[:, positions - SUMMARY :].add(shares[0])
    value_grad = value_grad.at[:, positions - SUMMARY :].add(shares[1])
    return (
        join_heads(attended, strided_out[0]),
        join_heads(query_grad.astype(jnp.bfloat16), strided_out[1]),
        join_heads(key_grad.astype(jnp.bfloat16), strided_out[2]),
        join_heads(value_grad.astype(jnp.bfloat16), strided_out[3]),
    )


def solution(mesh):
    return jax.shard_map(
        shards,
        mesh=mesh,
        in_specs=(P("ctx", "head"), P("ctx", "head"), P("ctx", "head"), P("ctx", "head")),
        out_specs=(P("ctx", "head"), P("ctx", "head"), P("ctx", "head"), P("ctx", "head")),
        check_vma=False,
    )
```

```python
import math

import jax
import jax.numpy as jnp
from jax import lax
from jax.sharding import PartitionSpec as P

HD = 128
STRIDE = 128
SUMMARY = 4


def split_heads(matrix):
    blocks = matrix.shape[0] // STRIDE
    half_heads = matrix.shape[1] // (2 * HD)
    shaped = matrix.reshape(blocks, STRIDE, matrix.shape[1] // (4 * HD), 4, HD)
    fixed = shaped[:, :, :, :2].reshape(blocks, STRIDE, half_heads, HD)
    strided = shaped[:, :, :, 2:].reshape(blocks, STRIDE, half_heads, HD)
    return (fixed, strided)


def join_heads(fixed, strided):
    blocks, positions, half_heads, head_dim = fixed.shape
    paired = jnp.concatenate(
        [
            fixed.reshape(blocks, positions, half_heads // 2, 2, head_dim),
            strided.reshape(blocks, positions, half_heads // 2, 2, head_dim),
        ],
        axis=3,
    )
    return paired.reshape(blocks * positions, 2 * half_heads * head_dim)


def fixed_heads(query, key_rows, value_rows, grad_rows, flat_keys, flat_values, scaling):
    blocks_here, positions, half_heads, head_dim = query.shape
    summary_count = flat_keys.shape[0]
    block_ids = lax.axis_index("ctx") * blocks_here + jnp.arange(blocks_here, dtype=jnp.int32)
    summary_block = jnp.arange(summary_count, dtype=jnp.int32) // SUMMARY
    earlier = (summary_block[None, :] < block_ids[:, None])[:, None, None, :]
    causal = (jnp.arange(positions)[:, None] >= jnp.arange(positions)[None, :])[None, None]
    local_scores = (
        jnp.einsum("bqgd,bkgd->bgqk", query, key_rows, preferred_element_type=jnp.float32) * scaling
    )
    summary_scores = (
        jnp.einsum("bqgd,mgd->bgqm", query, flat_keys, preferred_element_type=jnp.float32) * scaling
    )
    local_scores = jnp.where(causal, local_scores, -jnp.inf)
    summary_scores = jnp.where(earlier, summary_scores, -jnp.inf)
    row_max = jnp.maximum(jnp.max(local_scores, axis=-1), jnp.max(summary_scores, axis=-1))[
        ..., None
    ]
    local_raised = jnp.exp(local_scores - row_max)
    summary_raised = jnp.exp(summary_scores - row_max)
    totals = jnp.sum(local_raised, axis=-1, keepdims=True) + jnp.sum(
        summary_raised, axis=-1, keepdims=True
    )
    local_weights = local_raised / totals
    summary_weights = summary_raised / totals
    local_low = local_weights.astype(jnp.bfloat16)
    summary_low = summary_weights.astype(jnp.bfloat16)
    attended = (
        jnp.einsum("bgqk,bkgd->bqgd", local_low, value_rows, preferred_element_type=jnp.float32)
        + jnp.einsum("bgqm,mgd->bqgd", summary_low, flat_values, preferred_element_type=jnp.float32)
    ).astype(jnp.bfloat16)
    local_dweights = jnp.einsum(
        "bqgd,bkgd->bgqk", grad_rows, value_rows, preferred_element_type=jnp.float32
    )
    summary_dweights = jnp.einsum(
        "bqgd,mgd->bgqm", grad_rows, flat_values, preferred_element_type=jnp.float32
    )
    row_delta = jnp.sum(grad_rows.astype(jnp.float32) * attended.astype(jnp.float32), axis=-1)
    row_delta = jnp.transpose(row_delta, (0, 2, 1))[..., None]
    local_dscores = (local_weights * (local_dweights - row_delta)).astype(jnp.bfloat16)
    summary_dscores = (summary_weights * (summary_dweights - row_delta)).astype(jnp.bfloat16)
    query_grad = (
        jnp.einsum("bgqk,bkgd->bqgd", local_dscores, key_rows, preferred_element_type=jnp.float32)
        + jnp.einsum(
            "bgqm,mgd->bqgd", summary_dscores, flat_keys, preferred_element_type=jnp.float32
        )
    ) * scaling
    key_grad = (
        jnp.einsum("bgqk,bqgd->bkgd", local_dscores, query, preferred_element_type=jnp.float32)
        * scaling
    )
    value_grad = jnp.einsum(
        "bgqk,bqgd->bkgd", local_low, grad_rows, preferred_element_type=jnp.float32
    )
    key_terms = (
        jnp.einsum("bgqm,bqgd->mgd", summary_dscores, query, preferred_element_type=jnp.float32)
        * scaling
    )
    value_terms = jnp.einsum(
        "bgqm,bqgd->mgd", summary_low, grad_rows, preferred_element_type=jnp.float32
    )
    return (attended, query_grad, key_grad, value_grad, jnp.stack([key_terms, value_terms]))


def strided_heads(query_all, keys_all, values_all, grads_all, scaling):
    blocks = query_all.shape[0]
    causal = (jnp.arange(blocks)[:, None] >= jnp.arange(blocks)[None, :])[None, None]
    scores = (
        jnp.einsum("brgd,crgd->rgbc", query_all, keys_all, preferred_element_type=jnp.float32)
        * scaling
    )
    scores = jnp.where(causal, scores, -jnp.inf)
    row_max = jnp.max(scores, axis=-1, keepdims=True)
    raised = jnp.exp(scores - row_max)
    weights = raised / jnp.sum(raised, axis=-1, keepdims=True)
    weights_low = weights.astype(jnp.bfloat16)
    attended = jnp.einsum(
        "rgbc,crgd->brgd", weights_low, values_all, preferred_element_type=jnp.float32
    ).astype(jnp.bfloat16)
    dweights = jnp.einsum(
        "brgd,crgd->rgbc", grads_all, values_all, preferred_element_type=jnp.float32
    )
    row_delta = jnp.sum(grads_all.astype(jnp.float32) * attended.astype(jnp.float32), axis=-1)
    row_delta = jnp.transpose(row_delta, (1, 2, 0))[..., None]
    dscores = (weights * (dweights - row_delta)).astype(jnp.bfloat16)
    query_grad = (
        jnp.einsum("rgbc,crgd->brgd", dscores, keys_all, preferred_element_type=jnp.float32)
        * scaling
    ).astype(jnp.bfloat16)
    key_grad = (
        jnp.einsum("rgbc,brgd->crgd", dscores, query_all, preferred_element_type=jnp.float32)
        * scaling
    ).astype(jnp.bfloat16)
    value_grad = jnp.einsum(
        "rgbc,brgd->crgd", weights_low, grads_all, preferred_element_type=jnp.float32
    ).astype(jnp.bfloat16)
    return jnp.stack([attended, query_grad, key_grad, value_grad])


def shards(queries, keys, values, out_grad):
    scaling = 1.0 / math.sqrt(HD)
    query_fixed, query_strided = split_heads(queries)
    key_fixed, key_strided = split_heads(keys)
    value_fixed, value_strided = split_heads(values)
    grad_fixed, grad_strided = split_heads(out_grad)
    blocks_here, positions, half_heads, head_dim = query_fixed.shape
    peers = lax.axis_size("ctx")
    residues = positions // peers

    strided_rows = jnp.stack([query_strided, key_strided, value_strided, grad_strided])
    strided_rows = strided_rows.reshape(4, blocks_here, peers, residues, half_heads, head_dim)
    strided_rows = strided_rows.transpose(2, 0, 1, 3, 4, 5).reshape(peers, -1, head_dim)
    summary_rows = jnp.stack(
        [key_fixed[:, positions - SUMMARY :], value_fixed[:, positions - SUMMARY :]]
    ).reshape(1, -1, head_dim)
    summary_rows = jnp.broadcast_to(summary_rows, (peers,) + summary_rows.shape[1:])
    strided_size = strided_rows.shape[1]
    received = lax.all_to_all(
        jnp.concatenate([strided_rows, summary_rows], axis=1), "ctx", 0, 0, tiled=True
    )
    gathered = received[:, :strided_size].reshape(
        peers, 4, blocks_here, residues, half_heads, head_dim
    )
    gathered = gathered.transpose(1, 0, 2, 3, 4, 5).reshape(
        4, peers * blocks_here, residues, half_heads, head_dim
    )
    summaries = received[:, strided_size:].reshape(
        peers, 2, blocks_here * SUMMARY, half_heads, head_dim
    )
    summaries = summaries.transpose(1, 0, 2, 3, 4).reshape(
        2, peers * blocks_here * SUMMARY, half_heads, head_dim
    )

    attended, query_grad, key_grad, value_grad, terms = fixed_heads(
        query_fixed,
        key_fixed,
        value_fixed,
        grad_fixed,
        summaries[0],
        summaries[1],
        scaling,
    )
    strided_out = strided_heads(gathered[0], gathered[1], gathered[2], gathered[3], scaling)

    strided_out = strided_out.reshape(4, peers, -1, head_dim).transpose(1, 0, 2, 3)
    strided_out = strided_out.reshape(peers, -1, head_dim)
    terms = terms.astype(jnp.bfloat16).reshape(2, peers, -1, head_dim).transpose(1, 0, 2, 3)
    terms = terms.reshape(peers, -1, head_dim)
    returned = lax.all_to_all(
        jnp.concatenate([strided_out, terms], axis=1), "ctx", 0, 0, tiled=True
    )
    strided_out = returned[:, :strided_size].reshape(
        peers, 4, blocks_here, residues, half_heads, head_dim
    )
    strided_out = strided_out.transpose(1, 2, 0, 3, 4, 5).reshape(
        4, blocks_here, positions, half_heads, head_dim
    )
    shares = jnp.sum(returned[:, strided_size:].astype(jnp.float32), axis=0)
    shares = shares.reshape(2, blocks_here, SUMMARY, half_heads, head_dim)
    key_grad = key_grad.at[:, positions - SUMMARY :].add(shares[0])
    value_grad = value_grad.at[:, positions - SUMMARY :].add(shares[1])
    return (
        join_heads(attended, strided_out[0]),
        join_heads(query_grad.astype(jnp.bfloat16), strided_out[1]),
        join_heads(key_grad.astype(jnp.bfloat16), strided_out[2]),
        join_heads(value_grad.astype(jnp.bfloat16), strided_out[3]),
    )


def solution(mesh):
    return jax.shard_map(
        shards,
        mesh=mesh,
        in_specs=(P("ctx", "head"), P("ctx", "head"), P("ctx", "head"), P("ctx", "head")),
        out_specs=(P("ctx", "head"), P("ctx", "head"), P("ctx", "head"), P("ctx", "head")),
        check_vma=False,
    )
```

```python
import math

import jax
import jax.numpy as jnp
from jax import lax
from jax.sharding import Mesh, PartitionSpec as P

HD = 128
STRIDE = 128
SUMMARY = 4


def split_heads(matrix):
    blocks = matrix.shape[0] // STRIDE
    half_heads = matrix.shape[1] // (2 * HD)
    shaped = matrix.reshape(blocks, STRIDE, matrix.shape[1] // (4 * HD), 4, HD)
    fixed = shaped[:, :, :, :2].reshape(blocks, STRIDE, half_heads, HD)
    strided = shaped[:, :, :, 2:].reshape(blocks, STRIDE, half_heads, HD)
    return (fixed, strided)


def join_heads(fixed, strided):
    blocks, positions, half_heads, head_dim = fixed.shape
    paired = jnp.concatenate(
        [
            fixed.reshape(blocks, positions, half_heads // 2, 2, head_dim),
            strided.reshape(blocks, positions, half_heads // 2, 2, head_dim),
        ],
        axis=3,
    )
    return paired.reshape(blocks * positions, 2 * half_heads * head_dim)


def fixed_heads(query, key_rows, value_rows, grad_rows, flat_keys, flat_values, scaling, here):
    blocks_here, positions, half_heads, head_dim = query.shape
    summary_count = flat_keys.shape[0]
    block_ids = here * blocks_here + jnp.arange(blocks_here, dtype=jnp.int32)
    summary_block = jnp.arange(summary_count, dtype=jnp.int32) // SUMMARY
    earlier = (summary_block[None, :] < block_ids[:, None])[:, None, None, :]
    causal = (jnp.arange(positions)[:, None] >= jnp.arange(positions)[None, :])[None, None]
    local_scores = (
        jnp.einsum("bqgd,bkgd->bgqk", query, key_rows, preferred_element_type=jnp.float32) * scaling
    )
    summary_scores = (
        jnp.einsum("bqgd,mgd->bgqm", query, flat_keys, preferred_element_type=jnp.float32) * scaling
    )
    local_scores = jnp.where(causal, local_scores, -jnp.inf)
    summary_scores = jnp.where(earlier, summary_scores, -jnp.inf)
    row_max = jnp.maximum(jnp.max(local_scores, axis=-1), jnp.max(summary_scores, axis=-1))[
        ..., None
    ]
    local_raised = jnp.exp(local_scores - row_max)
    summary_raised = jnp.exp(summary_scores - row_max)
    totals = jnp.sum(local_raised, axis=-1, keepdims=True) + jnp.sum(
        summary_raised, axis=-1, keepdims=True
    )
    local_weights = local_raised / totals
    summary_weights = summary_raised / totals
    local_low = local_weights.astype(jnp.bfloat16)
    summary_low = summary_weights.astype(jnp.bfloat16)
    attended = (
        jnp.einsum("bgqk,bkgd->bqgd", local_low, value_rows, preferred_element_type=jnp.float32)
        + jnp.einsum("bgqm,mgd->bqgd", summary_low, flat_values, preferred_element_type=jnp.float32)
    ).astype(jnp.bfloat16)
    local_dweights = jnp.einsum(
        "bqgd,bkgd->bgqk", grad_rows, value_rows, preferred_element_type=jnp.float32
    )
    summary_dweights = jnp.einsum(
        "bqgd,mgd->bgqm", grad_rows, flat_values, preferred_element_type=jnp.float32
    )
    row_delta = jnp.sum(grad_rows.astype(jnp.float32) * attended.astype(jnp.float32), axis=-1)
    row_delta = jnp.transpose(row_delta, (0, 2, 1))[..., None]
    local_dscores = (local_weights * (local_dweights - row_delta)).astype(jnp.bfloat16)
    summary_dscores = (summary_weights * (summary_dweights - row_delta)).astype(jnp.bfloat16)
    query_grad = (
        jnp.einsum("bgqk,bkgd->bqgd", local_dscores, key_rows, preferred_element_type=jnp.float32)
        + jnp.einsum(
            "bgqm,mgd->bqgd", summary_dscores, flat_keys, preferred_element_type=jnp.float32
        )
    ) * scaling
    key_grad = (
        jnp.einsum("bgqk,bqgd->bkgd", local_dscores, query, preferred_element_type=jnp.float32)
        * scaling
    )
    value_grad = jnp.einsum(
        "bgqk,bqgd->bkgd", local_low, grad_rows, preferred_element_type=jnp.float32
    )
    key_terms = (
        jnp.einsum("bgqm,bqgd->mgd", summary_dscores, query, preferred_element_type=jnp.float32)
        * scaling
    )
    value_terms = jnp.einsum(
        "bgqm,bqgd->mgd", summary_low, grad_rows, preferred_element_type=jnp.float32
    )
    return (attended, query_grad, key_grad, value_grad, jnp.stack([key_terms, value_terms]))


def strided_heads(query_all, keys_all, values_all, grads_all, scaling):
    blocks = query_all.shape[0]
    causal = (jnp.arange(blocks)[:, None] >= jnp.arange(blocks)[None, :])[None, None]
    scores = (
        jnp.einsum("brgd,crgd->rgbc", query_all, keys_all, preferred_element_type=jnp.float32)
        * scaling
    )
    scores = jnp.where(causal, scores, -jnp.inf)
    row_max = jnp.max(scores, axis=-1, keepdims=True)
    raised = jnp.exp(scores - row_max)
    weights = raised / jnp.sum(raised, axis=-1, keepdims=True)
    weights_low = weights.astype(jnp.bfloat16)
    attended = jnp.einsum(
        "rgbc,crgd->brgd", weights_low, values_all, preferred_element_type=jnp.float32
    ).astype(jnp.bfloat16)
    dweights = jnp.einsum(
        "brgd,crgd->rgbc", grads_all, values_all, preferred_element_type=jnp.float32
    )
    row_delta = jnp.sum(grads_all.astype(jnp.float32) * attended.astype(jnp.float32), axis=-1)
    row_delta = jnp.transpose(row_delta, (1, 2, 0))[..., None]
    dscores = (weights * (dweights - row_delta)).astype(jnp.bfloat16)
    query_grad = (
        jnp.einsum("rgbc,crgd->brgd", dscores, keys_all, preferred_element_type=jnp.float32)
        * scaling
    ).astype(jnp.bfloat16)
    key_grad = (
        jnp.einsum("rgbc,brgd->crgd", dscores, query_all, preferred_element_type=jnp.float32)
        * scaling
    ).astype(jnp.bfloat16)
    value_grad = jnp.einsum(
        "rgbc,brgd->crgd", weights_low, grads_all, preferred_element_type=jnp.float32
    ).astype(jnp.bfloat16)
    return jnp.stack([attended, query_grad, key_grad, value_grad])


def exchange(rows, axis):
    return lax.all_to_all(rows, axis, 0, 0, tiled=True)


def shards(queries, keys, values, out_grad):
    scaling = 1.0 / math.sqrt(HD)
    query_fixed, query_strided = split_heads(queries)
    key_fixed, key_strided = split_heads(keys)
    value_fixed, value_strided = split_heads(values)
    grad_fixed, grad_strided = split_heads(out_grad)
    blocks_here, positions, half_heads, head_dim = query_fixed.shape
    high = lax.axis_size("ctx_hi")
    low = lax.axis_size("ctx_lo")
    peers = high * low
    residues = positions // peers
    here = lax.axis_index("ctx_hi") * low + lax.axis_index("ctx_lo")

    strided_rows = jnp.stack([query_strided, key_strided, value_strided, grad_strided])
    strided_rows = strided_rows.reshape(4, blocks_here, high, low, residues, half_heads, head_dim)
    strided_rows = strided_rows.transpose(3, 0, 1, 2, 4, 5, 6).reshape(low, -1, head_dim)
    summary_rows = jnp.stack(
        [key_fixed[:, positions - SUMMARY :], value_fixed[:, positions - SUMMARY :]]
    ).reshape(1, -1, head_dim)
    summary_size = summary_rows.shape[1]
    summary_rows = jnp.broadcast_to(summary_rows, (low, summary_size, head_dim))
    strided_size = strided_rows.shape[1]
    first = exchange(jnp.concatenate([strided_rows, summary_rows], axis=1), "ctx_lo")
    strided_rows = first[:, :strided_size].reshape(
        low, 4, blocks_here, high, residues, half_heads, head_dim
    )
    strided_rows = strided_rows.transpose(3, 0, 1, 2, 4, 5, 6).reshape(high, -1, head_dim)
    summary_rows = first[:, strided_size:].reshape(1, low * summary_size, head_dim)
    summary_rows = jnp.broadcast_to(summary_rows, (high, low * summary_size, head_dim))
    plane_size = strided_rows.shape[1]
    second = exchange(jnp.concatenate([strided_rows, summary_rows], axis=1), "ctx_hi")
    gathered = second[:, :plane_size].reshape(
        high, low, 4, blocks_here, residues, half_heads, head_dim
    )
    gathered = gathered.transpose(2, 0, 1, 3, 4, 5, 6).reshape(
        4, peers * blocks_here, residues, half_heads, head_dim
    )
    summaries = second[:, plane_size:].reshape(
        peers, 2, blocks_here * SUMMARY, half_heads, head_dim
    )
    summaries = summaries.transpose(1, 0, 2, 3, 4).reshape(
        2, peers * blocks_here * SUMMARY, half_heads, head_dim
    )

    attended, query_grad, key_grad, value_grad, terms = fixed_heads(
        query_fixed,
        key_fixed,
        value_fixed,
        grad_fixed,
        summaries[0],
        summaries[1],
        scaling,
        here,
    )
    strided_out = strided_heads(gathered[0], gathered[1], gathered[2], gathered[3], scaling)

    strided_out = strided_out.reshape(
        4, high, low, blocks_here, residues, half_heads, head_dim
    ).transpose(1, 2, 0, 3, 4, 5, 6)
    strided_out = strided_out.reshape(high, -1, head_dim)
    terms = terms.astype(jnp.bfloat16).reshape(2, high, low, -1, head_dim)
    terms = terms.transpose(1, 2, 0, 3, 4).reshape(high, -1, head_dim)
    back = exchange(jnp.concatenate([strided_out, terms], axis=1), "ctx_hi")
    strided_out = back[:, :plane_size].reshape(
        high, low, 4, blocks_here, residues, half_heads, head_dim
    )
    strided_out = strided_out.transpose(1, 0, 2, 3, 4, 5, 6).reshape(low, -1, head_dim)
    terms = jnp.sum(back[:, plane_size:].astype(jnp.float32), axis=0).astype(jnp.bfloat16)
    terms = terms.reshape(low, -1, head_dim)
    back = exchange(jnp.concatenate([strided_out, terms], axis=1), "ctx_lo")
    strided_out = back[:, :strided_size].reshape(
        low, high, 4, blocks_here, residues, half_heads, head_dim
    )
    strided_out = strided_out.transpose(2, 3, 1, 0, 4, 5, 6).reshape(
        4, blocks_here, positions, half_heads, head_dim
    )
    shares = jnp.sum(back[:, strided_size:].astype(jnp.float32), axis=0)
    shares = shares.reshape(2, blocks_here, SUMMARY, half_heads, head_dim)
    key_grad = jnp.concatenate(
        [key_grad[:, : positions - SUMMARY], key_grad[:, positions - SUMMARY :] + shares[0]], axis=1
    )
    value_grad = jnp.concatenate(
        [value_grad[:, : positions - SUMMARY], value_grad[:, positions - SUMMARY :] + shares[1]],
        axis=1,
    )
    return (
        join_heads(attended, strided_out[0]),
        join_heads(query_grad.astype(jnp.bfloat16), strided_out[1]),
        join_heads(key_grad.astype(jnp.bfloat16), strided_out[2]),
        join_heads(value_grad.astype(jnp.bfloat16), strided_out[3]),
    )


def solution(mesh):
    peers, heads = mesh.devices.shape
    high = 4 if peers % 4 == 0 else 1
    split = Mesh(mesh.devices.reshape(high, peers // high, heads), ("ctx_hi", "ctx_lo", "head"))
    spec = P(("ctx_hi", "ctx_lo"), "head")
    return jax.shard_map(
        shards,
        mesh=split,
        in_specs=(spec, spec, spec, spec),
        out_specs=(spec, spec, spec, spec),
        check_vma=False,
    )
```

```python
import math

import jax
import jax.numpy as jnp
from jax import lax
from jax.sharding import PartitionSpec as P

HD = 128
STRIDE = 128
SUMMARY = 4


def split_heads(matrix):
    blocks = matrix.shape[0] // STRIDE
    half_heads = matrix.shape[1] // (2 * HD)
    shaped = matrix.reshape(blocks, STRIDE, matrix.shape[1] // (4 * HD), 4, HD)
    fixed = shaped[:, :, :, :2].reshape(blocks, STRIDE, half_heads, HD)
    strided = shaped[:, :, :, 2:].reshape(blocks, STRIDE, half_heads, HD)
    return (fixed, strided)


def join_heads(fixed, strided):
    blocks, positions, half_heads, head_dim = fixed.shape
    paired = jnp.concatenate(
        [
            fixed.reshape(blocks, positions, half_heads // 2, 2, head_dim),
            strided.reshape(blocks, positions, half_heads // 2, 2, head_dim),
        ],
        axis=3,
    )
    return paired.reshape(blocks * positions, 2 * half_heads * head_dim)


def fixed_heads(query, key_rows, value_rows, grad_rows, flat_keys, flat_values, scaling):
    blocks_here, positions, half_heads, head_dim = query.shape
    summary_count = flat_keys.shape[0]
    block_ids = lax.axis_index("ctx") * blocks_here + jnp.arange(blocks_here, dtype=jnp.int32)
    summary_block = jnp.arange(summary_count, dtype=jnp.int32) // SUMMARY
    earlier = (summary_block[None, :] < block_ids[:, None])[:, None, None, :]
    causal = (jnp.arange(positions)[:, None] >= jnp.arange(positions)[None, :])[None, None]
    local_scores = (
        jnp.einsum("bqgd,bkgd->bgqk", query, key_rows, preferred_element_type=jnp.float32) * scaling
    )
    summary_scores = (
        jnp.einsum("bqgd,mgd->bgqm", query, flat_keys, preferred_element_type=jnp.float32) * scaling
    )
    local_scores = jnp.where(causal, local_scores, -jnp.inf)
    summary_scores = jnp.where(earlier, summary_scores, -jnp.inf)
    row_max = jnp.maximum(jnp.max(local_scores, axis=-1), jnp.max(summary_scores, axis=-1))[
        ..., None
    ]
    local_raised = jnp.exp(local_scores - row_max)
    summary_raised = jnp.exp(summary_scores - row_max)
    totals = jnp.sum(local_raised, axis=-1, keepdims=True) + jnp.sum(
        summary_raised, axis=-1, keepdims=True
    )
    local_weights = local_raised / totals
    summary_weights = summary_raised / totals
    local_low = local_weights.astype(jnp.bfloat16)
    summary_low = summary_weights.astype(jnp.bfloat16)
    attended = (
        jnp.einsum("bgqk,bkgd->bqgd", local_low, value_rows, preferred_element_type=jnp.float32)
        + jnp.einsum("bgqm,mgd->bqgd", summary_low, flat_values, preferred_element_type=jnp.float32)
    ).astype(jnp.bfloat16)
    local_dweights = jnp.einsum(
        "bqgd,bkgd->bgqk", grad_rows, value_rows, preferred_element_type=jnp.float32
    )
    summary_dweights = jnp.einsum(
        "bqgd,mgd->bgqm", grad_rows, flat_values, preferred_element_type=jnp.float32
    )
    row_delta = jnp.sum(grad_rows.astype(jnp.float32) * attended.astype(jnp.float32), axis=-1)
    row_delta = jnp.transpose(row_delta, (0, 2, 1))[..., None]
    local_dscores = (local_weights * (local_dweights - row_delta)).astype(jnp.bfloat16)
    summary_dscores = (summary_weights * (summary_dweights - row_delta)).astype(jnp.bfloat16)
    query_grad = (
        jnp.einsum("bgqk,bkgd->bqgd", local_dscores, key_rows, preferred_element_type=jnp.float32)
        + jnp.einsum(
            "bgqm,mgd->bqgd", summary_dscores, flat_keys, preferred_element_type=jnp.float32
        )
    ) * scaling
    key_grad = (
        jnp.einsum("bgqk,bqgd->bkgd", local_dscores, query, preferred_element_type=jnp.float32)
        * scaling
    )
    value_grad = jnp.einsum(
        "bgqk,bqgd->bkgd", local_low, grad_rows, preferred_element_type=jnp.float32
    )
    key_terms = (
        jnp.einsum("bgqm,bqgd->mgd", summary_dscores, query, preferred_element_type=jnp.float32)
        * scaling
    )
    value_terms = jnp.einsum(
        "bgqm,bqgd->mgd", summary_low, grad_rows, preferred_element_type=jnp.float32
    )
    return (attended, query_grad, key_grad, value_grad, jnp.stack([key_terms, value_terms]))


def strided_heads(query_all, keys_all, values_all, grads_all, scaling):
    blocks = query_all.shape[0]
    causal = (jnp.arange(blocks)[:, None] >= jnp.arange(blocks)[None, :])[None, None]
    scores = (
        jnp.einsum("brgd,crgd->rgbc", query_all, keys_all, preferred_element_type=jnp.float32)
        * scaling
    )
    scores = jnp.where(causal, scores, -jnp.inf)
    row_max = jnp.max(scores, axis=-1, keepdims=True)
    raised = jnp.exp(scores - row_max)
    weights = raised / jnp.sum(raised, axis=-1, keepdims=True)
    weights_low = weights.astype(jnp.bfloat16)
    attended = jnp.einsum(
        "rgbc,crgd->brgd", weights_low, values_all, preferred_element_type=jnp.float32
    ).astype(jnp.bfloat16)
    dweights = jnp.einsum(
        "brgd,crgd->rgbc", grads_all, values_all, preferred_element_type=jnp.float32
    )
    row_delta = jnp.sum(grads_all.astype(jnp.float32) * attended.astype(jnp.float32), axis=-1)
    row_delta = jnp.transpose(row_delta, (1, 2, 0))[..., None]
    dscores = (weights * (dweights - row_delta)).astype(jnp.bfloat16)
    query_grad = (
        jnp.einsum("rgbc,crgd->brgd", dscores, keys_all, preferred_element_type=jnp.float32)
        * scaling
    ).astype(jnp.bfloat16)
    key_grad = (
        jnp.einsum("rgbc,brgd->crgd", dscores, query_all, preferred_element_type=jnp.float32)
        * scaling
    ).astype(jnp.bfloat16)
    value_grad = jnp.einsum(
        "rgbc,brgd->crgd", weights_low, grads_all, preferred_element_type=jnp.float32
    ).astype(jnp.bfloat16)
    return jnp.stack([attended, query_grad, key_grad, value_grad])


def shards(queries, keys, values, out_grad):
    scaling = 1.0 / math.sqrt(HD)
    query_fixed, query_strided = split_heads(queries)
    key_fixed, key_strided = split_heads(keys)
    value_fixed, value_strided = split_heads(values)
    grad_fixed, grad_strided = split_heads(out_grad)
    blocks_here, positions, half_heads, head_dim = query_fixed.shape
    peers = lax.axis_size("ctx")
    residues = positions // peers

    strided_rows = jnp.stack([query_strided, key_strided, value_strided, grad_strided])
    strided_rows = strided_rows.reshape(4, blocks_here, peers, residues, half_heads, head_dim)
    strided_rows = strided_rows.transpose(2, 0, 1, 3, 4, 5).reshape(peers, -1, head_dim)
    summary_rows = jnp.stack(
        [key_fixed[:, positions - SUMMARY :], value_fixed[:, positions - SUMMARY :]]
    ).reshape(1, -1, head_dim)
    summary_rows = jnp.broadcast_to(summary_rows, (peers,) + summary_rows.shape[1:])
    strided_size = strided_rows.shape[1]
    received = lax.all_to_all(
        jnp.concatenate([strided_rows, summary_rows], axis=1), "ctx", 0, 0, tiled=True
    )
    gathered = received[:, :strided_size].reshape(
        peers, 4, blocks_here, residues, half_heads, head_dim
    )
    gathered = gathered.transpose(1, 0, 2, 3, 4, 5).reshape(
        4, peers * blocks_here, residues, half_heads, head_dim
    )
    summaries = received[:, strided_size:].reshape(
        peers, 2, blocks_here * SUMMARY, half_heads, head_dim
    )
    summaries = summaries.transpose(1, 0, 2, 3, 4).reshape(
        2, peers * blocks_here * SUMMARY, half_heads, head_dim
    )

    attended, query_grad, key_grad, value_grad, terms = fixed_heads(
        query_fixed,
        key_fixed,
        value_fixed,
        grad_fixed,
        summaries[0],
        summaries[1],
        scaling,
    )
    strided_out = strided_heads(gathered[0], gathered[1], gathered[2], gathered[3], scaling)

    strided_out = strided_out.reshape(4, peers, -1, head_dim).transpose(1, 0, 2, 3)
    strided_out = strided_out.reshape(peers, -1, head_dim)
    terms = terms.astype(jnp.bfloat16).reshape(2, peers, -1, head_dim).transpose(1, 0, 2, 3)
    terms = terms.reshape(peers, -1, head_dim)
    returned = lax.all_to_all(
        jnp.concatenate([strided_out, terms], axis=1), "ctx", 0, 0, tiled=True
    )
    strided_out = returned[:, :strided_size].reshape(
        peers, 4, blocks_here, residues, half_heads, head_dim
    )
    strided_out = strided_out.transpose(1, 2, 0, 3, 4, 5).reshape(
        4, blocks_here, positions, half_heads, head_dim
    )
    shares = jnp.sum(returned[:, strided_size:].astype(jnp.float32), axis=0)
    shares = shares.reshape(2, blocks_here, SUMMARY, half_heads, head_dim)
    key_grad = jnp.concatenate(
        [key_grad[:, : positions - SUMMARY], key_grad[:, positions - SUMMARY :] + shares[0]], axis=1
    )
    value_grad = jnp.concatenate(
        [value_grad[:, : positions - SUMMARY], value_grad[:, positions - SUMMARY :] + shares[1]],
        axis=1,
    )
    return (
        join_heads(attended, strided_out[0]),
        join_heads(query_grad.astype(jnp.bfloat16), strided_out[1]),
        join_heads(key_grad.astype(jnp.bfloat16), strided_out[2]),
        join_heads(value_grad.astype(jnp.bfloat16), strided_out[3]),
    )


def solution(mesh):
    return jax.shard_map(
        shards,
        mesh=mesh,
        in_specs=(P("ctx", "head"), P("ctx", "head"), P("ctx", "head"), P("ctx", "head")),
        out_specs=(P("ctx", "head"), P("ctx", "head"), P("ctx", "head"), P("ctx", "head")),
        check_vma=False,
    )
```

```python
import functools
import math

import jax
import jax.numpy as jnp
from jax import lax
from jax.experimental import pallas as pl
from jax.experimental.pallas import tpu as pltpu
from jax.sharding import PartitionSpec as P

HD = 128
STRIDE = 128
SUMMARY = 4


def split_heads(matrix):
    blocks = matrix.shape[0] // STRIDE
    half_heads = matrix.shape[1] // (2 * HD)
    shaped = matrix.reshape(blocks, STRIDE, matrix.shape[1] // (4 * HD), 4, HD)
    fixed = shaped[:, :, :, :2].reshape(blocks, STRIDE, half_heads, HD)
    strided = shaped[:, :, :, 2:].reshape(blocks, STRIDE, half_heads, HD)
    return (fixed, strided)


def join_heads(fixed, strided):
    blocks, positions, half_heads, head_dim = fixed.shape
    paired = jnp.concatenate(
        [
            fixed.reshape(blocks, positions, half_heads // 2, 2, head_dim),
            strided.reshape(blocks, positions, half_heads // 2, 2, head_dim),
        ],
        axis=3,
    )
    return paired.reshape(blocks * positions, 2 * half_heads * head_dim)


def product(left, right, left_dim, right_dim):
    return lax.dot_general(
        left, right, (((left_dim,), (right_dim,)), ((), ())), preferred_element_type=jnp.float32
    )


def fixed_kernel(
    start_ref, q_ref, k_ref, v_ref, g_ref, sk_ref, sv_ref,
    att_ref, qg_ref, kg_ref, vg_ref, kt_ref, vt_ref, *, scaling,
):
    blocks_here, half_heads, positions, _ = q_ref.shape
    summary_count = sk_ref.shape[1]
    causal = lax.broadcasted_iota(jnp.int32, (positions, positions), 0) >= lax.broadcasted_iota(
        jnp.int32, (positions, positions), 1
    )
    summary_block = lax.broadcasted_iota(jnp.int32, (positions, summary_count), 1) // SUMMARY
    for head in range(half_heads):
        summary_keys = sk_ref[head]
        summary_values = sv_ref[head]
        key_terms = jnp.zeros(summary_keys.shape, jnp.float32)
        value_terms = jnp.zeros(summary_values.shape, jnp.float32)
        for block in range(blocks_here):
            query = q_ref[block, head]
            key_rows = k_ref[block, head]
            value_rows = v_ref[block, head]
            grad_rows = g_ref[block, head]
            earlier = summary_block < start_ref[0] + block
            local_scores = jnp.where(causal, product(query, key_rows, 1, 1) * scaling, -jnp.inf)
            summary_scores = jnp.where(
                earlier, product(query, summary_keys, 1, 1) * scaling, -jnp.inf
            )
            row_max = jnp.maximum(
                jnp.max(local_scores, axis=1, keepdims=True),
                jnp.max(summary_scores, axis=1, keepdims=True),
            )
            local_raised = jnp.exp(local_scores - row_max)
            summary_raised = jnp.exp(summary_scores - row_max)
            totals = jnp.sum(local_raised, axis=1, keepdims=True) + jnp.sum(
                summary_raised, axis=1, keepdims=True
            )
            local_weights = local_raised / totals
            summary_weights = summary_raised / totals
            local_low = local_weights.astype(jnp.bfloat16)
            summary_low = summary_weights.astype(jnp.bfloat16)
            attended = (
                product(local_low, value_rows, 1, 0) + product(summary_low, summary_values, 1, 0)
            ).astype(jnp.bfloat16)
            row_delta = jnp.sum(
                grad_rows.astype(jnp.float32) * attended.astype(jnp.float32), axis=1, keepdims=True
            )
            local_dscores = (
                local_weights * (product(grad_rows, value_rows, 1, 1) - row_delta)
            ).astype(jnp.bfloat16)
            summary_dscores = (
                summary_weights * (product(grad_rows, summary_values, 1, 1) - row_delta)
            ).astype(jnp.bfloat16)
            att_ref[block, head] = attended
            qg_ref[block, head] = (
                (product(local_dscores, key_rows, 1, 0) + product(summary_dscores, summary_keys, 1, 0))
                * scaling
            ).astype(jnp.bfloat16)
            kg_ref[block, head] = product(local_dscores, query, 0, 0) * scaling
            vg_ref[block, head] = product(local_low, grad_rows, 0, 0)
            key_terms = key_terms + product(summary_dscores, query, 0, 0)
            value_terms = value_terms + product(summary_low, grad_rows, 0, 0)
        kt_ref[head] = key_terms * scaling
        vt_ref[head] = value_terms


def fixed_heads(query, key_rows, value_rows, grad_rows, flat_keys, flat_values, scaling, here):
    blocks_here, positions, half_heads, head_dim = query.shape
    summary_count = flat_keys.shape[0]
    by_head = lambda rows: rows.transpose(0, 2, 1, 3)
    local_shape = (blocks_here, half_heads, positions, head_dim)
    summary_shape = (half_heads, summary_count, head_dim)
    vmem = pl.BlockSpec(memory_space=pltpu.VMEM)
    outs = pl.pallas_call(
        functools.partial(fixed_kernel, scaling=scaling),
        out_shape=(
            jax.ShapeDtypeStruct(local_shape, jnp.bfloat16),
            jax.ShapeDtypeStruct(local_shape, jnp.bfloat16),
            jax.ShapeDtypeStruct(local_shape, jnp.float32),
            jax.ShapeDtypeStruct(local_shape, jnp.float32),
            jax.ShapeDtypeStruct(summary_shape, jnp.float32),
            jax.ShapeDtypeStruct(summary_shape, jnp.float32),
        ),
        in_specs=[pl.BlockSpec(memory_space=pltpu.SMEM)] + [vmem] * 6,
        out_specs=[vmem] * 6,
    )(
        (here * blocks_here).reshape(1).astype(jnp.int32),
        by_head(query),
        by_head(key_rows),
        by_head(value_rows),
        by_head(grad_rows),
        flat_keys.transpose(1, 0, 2),
        flat_values.transpose(1, 0, 2),
    )
    attended, query_grad, key_grad, value_grad = (by_head(out) for out in outs[:4])
    terms = jnp.stack([outs[4], outs[5]]).transpose(0, 2, 1, 3)
    return (attended, query_grad, key_grad, value_grad, terms)


def strided_heads(query_all, keys_all, values_all, grads_all, scaling):
    blocks = query_all.shape[0]
    causal = (jnp.arange(blocks)[:, None] >= jnp.arange(blocks)[None, :])[None, None]
    scores = (
        jnp.einsum("brgd,crgd->rgbc", query_all, keys_all, preferred_element_type=jnp.float32)
        * scaling
    )
    scores = jnp.where(causal, scores, -jnp.inf)
    row_max = jnp.max(scores, axis=-1, keepdims=True)
    raised = jnp.exp(scores - row_max)
    weights = raised / jnp.sum(raised, axis=-1, keepdims=True)
    weights_low = weights.astype(jnp.bfloat16)
    attended = jnp.einsum(
        "rgbc,crgd->brgd", weights_low, values_all, preferred_element_type=jnp.float32
    ).astype(jnp.bfloat16)
    dweights = jnp.einsum(
        "brgd,crgd->rgbc", grads_all, values_all, preferred_element_type=jnp.float32
    )
    row_delta = jnp.sum(grads_all.astype(jnp.float32) * attended.astype(jnp.float32), axis=-1)
    row_delta = jnp.transpose(row_delta, (1, 2, 0))[..., None]
    dscores = (weights * (dweights - row_delta)).astype(jnp.bfloat16)
    query_grad = (
        jnp.einsum("rgbc,crgd->brgd", dscores, keys_all, preferred_element_type=jnp.float32)
        * scaling
    ).astype(jnp.bfloat16)
    key_grad = (
        jnp.einsum("rgbc,brgd->crgd", dscores, query_all, preferred_element_type=jnp.float32)
        * scaling
    ).astype(jnp.bfloat16)
    value_grad = jnp.einsum(
        "rgbc,brgd->crgd", weights_low, grads_all, preferred_element_type=jnp.float32
    ).astype(jnp.bfloat16)
    return jnp.stack([attended, query_grad, key_grad, value_grad])


def shards(queries, keys, values, out_grad):
    scaling = 1.0 / math.sqrt(HD)
    query_fixed, query_strided = split_heads(queries)
    key_fixed, key_strided = split_heads(keys)
    value_fixed, value_strided = split_heads(values)
    grad_fixed, grad_strided = split_heads(out_grad)
    blocks_here, positions, half_heads, head_dim = query_fixed.shape
    peers = lax.axis_size("ctx")
    residues = positions // peers

    strided_rows = jnp.stack([query_strided, key_strided, value_strided, grad_strided])
    strided_rows = strided_rows.reshape(4, blocks_here, peers, residues, half_heads, head_dim)
    strided_rows = strided_rows.transpose(2, 0, 1, 3, 4, 5).reshape(peers, -1, head_dim)
    summary_rows = jnp.stack(
        [key_fixed[:, positions - SUMMARY :], value_fixed[:, positions - SUMMARY :]]
    ).reshape(1, -1, head_dim)
    summary_rows = jnp.broadcast_to(summary_rows, (peers,) + summary_rows.shape[1:])
    strided_size = strided_rows.shape[1]
    received = lax.all_to_all(
        jnp.concatenate([strided_rows, summary_rows], axis=1), "ctx", 0, 0, tiled=True
    )
    gathered = received[:, :strided_size].reshape(
        peers, 4, blocks_here, residues, half_heads, head_dim
    )
    gathered = gathered.transpose(1, 0, 2, 3, 4, 5).reshape(
        4, peers * blocks_here, residues, half_heads, head_dim
    )
    summaries = received[:, strided_size:].reshape(
        peers, 2, blocks_here * SUMMARY, half_heads, head_dim
    )
    summaries = summaries.transpose(1, 0, 2, 3, 4).reshape(
        2, peers * blocks_here * SUMMARY, half_heads, head_dim
    )

    attended, query_grad, key_grad, value_grad, terms = fixed_heads(
        query_fixed,
        key_fixed,
        value_fixed,
        grad_fixed,
        summaries[0],
        summaries[1],
        scaling,
        lax.axis_index("ctx"),
    )
    strided_out = strided_heads(gathered[0], gathered[1], gathered[2], gathered[3], scaling)

    strided_out = strided_out.reshape(4, peers, -1, head_dim).transpose(1, 0, 2, 3)
    strided_out = strided_out.reshape(peers, -1, head_dim)
    terms = terms.astype(jnp.bfloat16).reshape(2, peers, -1, head_dim).transpose(1, 0, 2, 3)
    terms = terms.reshape(peers, -1, head_dim)
    returned = lax.all_to_all(
        jnp.concatenate([strided_out, terms], axis=1), "ctx", 0, 0, tiled=True
    )
    strided_out = returned[:, :strided_size].reshape(
        peers, 4, blocks_here, residues, half_heads, head_dim
    )
    strided_out = strided_out.transpose(1, 2, 0, 3, 4, 5).reshape(
        4, blocks_here, positions, half_heads, head_dim
    )
    shares = jnp.sum(returned[:, strided_size:].astype(jnp.float32), axis=0)
    shares = shares.reshape(2, blocks_here, SUMMARY, half_heads, head_dim)
    key_grad = jnp.concatenate(
        [key_grad[:, : positions - SUMMARY], key_grad[:, positions - SUMMARY :] + shares[0]], axis=1
    )
    value_grad = jnp.concatenate(
        [value_grad[:, : positions - SUMMARY], value_grad[:, positions - SUMMARY :] + shares[1]],
        axis=1,
    )
    return (
        join_heads(attended, strided_out[0]),
        join_heads(query_grad.astype(jnp.bfloat16), strided_out[1]),
        join_heads(key_grad.astype(jnp.bfloat16), strided_out[2]),
        join_heads(value_grad.astype(jnp.bfloat16), strided_out[3]),
    )


def solution(mesh):
    return jax.shard_map(
        shards,
        mesh=mesh,
        in_specs=(P("ctx", "head"), P("ctx", "head"), P("ctx", "head"), P("ctx", "head")),
        out_specs=(P("ctx", "head"), P("ctx", "head"), P("ctx", "head"), P("ctx", "head")),
        check_vma=False,
    )
```

```python
import math

import jax
import jax.numpy as jnp
from jax import lax
from jax.sharding import Mesh, PartitionSpec as P

HD = 128
STRIDE = 128
SUMMARY = 4
CTX = ("ctx_chip", "ctx_core")


def split_heads(matrix):
    blocks = matrix.shape[0] // STRIDE
    half_heads = matrix.shape[1] // (2 * HD)
    shaped = matrix.reshape(blocks, STRIDE, matrix.shape[1] // (4 * HD), 4, HD)
    fixed = shaped[:, :, :, :2].reshape(blocks, STRIDE, half_heads, HD)
    strided = shaped[:, :, :, 2:].reshape(blocks, STRIDE, half_heads, HD)
    return (fixed, strided)


def join_heads(fixed, strided):
    blocks, positions, half_heads, head_dim = fixed.shape
    paired = jnp.concatenate(
        [
            fixed.reshape(blocks, positions, half_heads // 2, 2, head_dim),
            strided.reshape(blocks, positions, half_heads // 2, 2, head_dim),
        ],
        axis=3,
    )
    return paired.reshape(blocks * positions, 2 * half_heads * head_dim)


def fixed_heads(query, key_rows, value_rows, grad_rows, flat_keys, flat_values, scaling, here):
    blocks_here, positions, half_heads, head_dim = query.shape
    summary_count = flat_keys.shape[0]
    block_ids = here * blocks_here + jnp.arange(blocks_here, dtype=jnp.int32)
    summary_block = jnp.arange(summary_count, dtype=jnp.int32) // SUMMARY
    earlier = (summary_block[None, :] < block_ids[:, None])[:, None, None, :]
    causal = (jnp.arange(positions)[:, None] >= jnp.arange(positions)[None, :])[None, None]
    local_scores = (
        jnp.einsum("bqgd,bkgd->bgqk", query, key_rows, preferred_element_type=jnp.float32) * scaling
    )
    summary_scores = (
        jnp.einsum("bqgd,mgd->bgqm", query, flat_keys, preferred_element_type=jnp.float32) * scaling
    )
    local_scores = jnp.where(causal, local_scores, -jnp.inf)
    summary_scores = jnp.where(earlier, summary_scores, -jnp.inf)
    row_max = jnp.maximum(jnp.max(local_scores, axis=-1), jnp.max(summary_scores, axis=-1))[
        ..., None
    ]
    local_raised = jnp.exp(local_scores - row_max)
    summary_raised = jnp.exp(summary_scores - row_max)
    totals = jnp.sum(local_raised, axis=-1, keepdims=True) + jnp.sum(
        summary_raised, axis=-1, keepdims=True
    )
    local_weights = local_raised / totals
    summary_weights = summary_raised / totals
    local_low = local_weights.astype(jnp.bfloat16)
    summary_low = summary_weights.astype(jnp.bfloat16)
    attended = (
        jnp.einsum("bgqk,bkgd->bqgd", local_low, value_rows, preferred_element_type=jnp.float32)
        + jnp.einsum("bgqm,mgd->bqgd", summary_low, flat_values, preferred_element_type=jnp.float32)
    ).astype(jnp.bfloat16)
    local_dweights = jnp.einsum(
        "bqgd,bkgd->bgqk", grad_rows, value_rows, preferred_element_type=jnp.float32
    )
    summary_dweights = jnp.einsum(
        "bqgd,mgd->bgqm", grad_rows, flat_values, preferred_element_type=jnp.float32
    )
    row_delta = jnp.sum(grad_rows.astype(jnp.float32) * attended.astype(jnp.float32), axis=-1)
    row_delta = jnp.transpose(row_delta, (0, 2, 1))[..., None]
    local_dscores = (local_weights * (local_dweights - row_delta)).astype(jnp.bfloat16)
    summary_dscores = (summary_weights * (summary_dweights - row_delta)).astype(jnp.bfloat16)
    query_grad = (
        jnp.einsum("bgqk,bkgd->bqgd", local_dscores, key_rows, preferred_element_type=jnp.float32)
        + jnp.einsum(
            "bgqm,mgd->bqgd", summary_dscores, flat_keys, preferred_element_type=jnp.float32
        )
    ) * scaling
    key_grad = (
        jnp.einsum("bgqk,bqgd->bkgd", local_dscores, query, preferred_element_type=jnp.float32)
        * scaling
    )
    value_grad = jnp.einsum(
        "bgqk,bqgd->bkgd", local_low, grad_rows, preferred_element_type=jnp.float32
    )
    key_terms = (
        jnp.einsum("bgqm,bqgd->mgd", summary_dscores, query, preferred_element_type=jnp.float32)
        * scaling
    )
    value_terms = jnp.einsum(
        "bgqm,bqgd->mgd", summary_low, grad_rows, preferred_element_type=jnp.float32
    )
    return (attended, query_grad, key_grad, value_grad, jnp.stack([key_terms, value_terms]))


def strided_heads(query_all, keys_all, values_all, grads_all, scaling):
    blocks = query_all.shape[0]
    causal = (jnp.arange(blocks)[:, None] >= jnp.arange(blocks)[None, :])[None, None]
    scores = (
        jnp.einsum("brgd,crgd->rgbc", query_all, keys_all, preferred_element_type=jnp.float32)
        * scaling
    )
    scores = jnp.where(causal, scores, -jnp.inf)
    row_max = jnp.max(scores, axis=-1, keepdims=True)
    raised = jnp.exp(scores - row_max)
    weights = raised / jnp.sum(raised, axis=-1, keepdims=True)
    weights_low = weights.astype(jnp.bfloat16)
    attended = jnp.einsum(
        "rgbc,crgd->brgd", weights_low, values_all, preferred_element_type=jnp.float32
    ).astype(jnp.bfloat16)
    dweights = jnp.einsum(
        "brgd,crgd->rgbc", grads_all, values_all, preferred_element_type=jnp.float32
    )
    row_delta = jnp.sum(grads_all.astype(jnp.float32) * attended.astype(jnp.float32), axis=-1)
    row_delta = jnp.transpose(row_delta, (1, 2, 0))[..., None]
    dscores = (weights * (dweights - row_delta)).astype(jnp.bfloat16)
    query_grad = (
        jnp.einsum("rgbc,crgd->brgd", dscores, keys_all, preferred_element_type=jnp.float32)
        * scaling
    ).astype(jnp.bfloat16)
    key_grad = (
        jnp.einsum("rgbc,brgd->crgd", dscores, query_all, preferred_element_type=jnp.float32)
        * scaling
    ).astype(jnp.bfloat16)
    value_grad = jnp.einsum(
        "rgbc,brgd->crgd", weights_low, grads_all, preferred_element_type=jnp.float32
    ).astype(jnp.bfloat16)
    return jnp.stack([attended, query_grad, key_grad, value_grad])


def shards(queries, keys, values, out_grad):
    scaling = 1.0 / math.sqrt(HD)
    query_fixed, query_strided = split_heads(queries)
    key_fixed, key_strided = split_heads(keys)
    value_fixed, value_strided = split_heads(values)
    grad_fixed, grad_strided = split_heads(out_grad)
    blocks_here, positions, half_heads, head_dim = query_fixed.shape
    peers = lax.axis_size("ctx_chip") * 2
    residues = positions // peers
    core = lax.axis_index("ctx_core")
    swap = [(0, 1), (1, 0)]

    strided_rows = jnp.stack([query_strided, key_strided, value_strided, grad_strided])
    strided_rows = strided_rows.reshape(4, blocks_here, peers, residues, half_heads, head_dim)
    strided_rows = strided_rows.transpose(2, 0, 1, 3, 4, 5).reshape(peers, -1, head_dim)
    summary_rows = jnp.stack(
        [key_fixed[:, positions - SUMMARY :], value_fixed[:, positions - SUMMARY :]]
    ).reshape(1, 2, -1, head_dim)
    summary_rows = jnp.broadcast_to(summary_rows, (peers // 2,) + summary_rows.shape[1:])
    summary_rows = summary_rows.reshape(peers, -1, head_dim)
    strided_size = strided_rows.shape[1]
    received = lax.all_to_all(
        jnp.concatenate([strided_rows, summary_rows], axis=1), CTX, 0, 0, tiled=True
    )
    gathered = received[:, :strided_size].reshape(
        peers, 4, blocks_here, residues, half_heads, head_dim
    )
    gathered = gathered.transpose(1, 0, 2, 3, 4, 5).reshape(
        4, peers * blocks_here, residues, half_heads, head_dim
    )
    mine = received[:, strided_size:]
    sibling = lax.ppermute(mine, "ctx_core", swap)
    summary_shape = (peers * blocks_here * SUMMARY, half_heads, head_dim)
    summary_keys = jnp.where(core == 0, mine, sibling).reshape(summary_shape)
    summary_values = jnp.where(core == 0, sibling, mine).reshape(summary_shape)

    attended, query_grad, key_grad, value_grad, terms = fixed_heads(
        query_fixed,
        key_fixed,
        value_fixed,
        grad_fixed,
        summary_keys,
        summary_values,
        scaling,
        lax.axis_index("ctx_chip") * 2 + core,
    )
    strided_out = strided_heads(gathered[0], gathered[1], gathered[2], gathered[3], scaling)

    strided_out = strided_out.reshape(4, peers, -1, head_dim).transpose(1, 0, 2, 3)
    strided_out = strided_out.reshape(peers, -1, head_dim)
    terms = terms.reshape(2, peers, -1, head_dim)
    keep = jnp.where(core == 0, terms[0], terms[1])
    give = jnp.where(core == 0, terms[1], terms[0])
    terms = (keep + lax.ppermute(give, "ctx_core", swap)).astype(jnp.bfloat16)
    returned = lax.all_to_all(
        jnp.concatenate([strided_out, terms], axis=1), CTX, 0, 0, tiled=True
    )
    strided_out = returned[:, :strided_size].reshape(
        peers, 4, blocks_here, residues, half_heads, head_dim
    )
    strided_out = strided_out.transpose(1, 2, 0, 3, 4, 5).reshape(
        4, blocks_here, positions, half_heads, head_dim
    )
    shares = returned[:, strided_size:].astype(jnp.float32)
    shares = jnp.sum(shares.reshape(peers // 2, 2, -1, head_dim), axis=0)
    shares = shares.reshape(2, blocks_here, SUMMARY, half_heads, head_dim)
    key_grad = jnp.concatenate(
        [key_grad[:, : positions - SUMMARY], key_grad[:, positions - SUMMARY :] + shares[0]], axis=1
    )
    value_grad = jnp.concatenate(
        [value_grad[:, : positions - SUMMARY], value_grad[:, positions - SUMMARY :] + shares[1]],
        axis=1,
    )
    return (
        join_heads(attended, strided_out[0]),
        join_heads(query_grad.astype(jnp.bfloat16), strided_out[1]),
        join_heads(key_grad.astype(jnp.bfloat16), strided_out[2]),
        join_heads(value_grad.astype(jnp.bfloat16), strided_out[3]),
    )


def solution(mesh):
    peers, heads = mesh.devices.shape
    split = Mesh(mesh.devices.reshape(peers // 2, 2, heads), CTX + ("head",))
    spec = P(CTX, "head")
    return jax.shard_map(
        shards,
        mesh=split,
        in_specs=(spec, spec, spec, spec),
        out_specs=(spec, spec, spec, spec),
        check_vma=False,
    )
```

```python
import math

import jax
import jax.numpy as jnp
from jax import lax
from jax.sharding import Mesh, PartitionSpec as P

HD = 128
STRIDE = 128
SUMMARY = 4
CTX = ("ctx_chip", "ctx_core")


def split_heads(matrix):
    blocks = matrix.shape[0] // STRIDE
    half_heads = matrix.shape[1] // (2 * HD)
    shaped = matrix.reshape(blocks, STRIDE, matrix.shape[1] // (4 * HD), 4, HD)
    fixed = shaped[:, :, :, :2].reshape(blocks, STRIDE, half_heads, HD)
    strided = shaped[:, :, :, 2:].reshape(blocks, STRIDE, half_heads, HD)
    return (fixed, strided)


def join_heads(fixed, strided):
    blocks, positions, half_heads, head_dim = fixed.shape
    paired = jnp.concatenate(
        [
            fixed.reshape(blocks, positions, half_heads // 2, 2, head_dim),
            strided.reshape(blocks, positions, half_heads // 2, 2, head_dim),
        ],
        axis=3,
    )
    return paired.reshape(blocks * positions, 2 * half_heads * head_dim)


def fixed_heads(query, key_rows, value_rows, grad_rows, flat_keys, flat_values, scaling, here):
    blocks_here, positions, half_heads, head_dim = query.shape
    summary_count = flat_keys.shape[0]
    block_ids = here * blocks_here + jnp.arange(blocks_here, dtype=jnp.int32)
    summary_block = jnp.arange(summary_count, dtype=jnp.int32) // SUMMARY
    earlier = (summary_block[None, :] < block_ids[:, None])[:, None, None, :]
    causal = (jnp.arange(positions)[:, None] >= jnp.arange(positions)[None, :])[None, None]
    local_scores = (
        jnp.einsum("bqgd,bkgd->bgqk", query, key_rows, preferred_element_type=jnp.float32) * scaling
    )
    summary_scores = (
        jnp.einsum("bqgd,mgd->bgqm", query, flat_keys, preferred_element_type=jnp.float32) * scaling
    )
    local_scores = jnp.where(causal, local_scores, -jnp.inf)
    summary_scores = jnp.where(earlier, summary_scores, -jnp.inf)
    row_max = jnp.maximum(jnp.max(local_scores, axis=-1), jnp.max(summary_scores, axis=-1))[
        ..., None
    ]
    local_raised = jnp.exp(local_scores - row_max)
    summary_raised = jnp.exp(summary_scores - row_max)
    totals = jnp.sum(local_raised, axis=-1, keepdims=True) + jnp.sum(
        summary_raised, axis=-1, keepdims=True
    )
    local_weights = local_raised / totals
    summary_weights = summary_raised / totals
    local_low = local_weights.astype(jnp.bfloat16)
    summary_low = summary_weights.astype(jnp.bfloat16)
    attended = (
        jnp.einsum("bgqk,bkgd->bqgd", local_low, value_rows, preferred_element_type=jnp.float32)
        + jnp.einsum("bgqm,mgd->bqgd", summary_low, flat_values, preferred_element_type=jnp.float32)
    ).astype(jnp.bfloat16)
    local_dweights = jnp.einsum(
        "bqgd,bkgd->bgqk", grad_rows, value_rows, preferred_element_type=jnp.float32
    )
    summary_dweights = jnp.einsum(
        "bqgd,mgd->bgqm", grad_rows, flat_values, preferred_element_type=jnp.float32
    )
    row_delta = jnp.sum(grad_rows.astype(jnp.float32) * attended.astype(jnp.float32), axis=-1)
    row_delta = jnp.transpose(row_delta, (0, 2, 1))[..., None]
    local_dscores = (local_weights * (local_dweights - row_delta)).astype(jnp.bfloat16)
    summary_dscores = (summary_weights * (summary_dweights - row_delta)).astype(jnp.bfloat16)
    query_grad = (
        jnp.einsum("bgqk,bkgd->bqgd", local_dscores, key_rows, preferred_element_type=jnp.float32)
        + jnp.einsum(
            "bgqm,mgd->bqgd", summary_dscores, flat_keys, preferred_element_type=jnp.float32
        )
    ) * scaling
    key_grad = (
        jnp.einsum("bgqk,bqgd->bkgd", local_dscores, query, preferred_element_type=jnp.float32)
        * scaling
    )
    value_grad = jnp.einsum(
        "bgqk,bqgd->bkgd", local_low, grad_rows, preferred_element_type=jnp.float32
    )
    key_terms = (
        jnp.einsum("bgqm,bqgd->mgd", summary_dscores, query, preferred_element_type=jnp.float32)
        * scaling
    )
    value_terms = jnp.einsum(
        "bgqm,bqgd->mgd", summary_low, grad_rows, preferred_element_type=jnp.float32
    )
    return (attended, query_grad, key_grad, value_grad, jnp.stack([key_terms, value_terms]))


def strided_heads(query_all, keys_all, values_all, grads_all, scaling):
    blocks = query_all.shape[0]
    causal = (jnp.arange(blocks)[:, None] >= jnp.arange(blocks)[None, :])[None, None]
    scores = (
        jnp.einsum("brgd,crgd->rgbc", query_all, keys_all, preferred_element_type=jnp.float32)
        * scaling
    )
    scores = jnp.where(causal, scores, -jnp.inf)
    row_max = jnp.max(scores, axis=-1, keepdims=True)
    raised = jnp.exp(scores - row_max)
    weights = raised / jnp.sum(raised, axis=-1, keepdims=True)
    weights_low = weights.astype(jnp.bfloat16)
    attended = jnp.einsum(
        "rgbc,crgd->brgd", weights_low, values_all, preferred_element_type=jnp.float32
    ).astype(jnp.bfloat16)
    dweights = jnp.einsum(
        "brgd,crgd->rgbc", grads_all, values_all, preferred_element_type=jnp.float32
    )
    row_delta = jnp.sum(grads_all.astype(jnp.float32) * attended.astype(jnp.float32), axis=-1)
    row_delta = jnp.transpose(row_delta, (1, 2, 0))[..., None]
    dscores = (weights * (dweights - row_delta)).astype(jnp.bfloat16)
    query_grad = (
        jnp.einsum("rgbc,crgd->brgd", dscores, keys_all, preferred_element_type=jnp.float32)
        * scaling
    ).astype(jnp.bfloat16)
    key_grad = (
        jnp.einsum("rgbc,brgd->crgd", dscores, query_all, preferred_element_type=jnp.float32)
        * scaling
    ).astype(jnp.bfloat16)
    value_grad = jnp.einsum(
        "rgbc,brgd->crgd", weights_low, grads_all, preferred_element_type=jnp.float32
    ).astype(jnp.bfloat16)
    return jnp.stack([attended, query_grad, key_grad, value_grad])


def shards(queries, keys, values, out_grad):
    scaling = 1.0 / math.sqrt(HD)
    query_fixed, query_strided = split_heads(queries)
    key_fixed, key_strided = split_heads(keys)
    value_fixed, value_strided = split_heads(values)
    grad_fixed, grad_strided = split_heads(out_grad)
    blocks_here, positions, half_heads, head_dim = query_fixed.shape
    peers = lax.axis_size("ctx_chip") * 2
    residues = positions // peers
    core = lax.axis_index("ctx_core")
    swap = [(0, 1), (1, 0)]

    strided_rows = jnp.stack([query_strided, key_strided, value_strided, grad_strided])
    strided_rows = strided_rows.reshape(4, blocks_here, peers, residues, half_heads, head_dim)
    strided_rows = strided_rows.transpose(2, 0, 1, 3, 4, 5).reshape(peers, -1, head_dim)
    summary_rows = jnp.stack(
        [key_fixed[:, positions - SUMMARY :], value_fixed[:, positions - SUMMARY :]]
    ).reshape(1, 2, -1, head_dim)
    summary_rows = jnp.broadcast_to(summary_rows, (peers // 2,) + summary_rows.shape[1:])
    summary_rows = summary_rows.reshape(peers, -1, head_dim)
    strided_size = strided_rows.shape[1]
    received = lax.all_to_all(
        jnp.concatenate([strided_rows, summary_rows], axis=1), CTX, 0, 0, tiled=True
    )
    gathered = received[:, :strided_size].reshape(
        peers, 4, blocks_here, residues, half_heads, head_dim
    )
    gathered = gathered.transpose(1, 0, 2, 3, 4, 5).reshape(
        4, peers * blocks_here, residues, half_heads, head_dim
    )
    mine = received[:, strided_size:]
    sibling = lax.ppermute(mine, "ctx_core", swap)
    summary_shape = (peers * blocks_here * SUMMARY, half_heads, head_dim)
    both = lax.dynamic_slice_in_dim(jnp.stack([mine, sibling, mine]), core, 2, axis=0)
    summary_keys = both[0].reshape(summary_shape)
    summary_values = both[1].reshape(summary_shape)

    attended, query_grad, key_grad, value_grad, terms = fixed_heads(
        query_fixed,
        key_fixed,
        value_fixed,
        grad_fixed,
        summary_keys,
        summary_values,
        scaling,
        lax.axis_index("ctx_chip") * 2 + core,
    )
    strided_out = strided_heads(gathered[0], gathered[1], gathered[2], gathered[3], scaling)

    strided_out = strided_out.reshape(4, peers, -1, head_dim).transpose(1, 0, 2, 3)
    strided_out = strided_out.reshape(peers, -1, head_dim)
    terms = terms.reshape(2, peers, -1, head_dim)
    keep = lax.dynamic_index_in_dim(terms, core, 0, keepdims=False)
    give = lax.dynamic_index_in_dim(terms, 1 - core, 0, keepdims=False)
    terms = (keep + lax.ppermute(give, "ctx_core", swap)).astype(jnp.bfloat16)
    returned = lax.all_to_all(
        jnp.concatenate([strided_out, terms], axis=1), CTX, 0, 0, tiled=True
    )
    strided_out = returned[:, :strided_size].reshape(
        peers, 4, blocks_here, residues, half_heads, head_dim
    )
    strided_out = strided_out.transpose(1, 2, 0, 3, 4, 5).reshape(
        4, blocks_here, positions, half_heads, head_dim
    )
    shares = returned[:, strided_size:].astype(jnp.float32)
    shares = jnp.sum(shares.reshape(peers // 2, 2, -1, head_dim), axis=0)
    shares = shares.reshape(2, blocks_here, SUMMARY, half_heads, head_dim)
    key_grad = jnp.concatenate(
        [key_grad[:, : positions - SUMMARY], key_grad[:, positions - SUMMARY :] + shares[0]], axis=1
    )
    value_grad = jnp.concatenate(
        [value_grad[:, : positions - SUMMARY], value_grad[:, positions - SUMMARY :] + shares[1]],
        axis=1,
    )
    return (
        join_heads(attended, strided_out[0]),
        join_heads(query_grad.astype(jnp.bfloat16), strided_out[1]),
        join_heads(key_grad.astype(jnp.bfloat16), strided_out[2]),
        join_heads(value_grad.astype(jnp.bfloat16), strided_out[3]),
    )


def solution(mesh):
    peers, heads = mesh.devices.shape
    split = Mesh(mesh.devices.reshape(peers // 2, 2, heads), CTX + ("head",))
    spec = P(CTX, "head")
    return jax.shard_map(
        shards,
        mesh=split,
        in_specs=(spec, spec, spec, spec),
        out_specs=(spec, spec, spec, spec),
        check_vma=False,
    )
```

```python
import math

import jax
import jax.numpy as jnp
from jax import lax
from jax.sharding import Mesh, PartitionSpec as P

HD = 128
STRIDE = 128
SUMMARY = 4
CTX = ("ctx_chip", "ctx_core")


def split_heads(matrix):
    blocks = matrix.shape[0] // STRIDE
    half_heads = matrix.shape[1] // (2 * HD)
    shaped = matrix.reshape(blocks, STRIDE, matrix.shape[1] // (4 * HD), 4, HD)
    fixed = shaped[:, :, :, :2].reshape(blocks, STRIDE, half_heads, HD)
    strided = shaped[:, :, :, 2:].reshape(blocks, STRIDE, half_heads, HD)
    return (fixed, strided)


def join_heads(fixed, strided):
    blocks, positions, half_heads, head_dim = fixed.shape
    paired = jnp.concatenate(
        [
            fixed.reshape(blocks, positions, half_heads // 2, 2, head_dim),
            strided.reshape(blocks, positions, half_heads // 2, 2, head_dim),
        ],
        axis=3,
    )
    return paired.reshape(blocks * positions, 2 * half_heads * head_dim)


def fixed_heads(query, key_rows, value_rows, grad_rows, flat_keys, flat_values, scaling, here):
    blocks_here, positions, half_heads, head_dim = query.shape
    summary_count = flat_keys.shape[0]
    block_ids = here * blocks_here + jnp.arange(blocks_here, dtype=jnp.int32)
    summary_block = jnp.arange(summary_count, dtype=jnp.int32) // SUMMARY
    earlier = (summary_block[None, :] < block_ids[:, None])[:, None, None, :]
    causal = (jnp.arange(positions)[:, None] >= jnp.arange(positions)[None, :])[None, None]
    local_scores = (
        jnp.einsum("bqgd,bkgd->bgqk", query, key_rows, preferred_element_type=jnp.float32) * scaling
    )
    summary_scores = (
        jnp.einsum("bqgd,mgd->bgqm", query, flat_keys, preferred_element_type=jnp.float32) * scaling
    )
    local_scores = jnp.where(causal, local_scores, -jnp.inf)
    summary_scores = jnp.where(earlier, summary_scores, -jnp.inf)
    row_max = jnp.maximum(jnp.max(local_scores, axis=-1), jnp.max(summary_scores, axis=-1))[
        ..., None
    ]
    local_raised = jnp.exp(local_scores - row_max)
    summary_raised = jnp.exp(summary_scores - row_max)
    totals = jnp.sum(local_raised, axis=-1, keepdims=True) + jnp.sum(
        summary_raised, axis=-1, keepdims=True
    )
    local_weights = local_raised / totals
    summary_weights = summary_raised / totals
    local_low = local_weights.astype(jnp.bfloat16)
    summary_low = summary_weights.astype(jnp.bfloat16)
    attended = (
        jnp.einsum("bgqk,bkgd->bqgd", local_low, value_rows, preferred_element_type=jnp.float32)
        + jnp.einsum("bgqm,mgd->bqgd", summary_low, flat_values, preferred_element_type=jnp.float32)
    ).astype(jnp.bfloat16)
    local_dweights = jnp.einsum(
        "bqgd,bkgd->bgqk", grad_rows, value_rows, preferred_element_type=jnp.float32
    )
    summary_dweights = jnp.einsum(
        "bqgd,mgd->bgqm", grad_rows, flat_values, preferred_element_type=jnp.float32
    )
    row_delta = jnp.sum(grad_rows.astype(jnp.float32) * attended.astype(jnp.float32), axis=-1)
    row_delta = jnp.transpose(row_delta, (0, 2, 1))[..., None]
    local_dscores = (local_weights * (local_dweights - row_delta)).astype(jnp.bfloat16)
    summary_dscores = (summary_weights * (summary_dweights - row_delta)).astype(jnp.bfloat16)
    query_grad = (
        jnp.einsum("bgqk,bkgd->bqgd", local_dscores, key_rows, preferred_element_type=jnp.float32)
        + jnp.einsum(
            "bgqm,mgd->bqgd", summary_dscores, flat_keys, preferred_element_type=jnp.float32
        )
    ) * scaling
    key_grad = (
        jnp.einsum("bgqk,bqgd->bkgd", local_dscores, query, preferred_element_type=jnp.float32)
        * scaling
    )
    value_grad = jnp.einsum(
        "bgqk,bqgd->bkgd", local_low, grad_rows, preferred_element_type=jnp.float32
    )
    key_terms = (
        jnp.einsum("bgqm,bqgd->mgd", summary_dscores, query, preferred_element_type=jnp.float32)
        * scaling
    )
    value_terms = jnp.einsum(
        "bgqm,bqgd->mgd", summary_low, grad_rows, preferred_element_type=jnp.float32
    )
    return (attended, query_grad, key_grad, value_grad, jnp.stack([key_terms, value_terms]))


def strided_heads(query_all, keys_all, values_all, grads_all, scaling):
    blocks = query_all.shape[0]
    causal = (jnp.arange(blocks)[:, None] >= jnp.arange(blocks)[None, :])[None, None]
    scores = (
        jnp.einsum("brgd,crgd->rgbc", query_all, keys_all, preferred_element_type=jnp.float32)
        * scaling
    )
    scores = jnp.where(causal, scores, -jnp.inf)
    row_max = jnp.max(scores, axis=-1, keepdims=True)
    raised = jnp.exp(scores - row_max)
    weights = raised / jnp.sum(raised, axis=-1, keepdims=True)
    weights_low = weights.astype(jnp.bfloat16)
    attended = jnp.einsum(
        "rgbc,crgd->brgd", weights_low, values_all, preferred_element_type=jnp.float32
    ).astype(jnp.bfloat16)
    dweights = jnp.einsum(
        "brgd,crgd->rgbc", grads_all, values_all, preferred_element_type=jnp.float32
    )
    row_delta = jnp.sum(grads_all.astype(jnp.float32) * attended.astype(jnp.float32), axis=-1)
    row_delta = jnp.transpose(row_delta, (1, 2, 0))[..., None]
    dscores = (weights * (dweights - row_delta)).astype(jnp.bfloat16)
    query_grad = (
        jnp.einsum("rgbc,crgd->brgd", dscores, keys_all, preferred_element_type=jnp.float32)
        * scaling
    ).astype(jnp.bfloat16)
    key_grad = (
        jnp.einsum("rgbc,brgd->crgd", dscores, query_all, preferred_element_type=jnp.float32)
        * scaling
    ).astype(jnp.bfloat16)
    value_grad = jnp.einsum(
        "rgbc,brgd->crgd", weights_low, grads_all, preferred_element_type=jnp.float32
    ).astype(jnp.bfloat16)
    return jnp.stack([attended, query_grad, key_grad, value_grad])


def shards(queries, keys, values, out_grad):
    scaling = 1.0 / math.sqrt(HD)
    query_fixed, query_strided = split_heads(queries)
    key_fixed, key_strided = split_heads(keys)
    value_fixed, value_strided = split_heads(values)
    grad_fixed, grad_strided = split_heads(out_grad)
    blocks_here, positions, half_heads, head_dim = query_fixed.shape
    peers = lax.axis_size("ctx_chip") * 2
    residues = positions // peers
    core = lax.axis_index("ctx_core")
    swap = [(0, 1), (1, 0)]

    strided_rows = jnp.stack([query_strided, key_strided, value_strided, grad_strided])
    strided_rows = strided_rows.reshape(4, blocks_here, peers, residues, half_heads, head_dim)
    strided_rows = strided_rows.transpose(2, 0, 1, 3, 4, 5).reshape(peers, -1, head_dim)
    summary_rows = jnp.stack(
        [key_fixed[:, positions - SUMMARY :], value_fixed[:, positions - SUMMARY :]]
    ).reshape(1, 2, -1, head_dim)
    summary_rows = jnp.broadcast_to(summary_rows, (peers // 2,) + summary_rows.shape[1:])
    summary_rows = summary_rows.reshape(peers, -1, head_dim)
    strided_size = strided_rows.shape[1]
    received = lax.all_to_all(
        jnp.concatenate([strided_rows, summary_rows], axis=1), CTX, 0, 0, tiled=True
    )
    gathered = received[:, :strided_size].reshape(
        peers, 4, blocks_here, residues, half_heads, head_dim
    )
    gathered = gathered.transpose(1, 0, 2, 3, 4, 5).reshape(
        4, peers * blocks_here, residues, half_heads, head_dim
    )
    mine = received[:, strided_size:]
    sibling = lax.ppermute(mine, "ctx_core", swap)
    summary_shape = (peers * blocks_here * SUMMARY, half_heads, head_dim)
    summary_keys = jnp.where(core == 0, mine, sibling).reshape(summary_shape)
    summary_values = jnp.where(core == 0, sibling, mine).reshape(summary_shape)

    attended, query_grad, key_grad, value_grad, terms = fixed_heads(
        query_fixed,
        key_fixed,
        value_fixed,
        grad_fixed,
        summary_keys,
        summary_values,
        scaling,
        lax.axis_index("ctx_chip") * 2 + core,
    )
    strided_out = strided_heads(gathered[0], gathered[1], gathered[2], gathered[3], scaling)

    strided_out = strided_out.reshape(4, peers, -1, head_dim).transpose(1, 0, 2, 3)
    strided_out = strided_out.reshape(peers, -1, head_dim)
    terms = terms.astype(jnp.bfloat16).reshape(2, peers, -1, head_dim)
    keep = jnp.where(core == 0, terms[0], terms[1])
    give = jnp.where(core == 0, terms[1], terms[0])
    terms = (
        keep.astype(jnp.float32) + lax.ppermute(give, "ctx_core", swap).astype(jnp.float32)
    ).astype(jnp.bfloat16)
    returned = lax.all_to_all(
        jnp.concatenate([strided_out, terms], axis=1), CTX, 0, 0, tiled=True
    )
    strided_out = returned[:, :strided_size].reshape(
        peers, 4, blocks_here, residues, half_heads, head_dim
    )
    strided_out = strided_out.transpose(1, 2, 0, 3, 4, 5).reshape(
        4, blocks_here, positions, half_heads, head_dim
    )
    shares = returned[:, strided_size:].astype(jnp.float32)
    shares = jnp.sum(shares.reshape(peers // 2, 2, -1, head_dim), axis=0)
    shares = shares.reshape(2, blocks_here, SUMMARY, half_heads, head_dim)
    key_grad = jnp.concatenate(
        [key_grad[:, : positions - SUMMARY], key_grad[:, positions - SUMMARY :] + shares[0]], axis=1
    )
    value_grad = jnp.concatenate(
        [value_grad[:, : positions - SUMMARY], value_grad[:, positions - SUMMARY :] + shares[1]],
        axis=1,
    )
    return (
        join_heads(attended, strided_out[0]),
        join_heads(query_grad.astype(jnp.bfloat16), strided_out[1]),
        join_heads(key_grad.astype(jnp.bfloat16), strided_out[2]),
        join_heads(value_grad.astype(jnp.bfloat16), strided_out[3]),
    )


def solution(mesh):
    peers, heads = mesh.devices.shape
    split = Mesh(mesh.devices.reshape(peers // 2, 2, heads), CTX + ("head",))
    spec = P(CTX, "head")
    return jax.shard_map(
        shards,
        mesh=split,
        in_specs=(spec, spec, spec, spec),
        out_specs=(spec, spec, spec, spec),
        check_vma=False,
    )
```

```python
import math

import jax
import jax.numpy as jnp
from jax import lax
from jax.sharding import Mesh, PartitionSpec as P

HD = 128
STRIDE = 128
SUMMARY = 4
CTX = ("ctx_chip", "ctx_core")


def split_heads(matrix):
    blocks = matrix.shape[0] // STRIDE
    half_heads = matrix.shape[1] // (2 * HD)
    shaped = matrix.reshape(blocks, STRIDE, matrix.shape[1] // (4 * HD), 4, HD)
    fixed = shaped[:, :, :, :2].reshape(blocks, STRIDE, half_heads, HD)
    strided = shaped[:, :, :, 2:].reshape(blocks, STRIDE, half_heads, HD)
    return (fixed, strided)


def join_heads(fixed, strided):
    blocks, positions, half_heads, head_dim = fixed.shape
    paired = jnp.concatenate(
        [
            fixed.reshape(blocks, positions, half_heads // 2, 2, head_dim),
            strided.reshape(blocks, positions, half_heads // 2, 2, head_dim),
        ],
        axis=3,
    )
    return paired.reshape(blocks * positions, 2 * half_heads * head_dim)


def fixed_heads(query, key_rows, value_rows, grad_rows, flat_keys, flat_values, scaling, here):
    blocks_here, positions, half_heads, head_dim = query.shape
    summary_count = flat_keys.shape[0]
    block_ids = here * blocks_here + jnp.arange(blocks_here, dtype=jnp.int32)
    summary_block = jnp.arange(summary_count, dtype=jnp.int32) // SUMMARY
    earlier = (summary_block[None, :] < block_ids[:, None])[:, None, None, :]
    causal = (jnp.arange(positions)[:, None] >= jnp.arange(positions)[None, :])[None, None]
    local_scores = (
        jnp.einsum("bqgd,bkgd->bgqk", query, key_rows, preferred_element_type=jnp.float32) * scaling
    )
    summary_scores = (
        jnp.einsum("bqgd,mgd->bgqm", query, flat_keys, preferred_element_type=jnp.float32) * scaling
    )
    local_scores = jnp.where(causal, local_scores, -jnp.inf)
    summary_scores = jnp.where(earlier, summary_scores, -jnp.inf)
    row_max = jnp.maximum(jnp.max(local_scores, axis=-1), jnp.max(summary_scores, axis=-1))[
        ..., None
    ]
    local_raised = jnp.exp(local_scores - row_max)
    summary_raised = jnp.exp(summary_scores - row_max)
    totals = jnp.sum(local_raised, axis=-1, keepdims=True) + jnp.sum(
        summary_raised, axis=-1, keepdims=True
    )
    local_weights = local_raised / totals
    summary_weights = summary_raised / totals
    local_low = local_weights.astype(jnp.bfloat16)
    summary_low = summary_weights.astype(jnp.bfloat16)
    attended = (
        jnp.einsum("bgqk,bkgd->bqgd", local_low, value_rows, preferred_element_type=jnp.float32)
        + jnp.einsum("bgqm,mgd->bqgd", summary_low, flat_values, preferred_element_type=jnp.float32)
    ).astype(jnp.bfloat16)
    local_dweights = jnp.einsum(
        "bqgd,bkgd->bgqk", grad_rows, value_rows, preferred_element_type=jnp.float32
    )
    summary_dweights = jnp.einsum(
        "bqgd,mgd->bgqm", grad_rows, flat_values, preferred_element_type=jnp.float32
    )
    row_delta = jnp.sum(grad_rows.astype(jnp.float32) * attended.astype(jnp.float32), axis=-1)
    row_delta = jnp.transpose(row_delta, (0, 2, 1))[..., None]
    local_dscores = (local_weights * (local_dweights - row_delta)).astype(jnp.bfloat16)
    summary_dscores = (summary_weights * (summary_dweights - row_delta)).astype(jnp.bfloat16)
    query_grad = (
        jnp.einsum("bgqk,bkgd->bqgd", local_dscores, key_rows, preferred_element_type=jnp.float32)
        + jnp.einsum(
            "bgqm,mgd->bqgd", summary_dscores, flat_keys, preferred_element_type=jnp.float32
        )
    ) * scaling
    key_grad = (
        jnp.einsum("bgqk,bqgd->bkgd", local_dscores, query, preferred_element_type=jnp.float32)
        * scaling
    )
    value_grad = jnp.einsum(
        "bgqk,bqgd->bkgd", local_low, grad_rows, preferred_element_type=jnp.float32
    )
    key_terms = (
        jnp.einsum("bgqm,bqgd->mgd", summary_dscores, query, preferred_element_type=jnp.float32)
        * scaling
    )
    value_terms = jnp.einsum(
        "bgqm,bqgd->mgd", summary_low, grad_rows, preferred_element_type=jnp.float32
    )
    return (attended, query_grad, key_grad, value_grad, jnp.stack([key_terms, value_terms]))


def strided_heads(query_all, keys_all, values_all, grads_all, scaling):
    blocks = query_all.shape[0]
    causal = (jnp.arange(blocks)[:, None] >= jnp.arange(blocks)[None, :])[None, None]
    scores = (
        jnp.einsum("brgd,crgd->rgbc", query_all, keys_all, preferred_element_type=jnp.float32)
        * scaling
    )
    scores = jnp.where(causal, scores, -jnp.inf)
    row_max = jnp.max(scores, axis=-1, keepdims=True)
    raised = jnp.exp(scores - row_max)
    weights = raised / jnp.sum(raised, axis=-1, keepdims=True)
    weights_low = weights.astype(jnp.bfloat16)
    attended = jnp.einsum(
        "rgbc,crgd->brgd", weights_low, values_all, preferred_element_type=jnp.float32
    ).astype(jnp.bfloat16)
    dweights = jnp.einsum(
        "brgd,crgd->rgbc", grads_all, values_all, preferred_element_type=jnp.float32
    )
    row_delta = jnp.sum(grads_all.astype(jnp.float32) * attended.astype(jnp.float32), axis=-1)
    row_delta = jnp.transpose(row_delta, (1, 2, 0))[..., None]
    dscores = (weights * (dweights - row_delta)).astype(jnp.bfloat16)
    query_grad = (
        jnp.einsum("rgbc,crgd->brgd", dscores, keys_all, preferred_element_type=jnp.float32)
        * scaling
    ).astype(jnp.bfloat16)
    key_grad = (
        jnp.einsum("rgbc,brgd->crgd", dscores, query_all, preferred_element_type=jnp.float32)
        * scaling
    ).astype(jnp.bfloat16)
    value_grad = jnp.einsum(
        "rgbc,brgd->crgd", weights_low, grads_all, preferred_element_type=jnp.float32
    ).astype(jnp.bfloat16)
    return jnp.stack([attended, query_grad, key_grad, value_grad])


def head_columns(matrix, first):
    groups = matrix.shape[1] // (4 * HD)
    return jnp.stack(
        [
            matrix[:, (4 * group + first + head) * HD : (4 * group + first + head + 1) * HD]
            for group in range(groups)
            for head in range(2)
        ]
    )


def shards(queries, keys, values, out_grad):
    scaling = 1.0 / math.sqrt(HD)
    query_fixed, query_strided = split_heads(queries)
    key_fixed, key_strided = split_heads(keys)
    value_fixed, value_strided = split_heads(values)
    grad_fixed, grad_strided = split_heads(out_grad)
    blocks_here, positions, half_heads, head_dim = query_fixed.shape
    peers = lax.axis_size("ctx_chip") * 2
    residues = positions // peers
    core = lax.axis_index("ctx_core")
    swap = [(0, 1), (1, 0)]

    strided_rows = jnp.stack([head_columns(rows, 2) for rows in (queries, keys, values, out_grad)])
    strided_rows = strided_rows.reshape(4, half_heads, blocks_here, peers, residues, head_dim)
    strided_rows = strided_rows.transpose(3, 0, 2, 4, 1, 5).reshape(peers, -1, head_dim)
    summary_rows = jnp.stack([head_columns(keys, 0), head_columns(values, 0)])
    summary_rows = summary_rows.reshape(2, half_heads, blocks_here, positions, head_dim)
    summary_rows = summary_rows[:, :, :, positions - SUMMARY :].transpose(0, 2, 3, 1, 4)
    summary_rows = summary_rows.reshape(1, 2, -1, head_dim)
    summary_rows = jnp.broadcast_to(summary_rows, (peers // 2,) + summary_rows.shape[1:])
    summary_rows = summary_rows.reshape(peers, -1, head_dim)
    strided_size = strided_rows.shape[1]
    received = lax.all_to_all(
        jnp.concatenate([strided_rows, summary_rows], axis=1), CTX, 0, 0, tiled=True
    )
    gathered = received[:, :strided_size].reshape(
        peers, 4, blocks_here, residues, half_heads, head_dim
    )
    gathered = gathered.transpose(1, 0, 2, 3, 4, 5).reshape(
        4, peers * blocks_here, residues, half_heads, head_dim
    )
    mine = received[:, strided_size:]
    sibling = lax.ppermute(mine, "ctx_core", swap)
    summary_shape = (peers * blocks_here * SUMMARY, half_heads, head_dim)
    summary_keys = jnp.where(core == 0, mine, sibling).reshape(summary_shape)
    summary_values = jnp.where(core == 0, sibling, mine).reshape(summary_shape)

    attended, query_grad, key_grad, value_grad, terms = fixed_heads(
        query_fixed,
        key_fixed,
        value_fixed,
        grad_fixed,
        summary_keys,
        summary_values,
        scaling,
        lax.axis_index("ctx_chip") * 2 + core,
    )
    strided_out = strided_heads(gathered[0], gathered[1], gathered[2], gathered[3], scaling)

    strided_out = strided_out.reshape(4, peers, -1, head_dim).transpose(1, 0, 2, 3)
    strided_out = strided_out.reshape(peers, -1, head_dim)
    terms = terms.astype(jnp.bfloat16).reshape(2, peers, -1, head_dim)
    keep = jnp.where(core == 0, terms[0], terms[1])
    give = jnp.where(core == 0, terms[1], terms[0])
    terms = (
        keep.astype(jnp.float32) + lax.ppermute(give, "ctx_core", swap).astype(jnp.float32)
    ).astype(jnp.bfloat16)
    returned = lax.all_to_all(
        jnp.concatenate([strided_out, terms], axis=1), CTX, 0, 0, tiled=True
    )
    strided_out = returned[:, :strided_size].reshape(
        peers, 4, blocks_here, residues, half_heads, head_dim
    )
    strided_out = strided_out.transpose(1, 2, 0, 3, 4, 5).reshape(
        4, blocks_here, positions, half_heads, head_dim
    )
    shares = returned[:, strided_size:].astype(jnp.float32)
    shares = jnp.sum(shares.reshape(peers // 2, 2, -1, head_dim), axis=0)
    shares = shares.reshape(2, blocks_here, SUMMARY, half_heads, head_dim)
    key_grad = jnp.concatenate(
        [key_grad[:, : positions - SUMMARY], key_grad[:, positions - SUMMARY :] + shares[0]], axis=1
    )
    value_grad = jnp.concatenate(
        [value_grad[:, : positions - SUMMARY], value_grad[:, positions - SUMMARY :] + shares[1]],
        axis=1,
    )
    return (
        join_heads(attended, strided_out[0]),
        join_heads(query_grad.astype(jnp.bfloat16), strided_out[1]),
        join_heads(key_grad.astype(jnp.bfloat16), strided_out[2]),
        join_heads(value_grad.astype(jnp.bfloat16), strided_out[3]),
    )


def solution(mesh):
    peers, heads = mesh.devices.shape
    split = Mesh(mesh.devices.reshape(peers // 2, 2, heads), CTX + ("head",))
    spec = P(CTX, "head")
    return jax.shard_map(
        shards,
        mesh=split,
        in_specs=(spec, spec, spec, spec),
        out_specs=(spec, spec, spec, spec),
        check_vma=False,
    )
```

```python
import functools
import math

import jax
import jax.numpy as jnp
from jax import lax
from jax.experimental import pallas as pl
from jax.experimental.pallas import tpu as pltpu
from jax.sharding import Mesh, PartitionSpec as P

HD = 128
STRIDE = 128
SUMMARY = 4
CTX = ("ctx_chip", "ctx_core")


def split_heads(matrix):
    blocks = matrix.shape[0] // STRIDE
    half_heads = matrix.shape[1] // (2 * HD)
    shaped = matrix.reshape(blocks, STRIDE, matrix.shape[1] // (4 * HD), 4, HD)
    fixed = shaped[:, :, :, :2].reshape(blocks, STRIDE, half_heads, HD)
    strided = shaped[:, :, :, 2:].reshape(blocks, STRIDE, half_heads, HD)
    return (fixed, strided)


def join_heads(fixed, strided):
    blocks, positions, half_heads, head_dim = fixed.shape
    paired = jnp.concatenate(
        [
            fixed.reshape(blocks, positions, half_heads // 2, 2, head_dim),
            strided.reshape(blocks, positions, half_heads // 2, 2, head_dim),
        ],
        axis=3,
    )
    return paired.reshape(blocks * positions, 2 * half_heads * head_dim)


def fixed_heads(query, key_rows, value_rows, grad_rows, flat_keys, flat_values, scaling, here):
    blocks_here, positions, half_heads, head_dim = query.shape
    summary_count = flat_keys.shape[0]
    block_ids = here * blocks_here + jnp.arange(blocks_here, dtype=jnp.int32)
    summary_block = jnp.arange(summary_count, dtype=jnp.int32) // SUMMARY
    earlier = (summary_block[None, :] < block_ids[:, None])[:, None, None, :]
    causal = (jnp.arange(positions)[:, None] >= jnp.arange(positions)[None, :])[None, None]
    local_scores = (
        jnp.einsum("bqgd,bkgd->bgqk", query, key_rows, preferred_element_type=jnp.float32) * scaling
    )
    summary_scores = (
        jnp.einsum("bqgd,mgd->bgqm", query, flat_keys, preferred_element_type=jnp.float32) * scaling
    )
    local_scores = jnp.where(causal, local_scores, -jnp.inf)
    summary_scores = jnp.where(earlier, summary_scores, -jnp.inf)
    row_max = jnp.maximum(jnp.max(local_scores, axis=-1), jnp.max(summary_scores, axis=-1))[
        ..., None
    ]
    local_raised = jnp.exp(local_scores - row_max)
    summary_raised = jnp.exp(summary_scores - row_max)
    totals = jnp.sum(local_raised, axis=-1, keepdims=True) + jnp.sum(
        summary_raised, axis=-1, keepdims=True
    )
    local_weights = local_raised / totals
    summary_weights = summary_raised / totals
    local_low = local_weights.astype(jnp.bfloat16)
    summary_low = summary_weights.astype(jnp.bfloat16)
    attended = (
        jnp.einsum("bgqk,bkgd->bqgd", local_low, value_rows, preferred_element_type=jnp.float32)
        + jnp.einsum("bgqm,mgd->bqgd", summary_low, flat_values, preferred_element_type=jnp.float32)
    ).astype(jnp.bfloat16)
    local_dweights = jnp.einsum(
        "bqgd,bkgd->bgqk", grad_rows, value_rows, preferred_element_type=jnp.float32
    )
    summary_dweights = jnp.einsum(
        "bqgd,mgd->bgqm", grad_rows, flat_values, preferred_element_type=jnp.float32
    )
    row_delta = jnp.sum(grad_rows.astype(jnp.float32) * attended.astype(jnp.float32), axis=-1)
    row_delta = jnp.transpose(row_delta, (0, 2, 1))[..., None]
    local_dscores = (local_weights * (local_dweights - row_delta)).astype(jnp.bfloat16)
    summary_dscores = (summary_weights * (summary_dweights - row_delta)).astype(jnp.bfloat16)
    query_grad = (
        jnp.einsum("bgqk,bkgd->bqgd", local_dscores, key_rows, preferred_element_type=jnp.float32)
        + jnp.einsum(
            "bgqm,mgd->bqgd", summary_dscores, flat_keys, preferred_element_type=jnp.float32
        )
    ) * scaling
    key_grad = (
        jnp.einsum("bgqk,bqgd->bkgd", local_dscores, query, preferred_element_type=jnp.float32)
        * scaling
    )
    value_grad = jnp.einsum(
        "bgqk,bqgd->bkgd", local_low, grad_rows, preferred_element_type=jnp.float32
    )
    key_terms = (
        jnp.einsum("bgqm,bqgd->mgd", summary_dscores, query, preferred_element_type=jnp.float32)
        * scaling
    )
    value_terms = jnp.einsum(
        "bgqm,bqgd->mgd", summary_low, grad_rows, preferred_element_type=jnp.float32
    )
    return (attended, query_grad, key_grad, value_grad, jnp.stack([key_terms, value_terms]))


def product(left, right, left_dim, right_dim):
    return lax.dot_general(
        left, right, (((left_dim,), (right_dim,)), ((), ())), preferred_element_type=jnp.float32
    )


def strided_kernel(rows_ref, out_ref, *, scaling):
    _, half_heads, blocks, _ = rows_ref.shape
    causal = lax.broadcasted_iota(jnp.int32, (blocks, blocks), 0) >= lax.broadcasted_iota(
        jnp.int32, (blocks, blocks), 1
    )
    for head in range(half_heads):
        query = rows_ref[0, head]
        key_rows = rows_ref[1, head]
        value_rows = rows_ref[2, head]
        grad_rows = rows_ref[3, head]
        scores = jnp.where(causal, product(query, key_rows, 1, 1) * scaling, -jnp.inf)
        raised = jnp.exp(scores - jnp.max(scores, axis=1, keepdims=True))
        weights = raised / jnp.sum(raised, axis=1, keepdims=True)
        weights_low = weights.astype(jnp.bfloat16)
        attended = product(weights_low, value_rows, 1, 0).astype(jnp.bfloat16)
        row_delta = jnp.sum(
            grad_rows.astype(jnp.float32) * attended.astype(jnp.float32), axis=1, keepdims=True
        )
        dscores = (weights * (product(grad_rows, value_rows, 1, 1) - row_delta)).astype(
            jnp.bfloat16
        )
        out_ref[0, head] = attended
        out_ref[1, head] = (product(dscores, key_rows, 1, 0) * scaling).astype(jnp.bfloat16)
        out_ref[2, head] = (product(dscores, query, 0, 0) * scaling).astype(jnp.bfloat16)
        out_ref[3, head] = product(weights_low, grad_rows, 0, 0).astype(jnp.bfloat16)


def strided_heads(gathered, scaling):
    arrays, blocks, residues, half_heads, head_dim = gathered.shape
    rows = gathered.transpose(0, 2, 3, 1, 4).reshape(arrays, residues * half_heads, blocks, head_dim)
    vmem = pl.BlockSpec(memory_space=pltpu.VMEM)
    out = pl.pallas_call(
        functools.partial(strided_kernel, scaling=scaling),
        out_shape=jax.ShapeDtypeStruct(rows.shape, jnp.bfloat16),
        in_specs=[vmem],
        out_specs=vmem,
    )(rows)
    out = out.reshape(arrays, residues, half_heads, blocks, head_dim)
    return out.transpose(0, 3, 1, 2, 4)


def shards(queries, keys, values, out_grad):
    scaling = 1.0 / math.sqrt(HD)
    query_fixed, query_strided = split_heads(queries)
    key_fixed, key_strided = split_heads(keys)
    value_fixed, value_strided = split_heads(values)
    grad_fixed, grad_strided = split_heads(out_grad)
    blocks_here, positions, half_heads, head_dim = query_fixed.shape
    peers = lax.axis_size("ctx_chip") * 2
    residues = positions // peers
    core = lax.axis_index("ctx_core")
    swap = [(0, 1), (1, 0)]

    strided_rows = jnp.stack([query_strided, key_strided, value_strided, grad_strided])
    strided_rows = strided_rows.reshape(4, blocks_here, peers, residues, half_heads, head_dim)
    strided_rows = strided_rows.transpose(2, 0, 1, 3, 4, 5).reshape(peers, -1, head_dim)
    summary_rows = jnp.stack(
        [key_fixed[:, positions - SUMMARY :], value_fixed[:, positions - SUMMARY :]]
    ).reshape(1, 2, -1, head_dim)
    summary_rows = jnp.broadcast_to(summary_rows, (peers // 2,) + summary_rows.shape[1:])
    summary_rows = summary_rows.reshape(peers, -1, head_dim)
    strided_size = strided_rows.shape[1]
    received = lax.all_to_all(
        jnp.concatenate([strided_rows, summary_rows], axis=1), CTX, 0, 0, tiled=True
    )
    gathered = received[:, :strided_size].reshape(
        peers, 4, blocks_here, residues, half_heads, head_dim
    )
    gathered = gathered.transpose(1, 0, 2, 3, 4, 5).reshape(
        4, peers * blocks_here, residues, half_heads, head_dim
    )
    mine = received[:, strided_size:]
    sibling = lax.ppermute(mine, "ctx_core", swap)
    summary_shape = (peers * blocks_here * SUMMARY, half_heads, head_dim)
    summary_keys = jnp.where(core == 0, mine, sibling).reshape(summary_shape)
    summary_values = jnp.where(core == 0, sibling, mine).reshape(summary_shape)

    attended, query_grad, key_grad, value_grad, terms = fixed_heads(
        query_fixed,
        key_fixed,
        value_fixed,
        grad_fixed,
        summary_keys,
        summary_values,
        scaling,
        lax.axis_index("ctx_chip") * 2 + core,
    )
    strided_out = strided_heads(gathered, scaling)

    strided_out = strided_out.reshape(4, peers, -1, head_dim).transpose(1, 0, 2, 3)
    strided_out = strided_out.reshape(peers, -1, head_dim)
    terms = terms.astype(jnp.bfloat16).reshape(2, peers, -1, head_dim)
    keep = jnp.where(core == 0, terms[0], terms[1])
    give = jnp.where(core == 0, terms[1], terms[0])
    terms = (
        keep.astype(jnp.float32) + lax.ppermute(give, "ctx_core", swap).astype(jnp.float32)
    ).astype(jnp.bfloat16)
    returned = lax.all_to_all(
        jnp.concatenate([strided_out, terms], axis=1), CTX, 0, 0, tiled=True
    )
    strided_out = returned[:, :strided_size].reshape(
        peers, 4, blocks_here, residues, half_heads, head_dim
    )
    strided_out = strided_out.transpose(1, 2, 0, 3, 4, 5).reshape(
        4, blocks_here, positions, half_heads, head_dim
    )
    shares = returned[:, strided_size:].astype(jnp.float32)
    shares = jnp.sum(shares.reshape(peers // 2, 2, -1, head_dim), axis=0)
    shares = shares.reshape(2, blocks_here, SUMMARY, half_heads, head_dim)
    key_grad = jnp.concatenate(
        [key_grad[:, : positions - SUMMARY], key_grad[:, positions - SUMMARY :] + shares[0]], axis=1
    )
    value_grad = jnp.concatenate(
        [value_grad[:, : positions - SUMMARY], value_grad[:, positions - SUMMARY :] + shares[1]],
        axis=1,
    )
    return (
        join_heads(attended, strided_out[0]),
        join_heads(query_grad.astype(jnp.bfloat16), strided_out[1]),
        join_heads(key_grad.astype(jnp.bfloat16), strided_out[2]),
        join_heads(value_grad.astype(jnp.bfloat16), strided_out[3]),
    )


def solution(mesh):
    peers, heads = mesh.devices.shape
    split = Mesh(mesh.devices.reshape(peers // 2, 2, heads), CTX + ("head",))
    spec = P(CTX, "head")
    return jax.shard_map(
        shards,
        mesh=split,
        in_specs=(spec, spec, spec, spec),
        out_specs=(spec, spec, spec, spec),
        check_vma=False,
    )
```

```python
import functools
import math

import jax
import jax.numpy as jnp
from jax import lax
from jax.experimental import pallas as pl
from jax.experimental.pallas import tpu as pltpu
from jax.sharding import Mesh, PartitionSpec as P

HD = 128
STRIDE = 128
SUMMARY = 4
CTX = ("ctx_chip", "ctx_core")


def split_heads(matrix):
    blocks = matrix.shape[0] // STRIDE
    half_heads = matrix.shape[1] // (2 * HD)
    shaped = matrix.reshape(blocks, STRIDE, matrix.shape[1] // (4 * HD), 4, HD)
    fixed = shaped[:, :, :, :2].reshape(blocks, STRIDE, half_heads, HD)
    strided = shaped[:, :, :, 2:].reshape(blocks, STRIDE, half_heads, HD)
    return (fixed, strided)


def join_heads(fixed, strided):
    blocks, positions, half_heads, head_dim = fixed.shape
    paired = jnp.concatenate(
        [
            fixed.reshape(blocks, positions, half_heads // 2, 2, head_dim),
            strided.reshape(blocks, positions, half_heads // 2, 2, head_dim),
        ],
        axis=3,
    )
    return paired.reshape(blocks * positions, 2 * half_heads * head_dim)


def fixed_heads(query, key_rows, value_rows, grad_rows, flat_keys, flat_values, scaling, here):
    blocks_here, positions, half_heads, head_dim = query.shape
    summary_count = flat_keys.shape[0]
    block_ids = here * blocks_here + jnp.arange(blocks_here, dtype=jnp.int32)
    summary_block = jnp.arange(summary_count, dtype=jnp.int32) // SUMMARY
    earlier = (summary_block[None, :] < block_ids[:, None])[:, None, None, :]
    causal = (jnp.arange(positions)[:, None] >= jnp.arange(positions)[None, :])[None, None]
    local_scores = (
        jnp.einsum("bqgd,bkgd->bgqk", query, key_rows, preferred_element_type=jnp.float32) * scaling
    )
    summary_scores = (
        jnp.einsum("bqgd,mgd->bgqm", query, flat_keys, preferred_element_type=jnp.float32) * scaling
    )
    local_scores = jnp.where(causal, local_scores, -jnp.inf)
    summary_scores = jnp.where(earlier, summary_scores, -jnp.inf)
    row_max = jnp.maximum(jnp.max(local_scores, axis=-1), jnp.max(summary_scores, axis=-1))[
        ..., None
    ]
    local_raised = jnp.exp(local_scores - row_max)
    summary_raised = jnp.exp(summary_scores - row_max)
    totals = jnp.sum(local_raised, axis=-1, keepdims=True) + jnp.sum(
        summary_raised, axis=-1, keepdims=True
    )
    local_weights = local_raised / totals
    summary_weights = summary_raised / totals
    local_low = local_weights.astype(jnp.bfloat16)
    summary_low = summary_weights.astype(jnp.bfloat16)
    attended = (
        jnp.einsum("bgqk,bkgd->bqgd", local_low, value_rows, preferred_element_type=jnp.float32)
        + jnp.einsum("bgqm,mgd->bqgd", summary_low, flat_values, preferred_element_type=jnp.float32)
    ).astype(jnp.bfloat16)
    local_dweights = jnp.einsum(
        "bqgd,bkgd->bgqk", grad_rows, value_rows, preferred_element_type=jnp.float32
    )
    summary_dweights = jnp.einsum(
        "bqgd,mgd->bgqm", grad_rows, flat_values, preferred_element_type=jnp.float32
    )
    row_delta = jnp.sum(grad_rows.astype(jnp.float32) * attended.astype(jnp.float32), axis=-1)
    row_delta = jnp.transpose(row_delta, (0, 2, 1))[..., None]
    local_dscores = (local_weights * (local_dweights - row_delta)).astype(jnp.bfloat16)
    summary_dscores = (summary_weights * (summary_dweights - row_delta)).astype(jnp.bfloat16)
    query_grad = (
        jnp.einsum("bgqk,bkgd->bqgd", local_dscores, key_rows, preferred_element_type=jnp.float32)
        + jnp.einsum(
            "bgqm,mgd->bqgd", summary_dscores, flat_keys, preferred_element_type=jnp.float32
        )
    ) * scaling
    key_grad = (
        jnp.einsum("bgqk,bqgd->bkgd", local_dscores, query, preferred_element_type=jnp.float32)
        * scaling
    )
    value_grad = jnp.einsum(
        "bgqk,bqgd->bkgd", local_low, grad_rows, preferred_element_type=jnp.float32
    )
    key_terms = (
        jnp.einsum("bgqm,bqgd->mgd", summary_dscores, query, preferred_element_type=jnp.float32)
        * scaling
    )
    value_terms = jnp.einsum(
        "bgqm,bqgd->mgd", summary_low, grad_rows, preferred_element_type=jnp.float32
    )
    return (attended, query_grad, key_grad, value_grad, jnp.stack([key_terms, value_terms]))


def product(left, right, left_dim, right_dim):
    return lax.dot_general(
        left, right, (((left_dim,), (right_dim,)), ((), ())), preferred_element_type=jnp.float32
    )


def strided_kernel(rows_ref, out_ref, *, scaling, arrays, half_heads):
    width = arrays * 2 * half_heads
    peers = rows_ref.shape[0] // width
    blocks = 2 * peers
    order = lambda dim: 2 * (lax.broadcasted_iota(jnp.int32, (blocks, blocks), dim) % peers) + (
        lax.broadcasted_iota(jnp.int32, (blocks, blocks), dim) // peers
    )
    causal = order(0) >= order(1)

    def load(array, head):
        return jnp.concatenate(
            [
                rows_ref[pl.ds((array * 2 + block) * half_heads + head, peers, stride=width), :]
                for block in range(2)
            ],
            axis=0,
        )

    def store(array, head, value):
        out_ref[array, head] = value

    for head in range(half_heads):
        query = load(0, head)
        key_rows = load(1, head)
        value_rows = load(2, head)
        grad_rows = load(3, head)
        scores = jnp.where(causal, product(query, key_rows, 1, 1) * scaling, -jnp.inf)
        raised = jnp.exp(scores - jnp.max(scores, axis=1, keepdims=True))
        weights = raised / jnp.sum(raised, axis=1, keepdims=True)
        weights_low = weights.astype(jnp.bfloat16)
        attended = product(weights_low, value_rows, 1, 0).astype(jnp.bfloat16)
        row_delta = jnp.sum(
            grad_rows.astype(jnp.float32) * attended.astype(jnp.float32), axis=1, keepdims=True
        )
        dscores = (weights * (product(grad_rows, value_rows, 1, 1) - row_delta)).astype(
            jnp.bfloat16
        )
        store(0, head, attended)
        store(1, head, (product(dscores, key_rows, 1, 0) * scaling).astype(jnp.bfloat16))
        store(2, head, (product(dscores, query, 0, 0) * scaling).astype(jnp.bfloat16))
        store(3, head, product(weights_low, grad_rows, 0, 0).astype(jnp.bfloat16))


def strided_heads(rows, scaling, half_heads):
    peers, width, head_dim = rows.shape
    vmem = pl.BlockSpec(memory_space=pltpu.VMEM)
    out = pl.pallas_call(
        functools.partial(strided_kernel, scaling=scaling, arrays=4, half_heads=half_heads),
        out_shape=jax.ShapeDtypeStruct((4, half_heads, 2 * peers, head_dim), jnp.bfloat16),
        in_specs=[vmem],
        out_specs=vmem,
    )(rows.reshape(peers * width, head_dim))
    out = out.reshape(4, half_heads, 2, peers, head_dim).transpose(3, 0, 2, 1, 4)
    return out.reshape(peers, width, head_dim)


def shards(queries, keys, values, out_grad):
    scaling = 1.0 / math.sqrt(HD)
    query_fixed, query_strided = split_heads(queries)
    key_fixed, key_strided = split_heads(keys)
    value_fixed, value_strided = split_heads(values)
    grad_fixed, grad_strided = split_heads(out_grad)
    blocks_here, positions, half_heads, head_dim = query_fixed.shape
    peers = lax.axis_size("ctx_chip") * 2
    residues = positions // peers
    core = lax.axis_index("ctx_core")
    swap = [(0, 1), (1, 0)]

    strided_rows = jnp.stack([query_strided, key_strided, value_strided, grad_strided])
    strided_rows = strided_rows.reshape(4, blocks_here, peers, residues, half_heads, head_dim)
    strided_rows = strided_rows.transpose(2, 0, 1, 3, 4, 5).reshape(peers, -1, head_dim)
    summary_rows = jnp.stack(
        [key_fixed[:, positions - SUMMARY :], value_fixed[:, positions - SUMMARY :]]
    ).reshape(1, 2, -1, head_dim)
    summary_rows = jnp.broadcast_to(summary_rows, (peers // 2,) + summary_rows.shape[1:])
    summary_rows = summary_rows.reshape(peers, -1, head_dim)
    strided_size = strided_rows.shape[1]
    received = lax.all_to_all(
        jnp.concatenate([strided_rows, summary_rows], axis=1), CTX, 0, 0, tiled=True
    )
    mine = received[:, strided_size:]
    sibling = lax.ppermute(mine, "ctx_core", swap)
    summary_shape = (peers * blocks_here * SUMMARY, half_heads, head_dim)
    summary_keys = jnp.where(core == 0, mine, sibling).reshape(summary_shape)
    summary_values = jnp.where(core == 0, sibling, mine).reshape(summary_shape)

    attended, query_grad, key_grad, value_grad, terms = fixed_heads(
        query_fixed,
        key_fixed,
        value_fixed,
        grad_fixed,
        summary_keys,
        summary_values,
        scaling,
        lax.axis_index("ctx_chip") * 2 + core,
    )
    strided_out = strided_heads(received[:, :strided_size], scaling, half_heads)

    terms = terms.astype(jnp.bfloat16).reshape(2, peers, -1, head_dim)
    keep = jnp.where(core == 0, terms[0], terms[1])
    give = jnp.where(core == 0, terms[1], terms[0])
    terms = (
        keep.astype(jnp.float32) + lax.ppermute(give, "ctx_core", swap).astype(jnp.float32)
    ).astype(jnp.bfloat16)
    returned = lax.all_to_all(
        jnp.concatenate([strided_out, terms], axis=1), CTX, 0, 0, tiled=True
    )
    strided_out = returned[:, :strided_size].reshape(
        peers, 4, blocks_here, residues, half_heads, head_dim
    )
    strided_out = strided_out.transpose(1, 2, 0, 3, 4, 5).reshape(
        4, blocks_here, positions, half_heads, head_dim
    )
    shares = returned[:, strided_size:].astype(jnp.float32)
    shares = jnp.sum(shares.reshape(peers // 2, 2, -1, head_dim), axis=0)
    shares = shares.reshape(2, blocks_here, SUMMARY, half_heads, head_dim)
    key_grad = jnp.concatenate(
        [key_grad[:, : positions - SUMMARY], key_grad[:, positions - SUMMARY :] + shares[0]], axis=1
    )
    value_grad = jnp.concatenate(
        [value_grad[:, : positions - SUMMARY], value_grad[:, positions - SUMMARY :] + shares[1]],
        axis=1,
    )
    return (
        join_heads(attended, strided_out[0]),
        join_heads(query_grad.astype(jnp.bfloat16), strided_out[1]),
        join_heads(key_grad.astype(jnp.bfloat16), strided_out[2]),
        join_heads(value_grad.astype(jnp.bfloat16), strided_out[3]),
    )


def solution(mesh):
    peers, heads = mesh.devices.shape
    split = Mesh(mesh.devices.reshape(peers // 2, 2, heads), CTX + ("head",))
    spec = P(CTX, "head")
    return jax.shard_map(
        shards,
        mesh=split,
        in_specs=(spec, spec, spec, spec),
        out_specs=(spec, spec, spec, spec),
        check_vma=False,
    )
```

```python
import functools
import math

import jax
import jax.numpy as jnp
from jax import lax
from jax.experimental import pallas as pl
from jax.experimental.pallas import tpu as pltpu
from jax.sharding import Mesh, PartitionSpec as P

HD = 128
STRIDE = 128
SUMMARY = 4
CTX = ("ctx_chip", "ctx_core")


def split_heads(matrix):
    blocks = matrix.shape[0] // STRIDE
    half_heads = matrix.shape[1] // (2 * HD)
    shaped = matrix.reshape(blocks, STRIDE, matrix.shape[1] // (4 * HD), 4, HD)
    fixed = shaped[:, :, :, :2].reshape(blocks, STRIDE, half_heads, HD)
    strided = shaped[:, :, :, 2:].reshape(blocks, STRIDE, half_heads, HD)
    return (fixed, strided)


def join_heads(fixed, strided):
    blocks, positions, half_heads, head_dim = fixed.shape
    paired = jnp.concatenate(
        [
            fixed.reshape(blocks, positions, half_heads // 2, 2, head_dim),
            strided.reshape(blocks, positions, half_heads // 2, 2, head_dim),
        ],
        axis=3,
    )
    return paired.reshape(blocks * positions, 2 * half_heads * head_dim)


def fixed_heads(query, key_rows, value_rows, grad_rows, flat_keys, flat_values, scaling, here):
    blocks_here, positions, half_heads, head_dim = query.shape
    summary_count = flat_keys.shape[0]
    block_ids = here * blocks_here + jnp.arange(blocks_here, dtype=jnp.int32)
    summary_block = jnp.arange(summary_count, dtype=jnp.int32) // SUMMARY
    earlier = (summary_block[None, :] < block_ids[:, None])[:, None, None, :]
    causal = (jnp.arange(positions)[:, None] >= jnp.arange(positions)[None, :])[None, None]
    local_scores = (
        jnp.einsum("bqgd,bkgd->bgqk", query, key_rows, preferred_element_type=jnp.float32) * scaling
    )
    summary_scores = (
        jnp.einsum("bqgd,mgd->bgqm", query, flat_keys, preferred_element_type=jnp.float32) * scaling
    )
    local_scores = jnp.where(causal, local_scores, -jnp.inf)
    summary_scores = jnp.where(earlier, summary_scores, -jnp.inf)
    row_max = jnp.maximum(jnp.max(local_scores, axis=-1), jnp.max(summary_scores, axis=-1))[
        ..., None
    ]
    local_raised = jnp.exp(local_scores - row_max)
    summary_raised = jnp.exp(summary_scores - row_max)
    totals = jnp.sum(local_raised, axis=-1, keepdims=True) + jnp.sum(
        summary_raised, axis=-1, keepdims=True
    )
    local_weights = local_raised / totals
    summary_weights = summary_raised / totals
    local_low = local_weights.astype(jnp.bfloat16)
    summary_low = summary_weights.astype(jnp.bfloat16)
    attended = (
        jnp.einsum("bgqk,bkgd->bqgd", local_low, value_rows, preferred_element_type=jnp.float32)
        + jnp.einsum("bgqm,mgd->bqgd", summary_low, flat_values, preferred_element_type=jnp.float32)
    ).astype(jnp.bfloat16)
    local_dweights = jnp.einsum(
        "bqgd,bkgd->bgqk", grad_rows, value_rows, preferred_element_type=jnp.float32
    )
    summary_dweights = jnp.einsum(
        "bqgd,mgd->bgqm", grad_rows, flat_values, preferred_element_type=jnp.float32
    )
    row_delta = jnp.sum(grad_rows.astype(jnp.float32) * attended.astype(jnp.float32), axis=-1)
    row_delta = jnp.transpose(row_delta, (0, 2, 1))[..., None]
    local_dscores = (local_weights * (local_dweights - row_delta)).astype(jnp.bfloat16)
    summary_dscores = (summary_weights * (summary_dweights - row_delta)).astype(jnp.bfloat16)
    query_grad = (
        jnp.einsum("bgqk,bkgd->bqgd", local_dscores, key_rows, preferred_element_type=jnp.float32)
        + jnp.einsum(
            "bgqm,mgd->bqgd", summary_dscores, flat_keys, preferred_element_type=jnp.float32
        )
    ) * scaling
    key_grad = (
        jnp.einsum("bgqk,bqgd->bkgd", local_dscores, query, preferred_element_type=jnp.float32)
        * scaling
    )
    value_grad = jnp.einsum(
        "bgqk,bqgd->bkgd", local_low, grad_rows, preferred_element_type=jnp.float32
    )
    key_terms = (
        jnp.einsum("bgqm,bqgd->mgd", summary_dscores, query, preferred_element_type=jnp.float32)
        * scaling
    )
    value_terms = jnp.einsum(
        "bgqm,bqgd->mgd", summary_low, grad_rows, preferred_element_type=jnp.float32
    )
    return (attended, query_grad, key_grad, value_grad, jnp.stack([key_terms, value_terms]))


def product(left, right, left_dim, right_dim):
    return lax.dot_general(
        left, right, (((left_dim,), (right_dim,)), ((), ())), preferred_element_type=jnp.float32
    )


def strided_kernel(rows_ref, out_ref, *, scaling, arrays, half_heads):
    width = arrays * 2 * half_heads
    peers = rows_ref.shape[0] // width
    blocks = 2 * peers
    order = lambda dim: 2 * (lax.broadcasted_iota(jnp.int32, (blocks, blocks), dim) % peers) + (
        lax.broadcasted_iota(jnp.int32, (blocks, blocks), dim) // peers
    )
    causal = order(0) >= order(1)

    def load(array, head):
        return jnp.concatenate(
            [
                rows_ref[pl.ds((array * 2 + block) * half_heads + head, peers, stride=width), :]
                for block in range(2)
            ],
            axis=0,
        )

    def store(array, head, value):
        value = value.astype(jnp.float32)
        for block in range(2):
            out_ref[pl.ds((array * 2 + block) * half_heads + head, peers, stride=width), :] = value[
                block * peers : (block + 1) * peers
            ]

    for head in range(half_heads):
        query = load(0, head)
        key_rows = load(1, head)
        value_rows = load(2, head)
        grad_rows = load(3, head)
        scores = jnp.where(causal, product(query, key_rows, 1, 1) * scaling, -jnp.inf)
        raised = jnp.exp(scores - jnp.max(scores, axis=1, keepdims=True))
        weights = raised / jnp.sum(raised, axis=1, keepdims=True)
        weights_low = weights.astype(jnp.bfloat16)
        attended = product(weights_low, value_rows, 1, 0).astype(jnp.bfloat16)
        row_delta = jnp.sum(
            grad_rows.astype(jnp.float32) * attended.astype(jnp.float32), axis=1, keepdims=True
        )
        dscores = (weights * (product(grad_rows, value_rows, 1, 1) - row_delta)).astype(
            jnp.bfloat16
        )
        store(0, head, attended)
        store(1, head, (product(dscores, key_rows, 1, 0) * scaling).astype(jnp.bfloat16))
        store(2, head, (product(dscores, query, 0, 0) * scaling).astype(jnp.bfloat16))
        store(3, head, product(weights_low, grad_rows, 0, 0).astype(jnp.bfloat16))


def strided_heads(rows, scaling, half_heads):
    peers, width, head_dim = rows.shape
    vmem = pl.BlockSpec(memory_space=pltpu.VMEM)
    out = pl.pallas_call(
        functools.partial(strided_kernel, scaling=scaling, arrays=4, half_heads=half_heads),
        out_shape=jax.ShapeDtypeStruct((peers * width, head_dim), jnp.float32),
        in_specs=[vmem],
        out_specs=vmem,
    )(rows.reshape(peers * width, head_dim))
    return out.reshape(peers, width, head_dim).astype(jnp.bfloat16)


def shards(queries, keys, values, out_grad):
    scaling = 1.0 / math.sqrt(HD)
    query_fixed, query_strided = split_heads(queries)
    key_fixed, key_strided = split_heads(keys)
    value_fixed, value_strided = split_heads(values)
    grad_fixed, grad_strided = split_heads(out_grad)
    blocks_here, positions, half_heads, head_dim = query_fixed.shape
    peers = lax.axis_size("ctx_chip") * 2
    residues = positions // peers
    core = lax.axis_index("ctx_core")
    swap = [(0, 1), (1, 0)]

    strided_rows = jnp.stack([query_strided, key_strided, value_strided, grad_strided])
    strided_rows = strided_rows.reshape(4, blocks_here, peers, residues, half_heads, head_dim)
    strided_rows = strided_rows.transpose(2, 0, 1, 3, 4, 5).reshape(peers, -1, head_dim)
    summary_rows = jnp.stack(
        [key_fixed[:, positions - SUMMARY :], value_fixed[:, positions - SUMMARY :]]
    ).reshape(1, 2, -1, head_dim)
    summary_rows = jnp.broadcast_to(summary_rows, (peers // 2,) + summary_rows.shape[1:])
    summary_rows = summary_rows.reshape(peers, -1, head_dim)
    strided_size = strided_rows.shape[1]
    received = lax.all_to_all(
        jnp.concatenate([strided_rows, summary_rows], axis=1), CTX, 0, 0, tiled=True
    )
    mine = received[:, strided_size:]
    sibling = lax.ppermute(mine, "ctx_core", swap)
    summary_shape = (peers * blocks_here * SUMMARY, half_heads, head_dim)
    summary_keys = jnp.where(core == 0, mine, sibling).reshape(summary_shape)
    summary_values = jnp.where(core == 0, sibling, mine).reshape(summary_shape)

    attended, query_grad, key_grad, value_grad, terms = fixed_heads(
        query_fixed,
        key_fixed,
        value_fixed,
        grad_fixed,
        summary_keys,
        summary_values,
        scaling,
        lax.axis_index("ctx_chip") * 2 + core,
    )
    strided_out = strided_heads(received[:, :strided_size], scaling, half_heads)

    terms = terms.astype(jnp.bfloat16).reshape(2, peers, -1, head_dim)
    keep = jnp.where(core == 0, terms[0], terms[1])
    give = jnp.where(core == 0, terms[1], terms[0])
    terms = (
        keep.astype(jnp.float32) + lax.ppermute(give, "ctx_core", swap).astype(jnp.float32)
    ).astype(jnp.bfloat16)
    returned = lax.all_to_all(
        jnp.concatenate([strided_out, terms], axis=1), CTX, 0, 0, tiled=True
    )
    strided_out = returned[:, :strided_size].reshape(
        peers, 4, blocks_here, residues, half_heads, head_dim
    )
    strided_out = strided_out.transpose(1, 2, 0, 3, 4, 5).reshape(
        4, blocks_here, positions, half_heads, head_dim
    )
    shares = returned[:, strided_size:].astype(jnp.float32)
    shares = jnp.sum(shares.reshape(peers // 2, 2, -1, head_dim), axis=0)
    shares = shares.reshape(2, blocks_here, SUMMARY, half_heads, head_dim)
    key_grad = jnp.concatenate(
        [key_grad[:, : positions - SUMMARY], key_grad[:, positions - SUMMARY :] + shares[0]], axis=1
    )
    value_grad = jnp.concatenate(
        [value_grad[:, : positions - SUMMARY], value_grad[:, positions - SUMMARY :] + shares[1]],
        axis=1,
    )
    return (
        join_heads(attended, strided_out[0]),
        join_heads(query_grad.astype(jnp.bfloat16), strided_out[1]),
        join_heads(key_grad.astype(jnp.bfloat16), strided_out[2]),
        join_heads(value_grad.astype(jnp.bfloat16), strided_out[3]),
    )


def solution(mesh):
    peers, heads = mesh.devices.shape
    split = Mesh(mesh.devices.reshape(peers // 2, 2, heads), CTX + ("head",))
    spec = P(CTX, "head")
    return jax.shard_map(
        shards,
        mesh=split,
        in_specs=(spec, spec, spec, spec),
        out_specs=(spec, spec, spec, spec),
        check_vma=False,
    )
```

```python
import functools
import math

import jax
import jax.numpy as jnp
from jax import lax
from jax.experimental import pallas as pl
from jax.experimental.pallas import tpu as pltpu
from jax.sharding import Mesh, PartitionSpec as P

HD = 128
STRIDE = 128
SUMMARY = 4
CTX = ("ctx_chip", "ctx_core")


def split_heads(matrix):
    blocks = matrix.shape[0] // STRIDE
    half_heads = matrix.shape[1] // (2 * HD)
    shaped = matrix.reshape(blocks, STRIDE, matrix.shape[1] // (4 * HD), 4, HD)
    fixed = shaped[:, :, :, :2].reshape(blocks, STRIDE, half_heads, HD)
    strided = shaped[:, :, :, 2:].reshape(blocks, STRIDE, half_heads, HD)
    return (fixed, strided)


def join_heads(fixed, strided):
    blocks, positions, half_heads, head_dim = fixed.shape
    paired = jnp.concatenate(
        [
            fixed.reshape(blocks, positions, half_heads // 2, 2, head_dim),
            strided.reshape(blocks, positions, half_heads // 2, 2, head_dim),
        ],
        axis=3,
    )
    return paired.reshape(blocks * positions, 2 * half_heads * head_dim)


def fixed_heads(query, key_rows, value_rows, grad_rows, flat_keys, flat_values, scaling, here):
    blocks_here, positions, half_heads, head_dim = query.shape
    summary_count = flat_keys.shape[0]
    block_ids = here * blocks_here + jnp.arange(blocks_here, dtype=jnp.int32)
    summary_block = jnp.arange(summary_count, dtype=jnp.int32) // SUMMARY
    earlier = (summary_block[None, :] < block_ids[:, None])[:, None, None, :]
    causal = (jnp.arange(positions)[:, None] >= jnp.arange(positions)[None, :])[None, None]
    local_scores = (
        jnp.einsum("bqgd,bkgd->bgqk", query, key_rows, preferred_element_type=jnp.float32) * scaling
    )
    summary_scores = (
        jnp.einsum("bqgd,mgd->bgqm", query, flat_keys, preferred_element_type=jnp.float32) * scaling
    )
    local_scores = jnp.where(causal, local_scores, -jnp.inf)
    summary_scores = jnp.where(earlier, summary_scores, -jnp.inf)
    row_max = jnp.maximum(jnp.max(local_scores, axis=-1), jnp.max(summary_scores, axis=-1))[
        ..., None
    ]
    local_raised = jnp.exp(local_scores - row_max)
    summary_raised = jnp.exp(summary_scores - row_max)
    totals = jnp.sum(local_raised, axis=-1, keepdims=True) + jnp.sum(
        summary_raised, axis=-1, keepdims=True
    )
    local_weights = local_raised / totals
    summary_weights = summary_raised / totals
    local_low = local_weights.astype(jnp.bfloat16)
    summary_low = summary_weights.astype(jnp.bfloat16)
    attended = (
        jnp.einsum("bgqk,bkgd->bqgd", local_low, value_rows, preferred_element_type=jnp.float32)
        + jnp.einsum("bgqm,mgd->bqgd", summary_low, flat_values, preferred_element_type=jnp.float32)
    ).astype(jnp.bfloat16)
    local_dweights = jnp.einsum(
        "bqgd,bkgd->bgqk", grad_rows, value_rows, preferred_element_type=jnp.float32
    )
    summary_dweights = jnp.einsum(
        "bqgd,mgd->bgqm", grad_rows, flat_values, preferred_element_type=jnp.float32
    )
    row_delta = jnp.sum(grad_rows.astype(jnp.float32) * attended.astype(jnp.float32), axis=-1)
    row_delta = jnp.transpose(row_delta, (0, 2, 1))[..., None]
    local_dscores = (local_weights * (local_dweights - row_delta)).astype(jnp.bfloat16)
    summary_dscores = (summary_weights * (summary_dweights - row_delta)).astype(jnp.bfloat16)
    query_grad = (
        jnp.einsum("bgqk,bkgd->bqgd", local_dscores, key_rows, preferred_element_type=jnp.float32)
        + jnp.einsum(
            "bgqm,mgd->bqgd", summary_dscores, flat_keys, preferred_element_type=jnp.float32
        )
    ) * scaling
    key_grad = (
        jnp.einsum("bgqk,bqgd->bkgd", local_dscores, query, preferred_element_type=jnp.float32)
        * scaling
    )
    value_grad = jnp.einsum(
        "bgqk,bqgd->bkgd", local_low, grad_rows, preferred_element_type=jnp.float32
    )
    key_terms = (
        jnp.einsum("bgqm,bqgd->mgd", summary_dscores, query, preferred_element_type=jnp.float32)
        * scaling
    )
    value_terms = jnp.einsum(
        "bgqm,bqgd->mgd", summary_low, grad_rows, preferred_element_type=jnp.float32
    )
    return (attended, query_grad, key_grad, value_grad, jnp.stack([key_terms, value_terms]))


def product(left, right, left_dim, right_dim):
    return lax.dot_general(
        left, right, (((left_dim,), (right_dim,)), ((), ())), preferred_element_type=jnp.float32
    )


def strided_kernel(rows_ref, out_ref, *, scaling, arrays, half_heads):
    width = arrays * 2 * half_heads
    peers = rows_ref.shape[0] // width
    blocks = 2 * peers
    order = lambda dim: 2 * (lax.broadcasted_iota(jnp.int32, (blocks, blocks), dim) % peers) + (
        lax.broadcasted_iota(jnp.int32, (blocks, blocks), dim) // peers
    )
    causal = order(0) >= order(1)

    def load(array, head):
        return jnp.concatenate(
            [
                rows_ref[pl.ds((array * 2 + block) * half_heads + head, peers, stride=width), :]
                for block in range(2)
            ],
            axis=0,
        )

    def store(array, head, value):
        value = value.astype(jnp.float32)
        for block in range(2):
            out_ref[pl.ds((array * 2 + block) * half_heads + head, peers, stride=width), :] = value[
                block * peers : (block + 1) * peers
            ]

    for head in range(half_heads):
        query = load(0, head)
        key_rows = load(1, head)
        value_rows = load(2, head)
        grad_rows = load(3, head)
        scores = jnp.where(causal, product(query, key_rows, 1, 1) * scaling, -jnp.inf)
        raised = jnp.exp(scores - jnp.max(scores, axis=1, keepdims=True))
        weights = raised / jnp.sum(raised, axis=1, keepdims=True)
        weights_low = weights.astype(jnp.bfloat16)
        attended = product(weights_low, value_rows, 1, 0).astype(jnp.bfloat16)
        row_delta = jnp.sum(
            grad_rows.astype(jnp.float32) * attended.astype(jnp.float32), axis=1, keepdims=True
        )
        dscores = (weights * (product(grad_rows, value_rows, 1, 1) - row_delta)).astype(
            jnp.bfloat16
        )
        store(0, head, attended)
        store(1, head, (product(dscores, key_rows, 1, 0) * scaling).astype(jnp.bfloat16))
        store(2, head, (product(dscores, query, 0, 0) * scaling).astype(jnp.bfloat16))
        store(3, head, product(weights_low, grad_rows, 0, 0).astype(jnp.bfloat16))


def strided_heads(rows, scaling, half_heads):
    peers, width, head_dim = rows.shape
    vmem = pl.BlockSpec(memory_space=pltpu.VMEM)
    out = pl.pallas_call(
        functools.partial(strided_kernel, scaling=scaling, arrays=4, half_heads=half_heads),
        out_shape=jax.ShapeDtypeStruct((peers * width, head_dim), jnp.float32),
        in_specs=[vmem],
        out_specs=vmem,
    )(rows.reshape(peers * width, head_dim))
    return out.reshape(peers, width, head_dim).astype(jnp.bfloat16)


def shards(queries, keys, values, out_grad):
    scaling = 1.0 / math.sqrt(HD)
    query_fixed, query_strided = split_heads(queries)
    key_fixed, key_strided = split_heads(keys)
    value_fixed, value_strided = split_heads(values)
    grad_fixed, grad_strided = split_heads(out_grad)
    blocks_here, positions, half_heads, head_dim = query_fixed.shape
    peers = lax.axis_size("ctx_chip") * 2
    residues = positions // peers
    core = lax.axis_index("ctx_core")
    swap = [(0, 1), (1, 0)]

    strided_rows = jnp.stack([query_strided, key_strided, value_strided, grad_strided])
    strided_rows = strided_rows.reshape(4, blocks_here, peers, residues, half_heads, head_dim)
    strided_rows = strided_rows.transpose(2, 0, 1, 3, 4, 5).reshape(peers, -1, head_dim)
    summary_rows = jnp.stack(
        [key_fixed[:, positions - SUMMARY :], value_fixed[:, positions - SUMMARY :]]
    ).reshape(1, 2, -1, head_dim)
    summary_rows = jnp.broadcast_to(summary_rows, (peers // 2,) + summary_rows.shape[1:])
    summary_rows = summary_rows.reshape(peers, -1, head_dim)
    strided_size = strided_rows.shape[1]
    received = lax.all_to_all(
        jnp.concatenate([strided_rows, summary_rows], axis=1), CTX, 0, 0, tiled=True
    )
    mine = received[:, strided_size:]
    sibling = lax.ppermute(mine, "ctx_core", swap)
    summary_shape = (peers * blocks_here * SUMMARY, half_heads, head_dim)
    summary_keys = jnp.where(core == 0, mine, sibling).reshape(summary_shape)
    summary_values = jnp.where(core == 0, sibling, mine).reshape(summary_shape)

    attended, query_grad, key_grad, value_grad, terms = fixed_heads(
        query_fixed,
        key_fixed,
        value_fixed,
        grad_fixed,
        summary_keys,
        summary_values,
        scaling,
        lax.axis_index("ctx_chip") * 2 + core,
    )
    strided_out = strided_heads(received[:, :strided_size], scaling, half_heads)

    terms = terms.astype(jnp.bfloat16).reshape(2, peers, -1, head_dim)
    keep = jnp.where(core == 0, terms[0], terms[1])
    give = jnp.where(core == 0, terms[1], terms[0])
    terms = (
        keep.astype(jnp.float32) + lax.ppermute(give, "ctx_core", swap).astype(jnp.float32)
    ).astype(jnp.bfloat16)
    returned = lax.all_to_all(
        jnp.concatenate([strided_out, terms], axis=1), CTX, 0, 0, tiled=True
    )
    shares = returned[:, strided_size:].astype(jnp.float32)
    shares = jnp.sum(shares.reshape(peers // 2, 2, -1, head_dim), axis=0)
    shares = shares.reshape(2, blocks_here, SUMMARY, half_heads, head_dim)
    key_grad = jnp.concatenate(
        [key_grad[:, : positions - SUMMARY], key_grad[:, positions - SUMMARY :] + shares[0]], axis=1
    )
    value_grad = jnp.concatenate(
        [value_grad[:, : positions - SUMMARY], value_grad[:, positions - SUMMARY :] + shares[1]],
        axis=1,
    )
    fixed = [
        part.astype(jnp.bfloat16).reshape(blocks_here * positions, half_heads * head_dim)
        for part in (attended, query_grad, key_grad, value_grad)
    ]
    width = returned.shape[1]
    vmem = pl.BlockSpec(memory_space=pltpu.VMEM)
    return pl.pallas_call(
        functools.partial(join_kernel, blocks_here=blocks_here, half_heads=half_heads, width=width),
        out_shape=[jax.ShapeDtypeStruct(queries.shape, jnp.bfloat16)] * 4,
        in_specs=[vmem] * 5,
        out_specs=[vmem] * 4,
    )(returned.reshape(peers * width, head_dim), *fixed)


def join_kernel(returned_ref, *refs, blocks_here, half_heads, width):
    fixed_refs, out_refs = refs[:4], refs[4:]
    peers = returned_ref.shape[0] // width
    fixed_width = fixed_refs[0].shape[1]
    for array in range(4):
        out_refs[array][:, :fixed_width] = fixed_refs[array][...]
        for block in range(blocks_here):
            for head in range(half_heads):
                row = (array * blocks_here + block) * half_heads + head
                out_refs[array][
                    block * peers : (block + 1) * peers,
                    fixed_width + head * HD : fixed_width + (head + 1) * HD,
                ] = returned_ref[pl.ds(row, peers, stride=width), :]


def solution(mesh):
    peers, heads = mesh.devices.shape
    split = Mesh(mesh.devices.reshape(peers // 2, 2, heads), CTX + ("head",))
    spec = P(CTX, "head")
    return jax.shard_map(
        shards,
        mesh=split,
        in_specs=(spec, spec, spec, spec),
        out_specs=(spec, spec, spec, spec),
        check_vma=False,
    )
```

```python
import functools
import math

import jax
import jax.numpy as jnp
from jax import lax
from jax.experimental import pallas as pl
from jax.experimental.pallas import tpu as pltpu
from jax.sharding import Mesh, PartitionSpec as P

HD = 128
STRIDE = 128
SUMMARY = 4
CTX = ("ctx_chip", "ctx_core")


def split_heads(matrix):
    blocks = matrix.shape[0] // STRIDE
    half_heads = matrix.shape[1] // (2 * HD)
    shaped = matrix.reshape(blocks, STRIDE, matrix.shape[1] // (4 * HD), 4, HD)
    fixed = shaped[:, :, :, :2].reshape(blocks, STRIDE, half_heads, HD)
    strided = shaped[:, :, :, 2:].reshape(blocks, STRIDE, half_heads, HD)
    return (fixed, strided)


def join_heads(fixed, strided):
    blocks, positions, half_heads, head_dim = fixed.shape
    paired = jnp.concatenate(
        [
            fixed.reshape(blocks, positions, half_heads // 2, 2, head_dim),
            strided.reshape(blocks, positions, half_heads // 2, 2, head_dim),
        ],
        axis=3,
    )
    return paired.reshape(blocks * positions, 2 * half_heads * head_dim)


def fixed_heads(query, key_rows, value_rows, grad_rows, flat_keys, flat_values, scaling, here):
    blocks_here, positions, half_heads, head_dim = query.shape
    summary_count = flat_keys.shape[0]
    block_ids = here * blocks_here + jnp.arange(blocks_here, dtype=jnp.int32)
    summary_block = jnp.arange(summary_count, dtype=jnp.int32) // SUMMARY
    earlier = (summary_block[None, :] < block_ids[:, None])[:, None, None, :]
    causal = (jnp.arange(positions)[:, None] >= jnp.arange(positions)[None, :])[None, None]
    local_scores = (
        jnp.einsum("bqgd,bkgd->bgqk", query, key_rows, preferred_element_type=jnp.float32) * scaling
    )
    summary_scores = (
        jnp.einsum("bqgd,mgd->bgqm", query, flat_keys, preferred_element_type=jnp.float32) * scaling
    )
    local_scores = jnp.where(causal, local_scores, -jnp.inf)
    summary_scores = jnp.where(earlier, summary_scores, -jnp.inf)
    row_max = jnp.maximum(jnp.max(local_scores, axis=-1), jnp.max(summary_scores, axis=-1))[
        ..., None
    ]
    local_raised = jnp.exp(local_scores - row_max)
    summary_raised = jnp.exp(summary_scores - row_max)
    totals = jnp.sum(local_raised, axis=-1, keepdims=True) + jnp.sum(
        summary_raised, axis=-1, keepdims=True
    )
    local_weights = local_raised / totals
    summary_weights = summary_raised / totals
    local_low = local_weights.astype(jnp.bfloat16)
    summary_low = summary_weights.astype(jnp.bfloat16)
    attended = (
        jnp.einsum("bgqk,bkgd->bqgd", local_low, value_rows, preferred_element_type=jnp.float32)
        + jnp.einsum("bgqm,mgd->bqgd", summary_low, flat_values, preferred_element_type=jnp.float32)
    ).astype(jnp.bfloat16)
    local_dweights = jnp.einsum(
        "bqgd,bkgd->bgqk", grad_rows, value_rows, preferred_element_type=jnp.float32
    )
    summary_dweights = jnp.einsum(
        "bqgd,mgd->bgqm", grad_rows, flat_values, preferred_element_type=jnp.float32
    )
    row_delta = jnp.sum(grad_rows.astype(jnp.float32) * attended.astype(jnp.float32), axis=-1)
    row_delta = jnp.transpose(row_delta, (0, 2, 1))[..., None]
    local_dscores = (local_weights * (local_dweights - row_delta)).astype(jnp.bfloat16)
    summary_dscores = (summary_weights * (summary_dweights - row_delta)).astype(jnp.bfloat16)
    query_grad = (
        jnp.einsum("bgqk,bkgd->bqgd", local_dscores, key_rows, preferred_element_type=jnp.float32)
        + jnp.einsum(
            "bgqm,mgd->bqgd", summary_dscores, flat_keys, preferred_element_type=jnp.float32
        )
    ) * scaling
    key_grad = (
        jnp.einsum("bgqk,bqgd->bkgd", local_dscores, query, preferred_element_type=jnp.float32)
        * scaling
    )
    value_grad = jnp.einsum(
        "bgqk,bqgd->bkgd", local_low, grad_rows, preferred_element_type=jnp.float32
    )
    key_terms = (
        jnp.einsum("bgqm,bqgd->mgd", summary_dscores, query, preferred_element_type=jnp.float32)
        * scaling
    )
    value_terms = jnp.einsum(
        "bgqm,bqgd->mgd", summary_low, grad_rows, preferred_element_type=jnp.float32
    )
    return (attended, query_grad, key_grad, value_grad, jnp.stack([key_terms, value_terms]))


def product(left, right, left_dim, right_dim):
    return lax.dot_general(
        left, right, (((left_dim,), (right_dim,)), ((), ())), preferred_element_type=jnp.float32
    )


def strided_kernel(rows_ref, out_ref, *, scaling, arrays, half_heads):
    width = arrays * 2 * half_heads
    peers = rows_ref.shape[0] // width
    blocks = 2 * peers
    order = lambda dim: 2 * (lax.broadcasted_iota(jnp.int32, (blocks, blocks), dim) % peers) + (
        lax.broadcasted_iota(jnp.int32, (blocks, blocks), dim) // peers
    )
    causal = order(0) >= order(1)

    def load(array, head):
        return jnp.concatenate(
            [
                rows_ref[pl.ds((array * 2 + block) * half_heads + head, peers, stride=width), :]
                for block in range(2)
            ],
            axis=0,
        )

    def store(array, head, value):
        value = value.astype(jnp.float32)
        for block in range(2):
            out_ref[pl.ds((array * 2 + block) * half_heads + head, peers, stride=width), :] = value[
                block * peers : (block + 1) * peers
            ]

    for head in range(half_heads):
        query = load(0, head)
        key_rows = load(1, head)
        value_rows = load(2, head)
        grad_rows = load(3, head)
        scores = jnp.where(causal, product(query, key_rows, 1, 1) * scaling, -jnp.inf)
        raised = jnp.exp(scores - jnp.max(scores, axis=1, keepdims=True))
        weights = raised / jnp.sum(raised, axis=1, keepdims=True)
        weights_low = weights.astype(jnp.bfloat16)
        attended = product(weights_low, value_rows, 1, 0).astype(jnp.bfloat16)
        row_delta = jnp.sum(
            grad_rows.astype(jnp.float32) * attended.astype(jnp.float32), axis=1, keepdims=True
        )
        dscores = (weights * (product(grad_rows, value_rows, 1, 1) - row_delta)).astype(
            jnp.bfloat16
        )
        store(0, head, attended)
        store(1, head, (product(dscores, key_rows, 1, 0) * scaling).astype(jnp.bfloat16))
        store(2, head, (product(dscores, query, 0, 0) * scaling).astype(jnp.bfloat16))
        store(3, head, product(weights_low, grad_rows, 0, 0).astype(jnp.bfloat16))


def strided_heads(rows, scaling, half_heads):
    peers, width, head_dim = rows.shape
    vmem = pl.BlockSpec(memory_space=pltpu.VMEM)
    out = pl.pallas_call(
        functools.partial(strided_kernel, scaling=scaling, arrays=4, half_heads=half_heads),
        out_shape=jax.ShapeDtypeStruct((peers * width, head_dim), jnp.float32),
        in_specs=[vmem],
        out_specs=vmem,
    )(rows.reshape(peers * width, head_dim))
    return out.reshape(peers, width, head_dim).astype(jnp.bfloat16)


def shards(queries, keys, values, out_grad):
    scaling = 1.0 / math.sqrt(HD)
    query_fixed, query_strided = split_heads(queries)
    key_fixed, key_strided = split_heads(keys)
    value_fixed, value_strided = split_heads(values)
    grad_fixed, grad_strided = split_heads(out_grad)
    blocks_here, positions, half_heads, head_dim = query_fixed.shape
    peers = lax.axis_size("ctx_chip") * 2
    residues = positions // peers
    core = lax.axis_index("ctx_core")
    swap = [(0, 1), (1, 0)]

    strided_rows = jnp.stack([query_strided, key_strided, value_strided, grad_strided])
    strided_rows = strided_rows.reshape(4, blocks_here, peers, residues, half_heads, head_dim)
    strided_rows = strided_rows.transpose(2, 0, 1, 3, 4, 5).reshape(peers, -1, head_dim)
    summary_rows = jnp.stack(
        [key_fixed[:, positions - SUMMARY :], value_fixed[:, positions - SUMMARY :]]
    ).reshape(1, 2, -1, head_dim)
    summary_rows = jnp.broadcast_to(summary_rows, (peers // 2,) + summary_rows.shape[1:])
    summary_rows = summary_rows.reshape(peers, -1, head_dim)
    strided_size = strided_rows.shape[1]
    received = lax.all_to_all(
        jnp.concatenate([strided_rows, summary_rows], axis=1), CTX, 0, 0, tiled=True
    )
    mine = received[:, strided_size:]
    sibling = lax.ppermute(mine, "ctx_core", swap)
    strided_out = strided_heads(received[:, :strided_size], scaling, half_heads)
    strided_out, sibling = lax.optimization_barrier((strided_out, sibling))
    summary_shape = (peers * blocks_here * SUMMARY, half_heads, head_dim)
    summary_keys = jnp.where(core == 0, mine, sibling).reshape(summary_shape)
    summary_values = jnp.where(core == 0, sibling, mine).reshape(summary_shape)

    attended, query_grad, key_grad, value_grad, terms = fixed_heads(
        query_fixed,
        key_fixed,
        value_fixed,
        grad_fixed,
        summary_keys,
        summary_values,
        scaling,
        lax.axis_index("ctx_chip") * 2 + core,
    )

    terms = terms.astype(jnp.bfloat16).reshape(2, peers, -1, head_dim)
    keep = jnp.where(core == 0, terms[0], terms[1])
    give = jnp.where(core == 0, terms[1], terms[0])
    terms = (
        keep.astype(jnp.float32) + lax.ppermute(give, "ctx_core", swap).astype(jnp.float32)
    ).astype(jnp.bfloat16)
    returned = lax.all_to_all(
        jnp.concatenate([strided_out, terms], axis=1), CTX, 0, 0, tiled=True
    )
    strided_out = returned[:, :strided_size].reshape(
        peers, 4, blocks_here, residues, half_heads, head_dim
    )
    strided_out = strided_out.transpose(1, 2, 0, 3, 4, 5).reshape(
        4, blocks_here, positions, half_heads, head_dim
    )
    shares = returned[:, strided_size:].astype(jnp.float32)
    shares = jnp.sum(shares.reshape(peers // 2, 2, -1, head_dim), axis=0)
    shares = shares.reshape(2, blocks_here, SUMMARY, half_heads, head_dim)
    key_grad = jnp.concatenate(
        [key_grad[:, : positions - SUMMARY], key_grad[:, positions - SUMMARY :] + shares[0]], axis=1
    )
    value_grad = jnp.concatenate(
        [value_grad[:, : positions - SUMMARY], value_grad[:, positions - SUMMARY :] + shares[1]],
        axis=1,
    )
    return (
        join_heads(attended, strided_out[0]),
        join_heads(query_grad.astype(jnp.bfloat16), strided_out[1]),
        join_heads(key_grad.astype(jnp.bfloat16), strided_out[2]),
        join_heads(value_grad.astype(jnp.bfloat16), strided_out[3]),
    )


def solution(mesh):
    peers, heads = mesh.devices.shape
    split = Mesh(mesh.devices.reshape(peers // 2, 2, heads), CTX + ("head",))
    spec = P(CTX, "head")
    return jax.shard_map(
        shards,
        mesh=split,
        in_specs=(spec, spec, spec, spec),
        out_specs=(spec, spec, spec, spec),
        check_vma=False,
    )
```

```python
import functools
import math

import jax
import jax.numpy as jnp
from jax import lax
from jax.experimental import pallas as pl
from jax.experimental.pallas import tpu as pltpu
from jax.sharding import Mesh, PartitionSpec as P

HD = 128
STRIDE = 128
SUMMARY = 4
CTX = ("ctx_chip", "ctx_core")


def split_heads(matrix):
    blocks = matrix.shape[0] // STRIDE
    half_heads = matrix.shape[1] // (2 * HD)
    shaped = matrix.reshape(blocks, STRIDE, matrix.shape[1] // (4 * HD), 4, HD)
    fixed = shaped[:, :, :, :2].reshape(blocks, STRIDE, half_heads, HD)
    strided = shaped[:, :, :, 2:].reshape(blocks, STRIDE, half_heads, HD)
    return (fixed, strided)


def join_heads(fixed, strided):
    blocks, positions, half_heads, head_dim = fixed.shape
    paired = jnp.concatenate(
        [
            fixed.reshape(blocks, positions, half_heads // 2, 2, head_dim),
            strided.reshape(blocks, positions, half_heads // 2, 2, head_dim),
        ],
        axis=3,
    )
    return paired.reshape(blocks * positions, 2 * half_heads * head_dim)


def fixed_heads(query, key_rows, value_rows, grad_rows, flat_keys, flat_values, scaling, here):
    blocks_here, positions, half_heads, head_dim = query.shape
    summary_count = flat_keys.shape[0]
    block_ids = here * blocks_here + jnp.arange(blocks_here, dtype=jnp.int32)
    summary_block = (jnp.arange(summary_count, dtype=jnp.int32) // (SUMMARY // 2)) % (
        summary_count // SUMMARY
    )
    earlier = (summary_block[None, :] < block_ids[:, None])[:, None, None, :]
    causal = (jnp.arange(positions)[:, None] >= jnp.arange(positions)[None, :])[None, None]
    local_scores = (
        jnp.einsum("bqgd,bkgd->bgqk", query, key_rows, preferred_element_type=jnp.float32) * scaling
    )
    summary_scores = (
        jnp.einsum("bqgd,mgd->bgqm", query, flat_keys, preferred_element_type=jnp.float32) * scaling
    )
    local_scores = jnp.where(causal, local_scores, -jnp.inf)
    summary_scores = jnp.where(earlier, summary_scores, -jnp.inf)
    row_max = jnp.maximum(jnp.max(local_scores, axis=-1), jnp.max(summary_scores, axis=-1))[
        ..., None
    ]
    local_raised = jnp.exp(local_scores - row_max)
    summary_raised = jnp.exp(summary_scores - row_max)
    totals = jnp.sum(local_raised, axis=-1, keepdims=True) + jnp.sum(
        summary_raised, axis=-1, keepdims=True
    )
    local_weights = local_raised / totals
    summary_weights = summary_raised / totals
    local_low = local_weights.astype(jnp.bfloat16)
    summary_low = summary_weights.astype(jnp.bfloat16)
    attended = (
        jnp.einsum("bgqk,bkgd->bqgd", local_low, value_rows, preferred_element_type=jnp.float32)
        + jnp.einsum("bgqm,mgd->bqgd", summary_low, flat_values, preferred_element_type=jnp.float32)
    ).astype(jnp.bfloat16)
    local_dweights = jnp.einsum(
        "bqgd,bkgd->bgqk", grad_rows, value_rows, preferred_element_type=jnp.float32
    )
    summary_dweights = jnp.einsum(
        "bqgd,mgd->bgqm", grad_rows, flat_values, preferred_element_type=jnp.float32
    )
    row_delta = jnp.sum(grad_rows.astype(jnp.float32) * attended.astype(jnp.float32), axis=-1)
    row_delta = jnp.transpose(row_delta, (0, 2, 1))[..., None]
    local_dscores = (local_weights * (local_dweights - row_delta)).astype(jnp.bfloat16)
    summary_dscores = (summary_weights * (summary_dweights - row_delta)).astype(jnp.bfloat16)
    query_grad = (
        jnp.einsum("bgqk,bkgd->bqgd", local_dscores, key_rows, preferred_element_type=jnp.float32)
        + jnp.einsum(
            "bgqm,mgd->bqgd", summary_dscores, flat_keys, preferred_element_type=jnp.float32
        )
    ) * scaling
    key_grad = (
        jnp.einsum("bgqk,bqgd->bkgd", local_dscores, query, preferred_element_type=jnp.float32)
        * scaling
    )
    value_grad = jnp.einsum(
        "bgqk,bqgd->bkgd", local_low, grad_rows, preferred_element_type=jnp.float32
    )
    key_terms = (
        jnp.einsum("bgqm,bqgd->mgd", summary_dscores, query, preferred_element_type=jnp.float32)
        * scaling
    )
    value_terms = jnp.einsum(
        "bgqm,bqgd->mgd", summary_low, grad_rows, preferred_element_type=jnp.float32
    )
    return (attended, query_grad, key_grad, value_grad, jnp.stack([key_terms, value_terms]))


def product(left, right, left_dim, right_dim):
    return lax.dot_general(
        left, right, (((left_dim,), (right_dim,)), ((), ())), preferred_element_type=jnp.float32
    )


def strided_kernel(rows_ref, out_ref, *, scaling, arrays, half_heads):
    width = arrays * 2 * half_heads
    peers = rows_ref.shape[0] // width
    blocks = 2 * peers
    order = lambda dim: 2 * (lax.broadcasted_iota(jnp.int32, (blocks, blocks), dim) % peers) + (
        lax.broadcasted_iota(jnp.int32, (blocks, blocks), dim) // peers
    )
    causal = order(0) >= order(1)

    def load(array, head):
        return jnp.concatenate(
            [
                rows_ref[pl.ds((array * 2 + block) * half_heads + head, peers, stride=width), :]
                for block in range(2)
            ],
            axis=0,
        )

    def store(array, head, value):
        value = value.astype(jnp.float32)
        for block in range(2):
            out_ref[pl.ds((array * 2 + block) * half_heads + head, peers, stride=width), :] = value[
                block * peers : (block + 1) * peers
            ]

    for head in range(half_heads):
        query = load(0, head)
        key_rows = load(1, head)
        value_rows = load(2, head)
        grad_rows = load(3, head)
        scores = jnp.where(causal, product(query, key_rows, 1, 1) * scaling, -jnp.inf)
        raised = jnp.exp(scores - jnp.max(scores, axis=1, keepdims=True))
        weights = raised / jnp.sum(raised, axis=1, keepdims=True)
        weights_low = weights.astype(jnp.bfloat16)
        attended = product(weights_low, value_rows, 1, 0).astype(jnp.bfloat16)
        row_delta = jnp.sum(
            grad_rows.astype(jnp.float32) * attended.astype(jnp.float32), axis=1, keepdims=True
        )
        dscores = (weights * (product(grad_rows, value_rows, 1, 1) - row_delta)).astype(
            jnp.bfloat16
        )
        store(0, head, attended)
        store(1, head, (product(dscores, key_rows, 1, 0) * scaling).astype(jnp.bfloat16))
        store(2, head, (product(dscores, query, 0, 0) * scaling).astype(jnp.bfloat16))
        store(3, head, product(weights_low, grad_rows, 0, 0).astype(jnp.bfloat16))


def strided_heads(rows, scaling, half_heads):
    peers, width, head_dim = rows.shape
    vmem = pl.BlockSpec(memory_space=pltpu.VMEM)
    out = pl.pallas_call(
        functools.partial(strided_kernel, scaling=scaling, arrays=4, half_heads=half_heads),
        out_shape=jax.ShapeDtypeStruct((peers * width, head_dim), jnp.float32),
        in_specs=[vmem],
        out_specs=vmem,
    )(rows.reshape(peers * width, head_dim))
    return out.reshape(peers, width, head_dim).astype(jnp.bfloat16)


def shards(queries, keys, values, out_grad):
    scaling = 1.0 / math.sqrt(HD)
    query_fixed, query_strided = split_heads(queries)
    key_fixed, key_strided = split_heads(keys)
    value_fixed, value_strided = split_heads(values)
    grad_fixed, grad_strided = split_heads(out_grad)
    blocks_here, positions, half_heads, head_dim = query_fixed.shape
    peers = lax.axis_size("ctx_chip") * 2
    residues = positions // peers
    core = lax.axis_index("ctx_core")
    swap = [(0, 1), (1, 0)]

    strided_rows = jnp.stack([query_strided, key_strided, value_strided, grad_strided])
    strided_rows = strided_rows.reshape(4, blocks_here, peers, residues, half_heads, head_dim)
    strided_rows = strided_rows.transpose(2, 0, 1, 3, 4, 5).reshape(peers, -1, head_dim)
    summary_rows = jnp.stack(
        [key_fixed[:, positions - SUMMARY :], value_fixed[:, positions - SUMMARY :]]
    ).reshape(2, blocks_here, 2, SUMMARY // 2, half_heads, head_dim)
    summary_rows = summary_rows.transpose(2, 0, 1, 3, 4, 5).reshape(1, 2, -1, head_dim)
    summary_rows = jnp.broadcast_to(summary_rows, (peers // 2,) + summary_rows.shape[1:])
    summary_rows = summary_rows.reshape(peers, -1, head_dim)
    strided_size = strided_rows.shape[1]
    received = lax.all_to_all(
        jnp.concatenate([strided_rows, summary_rows], axis=1), CTX, 0, 0, tiled=True
    )
    mine = received[:, strided_size:]
    sibling = lax.ppermute(mine, "ctx_core", swap)
    strided_out = strided_heads(received[:, :strided_size], scaling, half_heads)
    strided_out, sibling = lax.optimization_barrier((strided_out, sibling))
    both = jnp.stack([mine, sibling]).reshape(
        2, peers, 2, blocks_here * SUMMARY // 2, half_heads, head_dim
    )
    summary_shape = (peers * blocks_here * SUMMARY, half_heads, head_dim)
    summary_keys = both[:, :, 0].reshape(summary_shape)
    summary_values = both[:, :, 1].reshape(summary_shape)

    attended, query_grad, key_grad, value_grad, terms = fixed_heads(
        query_fixed,
        key_fixed,
        value_fixed,
        grad_fixed,
        summary_keys,
        summary_values,
        scaling,
        lax.axis_index("ctx_chip") * 2 + core,
    )

    terms = terms.astype(jnp.bfloat16).reshape(2, 2, peers, -1, head_dim).transpose(1, 2, 0, 3, 4)
    terms = terms.reshape(2, peers, -1, head_dim)
    keep, give = terms[0], terms[1]
    terms = (
        keep.astype(jnp.float32) + lax.ppermute(give, "ctx_core", swap).astype(jnp.float32)
    ).astype(jnp.bfloat16)
    returned = lax.all_to_all(
        jnp.concatenate([strided_out, terms], axis=1), CTX, 0, 0, tiled=True
    )
    strided_out = returned[:, :strided_size].reshape(
        peers, 4, blocks_here, residues, half_heads, head_dim
    )
    strided_out = strided_out.transpose(1, 2, 0, 3, 4, 5).reshape(
        4, blocks_here, positions, half_heads, head_dim
    )
    shares = returned[:, strided_size:].astype(jnp.float32)
    shares = jnp.sum(shares.reshape(peers // 2, 2, -1, head_dim), axis=0)
    shares = shares.reshape(2, 2, blocks_here, SUMMARY // 2, half_heads, head_dim)
    shares = shares.transpose(1, 2, 0, 3, 4, 5).reshape(2, blocks_here, SUMMARY, half_heads, head_dim)
    key_grad = jnp.concatenate(
        [key_grad[:, : positions - SUMMARY], key_grad[:, positions - SUMMARY :] + shares[0]], axis=1
    )
    value_grad = jnp.concatenate(
        [value_grad[:, : positions - SUMMARY], value_grad[:, positions - SUMMARY :] + shares[1]],
        axis=1,
    )
    return (
        join_heads(attended, strided_out[0]),
        join_heads(query_grad.astype(jnp.bfloat16), strided_out[1]),
        join_heads(key_grad.astype(jnp.bfloat16), strided_out[2]),
        join_heads(value_grad.astype(jnp.bfloat16), strided_out[3]),
    )


def solution(mesh):
    peers, heads = mesh.devices.shape
    split = Mesh(mesh.devices.reshape(peers // 2, 2, heads), CTX + ("head",))
    spec = P(CTX, "head")
    return jax.shard_map(
        shards,
        mesh=split,
        in_specs=(spec, spec, spec, spec),
        out_specs=(spec, spec, spec, spec),
        check_vma=False,
    )
```

```python
import functools
import math

import jax
import jax.numpy as jnp
from jax import lax
from jax.experimental import pallas as pl
from jax.experimental.pallas import tpu as pltpu
from jax.sharding import Mesh, PartitionSpec as P

HD = 128
STRIDE = 128
SUMMARY = 4
CTX = ("ctx_chip", "ctx_core")


def split_heads(matrix):
    blocks = matrix.shape[0] // STRIDE
    half_heads = matrix.shape[1] // (2 * HD)
    shaped = matrix.reshape(blocks, STRIDE, matrix.shape[1] // (4 * HD), 4, HD)
    fixed = shaped[:, :, :, :2].reshape(blocks, STRIDE, half_heads, HD)
    strided = shaped[:, :, :, 2:].reshape(blocks, STRIDE, half_heads, HD)
    return (fixed, strided)


def join_heads(fixed, strided):
    blocks, positions, half_heads, head_dim = fixed.shape
    paired = jnp.concatenate(
        [
            fixed.reshape(blocks, positions, half_heads // 2, 2, head_dim),
            strided.reshape(blocks, positions, half_heads // 2, 2, head_dim),
        ],
        axis=3,
    )
    return paired.reshape(blocks * positions, 2 * half_heads * head_dim)


def fixed_heads(query, key_rows, value_rows, grad_rows, flat_keys, flat_values, scaling, here):
    blocks_here, positions, half_heads, head_dim = query.shape
    summary_count = flat_keys.shape[0]
    block_ids = here * blocks_here + jnp.arange(blocks_here, dtype=jnp.int32)
    summary_block = jnp.arange(summary_count, dtype=jnp.int32) // SUMMARY
    earlier = (summary_block[None, :] < block_ids[:, None])[:, None, None, :]
    causal = (jnp.arange(positions)[:, None] >= jnp.arange(positions)[None, :])[None, None]
    local_scores = (
        jnp.einsum("bqgd,bkgd->bgqk", query, key_rows, preferred_element_type=jnp.float32) * scaling
    )
    summary_scores = (
        jnp.einsum("bqgd,mgd->bgqm", query, flat_keys, preferred_element_type=jnp.float32) * scaling
    )
    local_scores = jnp.where(causal, local_scores, -jnp.inf)
    summary_scores = jnp.where(earlier, summary_scores, -jnp.inf)
    row_max = jnp.maximum(jnp.max(local_scores, axis=-1), jnp.max(summary_scores, axis=-1))[
        ..., None
    ]
    local_raised = jnp.exp(local_scores - row_max)
    summary_raised = jnp.exp(summary_scores - row_max)
    totals = jnp.sum(local_raised, axis=-1, keepdims=True) + jnp.sum(
        summary_raised, axis=-1, keepdims=True
    )
    local_weights = local_raised / totals
    summary_weights = summary_raised / totals
    local_low = local_weights.astype(jnp.bfloat16)
    summary_low = summary_weights.astype(jnp.bfloat16)
    attended = (
        jnp.einsum("bgqk,bkgd->bqgd", local_low, value_rows, preferred_element_type=jnp.float32)
        + jnp.einsum("bgqm,mgd->bqgd", summary_low, flat_values, preferred_element_type=jnp.float32)
    ).astype(jnp.bfloat16)
    local_dweights = jnp.einsum(
        "bqgd,bkgd->bgqk", grad_rows, value_rows, preferred_element_type=jnp.float32
    )
    summary_dweights = jnp.einsum(
        "bqgd,mgd->bgqm", grad_rows, flat_values, preferred_element_type=jnp.float32
    )
    row_delta = jnp.sum(grad_rows.astype(jnp.float32) * attended.astype(jnp.float32), axis=-1)
    row_delta = jnp.transpose(row_delta, (0, 2, 1))[..., None]
    local_dscores = (local_weights * (local_dweights - row_delta)).astype(jnp.bfloat16)
    summary_dscores = (summary_weights * (summary_dweights - row_delta)).astype(jnp.bfloat16)
    query_grad = (
        jnp.einsum("bgqk,bkgd->bqgd", local_dscores, key_rows, preferred_element_type=jnp.float32)
        + jnp.einsum(
            "bgqm,mgd->bqgd", summary_dscores, flat_keys, preferred_element_type=jnp.float32
        )
    ) * scaling
    key_grad = (
        jnp.einsum("bgqk,bqgd->bkgd", local_dscores, query, preferred_element_type=jnp.float32)
        * scaling
    )
    value_grad = jnp.einsum(
        "bgqk,bqgd->bkgd", local_low, grad_rows, preferred_element_type=jnp.float32
    )
    key_terms = (
        jnp.einsum("bgqm,bqgd->mgd", summary_dscores, query, preferred_element_type=jnp.float32)
        * scaling
    )
    value_terms = jnp.einsum(
        "bgqm,bqgd->mgd", summary_low, grad_rows, preferred_element_type=jnp.float32
    )
    return (attended, query_grad, key_grad, value_grad, jnp.stack([key_terms, value_terms]))


def product(left, right, left_dim, right_dim):
    return lax.dot_general(
        left, right, (((left_dim,), (right_dim,)), ((), ())), preferred_element_type=jnp.float32
    )


def strided_kernel(rows_ref, *refs, scaling, arrays, half_heads, heads):
    out_ref = refs[-1]
    if len(refs) == 2:
        out_ref[...] = refs[0][...]
    width = arrays * 2 * half_heads
    peers = rows_ref.shape[0] // width
    blocks = 2 * peers
    order = lambda dim: 2 * (lax.broadcasted_iota(jnp.int32, (blocks, blocks), dim) % peers) + (
        lax.broadcasted_iota(jnp.int32, (blocks, blocks), dim) // peers
    )
    causal = order(0) >= order(1)

    def load(array, head):
        return jnp.concatenate(
            [
                rows_ref[pl.ds((array * 2 + block) * half_heads + head, peers, stride=width), :]
                for block in range(2)
            ],
            axis=0,
        )

    def store(array, head, value):
        value = value.astype(jnp.float32)
        for block in range(2):
            out_ref[pl.ds((array * 2 + block) * half_heads + head, peers, stride=width), :] = value[
                block * peers : (block + 1) * peers
            ]

    for head in heads:
        query = load(0, head)
        key_rows = load(1, head)
        value_rows = load(2, head)
        grad_rows = load(3, head)
        scores = jnp.where(causal, product(query, key_rows, 1, 1) * scaling, -jnp.inf)
        raised = jnp.exp(scores - jnp.max(scores, axis=1, keepdims=True))
        weights = raised / jnp.sum(raised, axis=1, keepdims=True)
        weights_low = weights.astype(jnp.bfloat16)
        attended = product(weights_low, value_rows, 1, 0).astype(jnp.bfloat16)
        row_delta = jnp.sum(
            grad_rows.astype(jnp.float32) * attended.astype(jnp.float32), axis=1, keepdims=True
        )
        dscores = (weights * (product(grad_rows, value_rows, 1, 1) - row_delta)).astype(
            jnp.bfloat16
        )
        store(0, head, attended)
        store(1, head, (product(dscores, key_rows, 1, 0) * scaling).astype(jnp.bfloat16))
        store(2, head, (product(dscores, query, 0, 0) * scaling).astype(jnp.bfloat16))
        store(3, head, product(weights_low, grad_rows, 0, 0).astype(jnp.bfloat16))


def strided_heads(rows, scaling, half_heads, heads, previous=None):
    peers, width, head_dim = rows.shape
    vmem = pl.BlockSpec(memory_space=pltpu.VMEM)
    operands = [rows.reshape(peers * width, head_dim)] + ([] if previous is None else [previous])
    return pl.pallas_call(
        functools.partial(
            strided_kernel, scaling=scaling, arrays=4, half_heads=half_heads, heads=heads
        ),
        out_shape=jax.ShapeDtypeStruct((peers * width, head_dim), jnp.float32),
        in_specs=[vmem] * len(operands),
        out_specs=vmem,
    )(*operands)


def shards(queries, keys, values, out_grad):
    scaling = 1.0 / math.sqrt(HD)
    query_fixed, query_strided = split_heads(queries)
    key_fixed, key_strided = split_heads(keys)
    value_fixed, value_strided = split_heads(values)
    grad_fixed, grad_strided = split_heads(out_grad)
    blocks_here, positions, half_heads, head_dim = query_fixed.shape
    peers = lax.axis_size("ctx_chip") * 2
    residues = positions // peers
    core = lax.axis_index("ctx_core")
    swap = [(0, 1), (1, 0)]

    strided_rows = jnp.stack([query_strided, key_strided, value_strided, grad_strided])
    strided_rows = strided_rows.reshape(4, blocks_here, peers, residues, half_heads, head_dim)
    strided_rows = strided_rows.transpose(2, 0, 1, 3, 4, 5).reshape(peers, -1, head_dim)
    summary_rows = jnp.stack(
        [key_fixed[:, positions - SUMMARY :], value_fixed[:, positions - SUMMARY :]]
    ).reshape(1, 2, -1, head_dim)
    summary_rows = jnp.broadcast_to(summary_rows, (peers // 2,) + summary_rows.shape[1:])
    summary_rows = summary_rows.reshape(peers, -1, head_dim)
    strided_size = strided_rows.shape[1]
    received = lax.all_to_all(
        jnp.concatenate([strided_rows, summary_rows], axis=1), CTX, 0, 0, tiled=True
    )
    mine = received[:, strided_size:]
    sibling = lax.ppermute(mine, "ctx_core", swap)
    strided_rows = received[:, :strided_size]
    strided_out = strided_heads(strided_rows, scaling, half_heads, (0,))
    strided_out, sibling = lax.optimization_barrier((strided_out, sibling))
    summary_shape = (peers * blocks_here * SUMMARY, half_heads, head_dim)
    summary_keys = jnp.where(core == 0, mine, sibling).reshape(summary_shape)
    summary_values = jnp.where(core == 0, sibling, mine).reshape(summary_shape)

    attended, query_grad, key_grad, value_grad, terms = fixed_heads(
        query_fixed,
        key_fixed,
        value_fixed,
        grad_fixed,
        summary_keys,
        summary_values,
        scaling,
        lax.axis_index("ctx_chip") * 2 + core,
    )

    terms = terms.astype(jnp.bfloat16).reshape(2, peers, -1, head_dim)
    keep = jnp.where(core == 0, terms[0], terms[1])
    give = jnp.where(core == 0, terms[1], terms[0])
    given = lax.ppermute(give, "ctx_core", swap)
    strided_out = strided_heads(strided_rows, scaling, half_heads, range(1, half_heads), strided_out)
    strided_out, given = lax.optimization_barrier((strided_out, given))
    strided_out = strided_out.reshape(peers, strided_size, head_dim).astype(jnp.bfloat16)
    terms = (keep.astype(jnp.float32) + given.astype(jnp.float32)).astype(jnp.bfloat16)
    returned = lax.all_to_all(
        jnp.concatenate([strided_out, terms], axis=1), CTX, 0, 0, tiled=True
    )
    strided_out = returned[:, :strided_size].reshape(
        peers, 4, blocks_here, residues, half_heads, head_dim
    )
    strided_out = strided_out.transpose(1, 2, 0, 3, 4, 5).reshape(
        4, blocks_here, positions, half_heads, head_dim
    )
    shares = returned[:, strided_size:].astype(jnp.float32)
    shares = jnp.sum(shares.reshape(peers // 2, 2, -1, head_dim), axis=0)
    shares = shares.reshape(2, blocks_here, SUMMARY, half_heads, head_dim)
    key_grad = jnp.concatenate(
        [key_grad[:, : positions - SUMMARY], key_grad[:, positions - SUMMARY :] + shares[0]], axis=1
    )
    value_grad = jnp.concatenate(
        [value_grad[:, : positions - SUMMARY], value_grad[:, positions - SUMMARY :] + shares[1]],
        axis=1,
    )
    return (
        join_heads(attended, strided_out[0]),
        join_heads(query_grad.astype(jnp.bfloat16), strided_out[1]),
        join_heads(key_grad.astype(jnp.bfloat16), strided_out[2]),
        join_heads(value_grad.astype(jnp.bfloat16), strided_out[3]),
    )


def solution(mesh):
    peers, heads = mesh.devices.shape
    split = Mesh(mesh.devices.reshape(peers // 2, 2, heads), CTX + ("head",))
    spec = P(CTX, "head")
    return jax.shard_map(
        shards,
        mesh=split,
        in_specs=(spec, spec, spec, spec),
        out_specs=(spec, spec, spec, spec),
        check_vma=False,
    )
```

```python
import functools
import math

import jax
import jax.numpy as jnp
from jax import lax
from jax.experimental import pallas as pl
from jax.experimental.pallas import tpu as pltpu
from jax.sharding import Mesh, PartitionSpec as P

HD = 128
STRIDE = 128
SUMMARY = 4
CTX = ("ctx_chip", "ctx_core")


def split_heads(matrix):
    blocks = matrix.shape[0] // STRIDE
    half_heads = matrix.shape[1] // (2 * HD)
    shaped = matrix.reshape(blocks, STRIDE, matrix.shape[1] // (4 * HD), 4, HD)
    fixed = shaped[:, :, :, :2].reshape(blocks, STRIDE, half_heads, HD)
    strided = shaped[:, :, :, 2:].reshape(blocks, STRIDE, half_heads, HD)
    return (fixed, strided)


def join_heads(fixed, strided):
    blocks, positions, half_heads, head_dim = fixed.shape
    paired = jnp.concatenate(
        [
            fixed.reshape(blocks, positions, half_heads // 2, 2, head_dim),
            strided.reshape(blocks, positions, half_heads // 2, 2, head_dim),
        ],
        axis=3,
    )
    return paired.reshape(blocks * positions, 2 * half_heads * head_dim)


def fixed_heads(query, key_rows, value_rows, grad_rows, flat_keys, flat_values, scaling, here):
    blocks_here, positions, half_heads, head_dim = query.shape
    summary_count = flat_keys.shape[0]
    block_ids = here * blocks_here + jnp.arange(blocks_here, dtype=jnp.int32)
    summary_block = jnp.arange(summary_count, dtype=jnp.int32) // SUMMARY
    earlier = (summary_block[None, :] < block_ids[:, None])[:, None, None, :]
    causal = (jnp.arange(positions)[:, None] >= jnp.arange(positions)[None, :])[None, None]
    local_scores = (
        jnp.einsum("bqgd,bkgd->bgqk", query, key_rows, preferred_element_type=jnp.float32) * scaling
    )
    summary_scores = (
        jnp.einsum("bqgd,mgd->bgqm", query, flat_keys, preferred_element_type=jnp.float32) * scaling
    )
    local_scores = jnp.where(causal, local_scores, -jnp.inf)
    summary_scores = jnp.where(earlier, summary_scores, -jnp.inf)
    row_max = jnp.maximum(jnp.max(local_scores, axis=-1), jnp.max(summary_scores, axis=-1))[
        ..., None
    ]
    local_raised = jnp.exp(local_scores - row_max)
    summary_raised = jnp.exp(summary_scores - row_max)
    totals = jnp.sum(local_raised, axis=-1, keepdims=True) + jnp.sum(
        summary_raised, axis=-1, keepdims=True
    )
    local_weights = local_raised / totals
    summary_weights = summary_raised / totals
    local_low = local_weights.astype(jnp.bfloat16)
    summary_low = summary_weights.astype(jnp.bfloat16)
    attended = (
        jnp.einsum("bgqk,bkgd->bqgd", local_low, value_rows, preferred_element_type=jnp.float32)
        + jnp.einsum("bgqm,mgd->bqgd", summary_low, flat_values, preferred_element_type=jnp.float32)
    ).astype(jnp.bfloat16)
    local_dweights = jnp.einsum(
        "bqgd,bkgd->bgqk", grad_rows, value_rows, preferred_element_type=jnp.float32
    )
    summary_dweights = jnp.einsum(
        "bqgd,mgd->bgqm", grad_rows, flat_values, preferred_element_type=jnp.float32
    )
    row_delta = jnp.sum(grad_rows.astype(jnp.float32) * attended.astype(jnp.float32), axis=-1)
    row_delta = jnp.transpose(row_delta, (0, 2, 1))[..., None]
    local_dscores = (local_weights * (local_dweights - row_delta)).astype(jnp.bfloat16)
    summary_dscores = (summary_weights * (summary_dweights - row_delta)).astype(jnp.bfloat16)
    query_grad = (
        jnp.einsum("bgqk,bkgd->bqgd", local_dscores, key_rows, preferred_element_type=jnp.float32)
        + jnp.einsum(
            "bgqm,mgd->bqgd", summary_dscores, flat_keys, preferred_element_type=jnp.float32
        )
    ) * scaling
    key_grad = (
        jnp.einsum("bgqk,bqgd->bkgd", local_dscores, query, preferred_element_type=jnp.float32)
        * scaling
    )
    value_grad = jnp.einsum(
        "bgqk,bqgd->bkgd", local_low, grad_rows, preferred_element_type=jnp.float32
    )
    key_terms = (
        jnp.einsum("bgqm,bqgd->mgd", summary_dscores, query, preferred_element_type=jnp.float32)
        * scaling
    )
    value_terms = jnp.einsum(
        "bgqm,bqgd->mgd", summary_low, grad_rows, preferred_element_type=jnp.float32
    )
    return (attended, query_grad, key_grad, value_grad, jnp.stack([key_terms, value_terms]))


def product(left, right, left_dim, right_dim):
    return lax.dot_general(
        left, right, (((left_dim,), (right_dim,)), ((), ())), preferred_element_type=jnp.float32
    )


def strided_kernel(rows_ref, out_ref, *, scaling, arrays, half_heads):
    width = arrays * 2 * half_heads
    peers = rows_ref.shape[0] // width
    blocks = 2 * peers
    order = lambda dim: 2 * (lax.broadcasted_iota(jnp.int32, (blocks, blocks), dim) % peers) + (
        lax.broadcasted_iota(jnp.int32, (blocks, blocks), dim) // peers
    )
    causal = order(0) >= order(1)

    def load(array, head):
        return jnp.concatenate(
            [
                rows_ref[pl.ds((array * 2 + block) * half_heads + head, peers, stride=width), :]
                for block in range(2)
            ],
            axis=0,
        )

    def store(array, head, value):
        value = value.astype(jnp.float32)
        for block in range(2):
            out_ref[pl.ds((array * 2 + block) * half_heads + head, peers, stride=width), :] = value[
                block * peers : (block + 1) * peers
            ]

    for head in range(half_heads):
        query = load(0, head)
        key_rows = load(1, head)
        value_rows = load(2, head)
        grad_rows = load(3, head)
        scores = jnp.where(causal, product(query, key_rows, 1, 1) * scaling, -jnp.inf)
        raised = jnp.exp(scores - jnp.max(scores, axis=1, keepdims=True))
        weights = raised / jnp.sum(raised, axis=1, keepdims=True)
        weights_low = weights.astype(jnp.bfloat16)
        attended = product(weights_low, value_rows, 1, 0).astype(jnp.bfloat16)
        row_delta = jnp.sum(
            grad_rows.astype(jnp.float32) * attended.astype(jnp.float32), axis=1, keepdims=True
        )
        dscores = (weights * (product(grad_rows, value_rows, 1, 1) - row_delta)).astype(
            jnp.bfloat16
        )
        store(0, head, attended)
        store(1, head, (product(dscores, key_rows, 1, 0) * scaling).astype(jnp.bfloat16))
        store(2, head, (product(dscores, query, 0, 0) * scaling).astype(jnp.bfloat16))
        store(3, head, product(weights_low, grad_rows, 0, 0).astype(jnp.bfloat16))


def strided_heads(rows, scaling, half_heads):
    peers, width, head_dim = rows.shape
    vmem = pl.BlockSpec(memory_space=pltpu.VMEM)
    out = pl.pallas_call(
        functools.partial(strided_kernel, scaling=scaling, arrays=4, half_heads=half_heads),
        out_shape=jax.ShapeDtypeStruct((peers * width, head_dim), jnp.float32),
        in_specs=[vmem],
        out_specs=vmem,
    )(rows.reshape(peers * width, head_dim))
    return out.reshape(peers, width, head_dim)


def shards(queries, keys, values, out_grad):
    scaling = 1.0 / math.sqrt(HD)
    query_fixed, query_strided = split_heads(queries)
    key_fixed, key_strided = split_heads(keys)
    value_fixed, value_strided = split_heads(values)
    grad_fixed, grad_strided = split_heads(out_grad)
    blocks_here, positions, half_heads, head_dim = query_fixed.shape
    peers = lax.axis_size("ctx_chip") * 2
    residues = positions // peers
    core = lax.axis_index("ctx_core")
    swap = [(0, 1), (1, 0)]

    strided_rows = jnp.stack([query_strided, key_strided, value_strided, grad_strided])
    strided_rows = strided_rows.reshape(4, blocks_here, peers, residues, half_heads, head_dim)
    strided_rows = strided_rows.transpose(2, 0, 1, 3, 4, 5).reshape(peers, -1, head_dim)
    summary_rows = jnp.stack(
        [key_fixed[:, positions - SUMMARY :], value_fixed[:, positions - SUMMARY :]]
    ).reshape(1, 2, -1, head_dim)
    summary_rows = jnp.broadcast_to(summary_rows, (peers // 2,) + summary_rows.shape[1:])
    summary_rows = summary_rows.reshape(peers, -1, head_dim)
    strided_size = strided_rows.shape[1]
    received = lax.all_to_all(
        jnp.concatenate([strided_rows, summary_rows], axis=1), CTX, 0, 0, tiled=True
    )
    mine = received[:, strided_size:]
    sibling = lax.ppermute(mine, "ctx_core", swap)
    strided_out = strided_heads(received[:, :strided_size], scaling, half_heads)
    strided_out, sibling = lax.optimization_barrier((strided_out, sibling))
    summary_shape = (peers * blocks_here * SUMMARY, half_heads, head_dim)
    summary_keys = jnp.where(core == 0, mine, sibling).reshape(summary_shape)
    summary_values = jnp.where(core == 0, sibling, mine).reshape(summary_shape)

    attended, query_grad, key_grad, value_grad, terms = fixed_heads(
        query_fixed,
        key_fixed,
        value_fixed,
        grad_fixed,
        summary_keys,
        summary_values,
        scaling,
        lax.axis_index("ctx_chip") * 2 + core,
    )

    terms = terms.astype(jnp.bfloat16).reshape(2, peers, -1, head_dim)
    keep = jnp.where(core == 0, terms[0], terms[1])
    give = jnp.where(core == 0, terms[1], terms[0])
    terms = (
        keep.astype(jnp.float32) + lax.ppermute(give, "ctx_core", swap).astype(jnp.float32)
    ).astype(jnp.bfloat16)
    returned = lax.all_to_all(
        jnp.concatenate([strided_out, terms.astype(jnp.float32)], axis=1).astype(jnp.bfloat16),
        CTX,
        0,
        0,
        tiled=True,
    )
    strided_out = returned[:, :strided_size].reshape(
        peers, 4, blocks_here, residues, half_heads, head_dim
    )
    strided_out = strided_out.transpose(1, 2, 0, 3, 4, 5).reshape(
        4, blocks_here, positions, half_heads, head_dim
    )
    shares = returned[:, strided_size:].astype(jnp.float32)
    shares = jnp.sum(shares.reshape(peers // 2, 2, -1, head_dim), axis=0)
    shares = shares.reshape(2, blocks_here, SUMMARY, half_heads, head_dim)
    key_grad = jnp.concatenate(
        [key_grad[:, : positions - SUMMARY], key_grad[:, positions - SUMMARY :] + shares[0]], axis=1
    )
    value_grad = jnp.concatenate(
        [value_grad[:, : positions - SUMMARY], value_grad[:, positions - SUMMARY :] + shares[1]],
        axis=1,
    )
    return (
        join_heads(attended, strided_out[0]),
        join_heads(query_grad.astype(jnp.bfloat16), strided_out[1]),
        join_heads(key_grad.astype(jnp.bfloat16), strided_out[2]),
        join_heads(value_grad.astype(jnp.bfloat16), strided_out[3]),
    )


def solution(mesh):
    peers, heads = mesh.devices.shape
    split = Mesh(mesh.devices.reshape(peers // 2, 2, heads), CTX + ("head",))
    spec = P(CTX, "head")
    return jax.shard_map(
        shards,
        mesh=split,
        in_specs=(spec, spec, spec, spec),
        out_specs=(spec, spec, spec, spec),
        check_vma=False,
    )
```
